32 devices in a mesh: dp: 4 (over z), expert: 8 (over y, x, core).
Axes of the slice: x: 2, y: 2, z: 4, core: 2. Of those that a mesh axis runs over, the one named last changes fastest.
Arguments:
- hidden: bfloat16 [3072, 2880], P('expert', 'dp'), may hold values from -6 to 6
- segments: int32 [8, 384], P('expert'), may hold values from 0 to 3, never falling along the last dimension, each value on 1 to 192 neighbouring positions
- request_adapter: int32 [8, 4], P('expert'), may hold values from 0 to 7
- routes: int32 [8, 384, 4], P('expert', 'dp'), may hold values from 0 to 7, all different within a row; in each aligned block of 96 rows (0 to 95, 96 to 191, ..., all dimensions but the last counted through in order) at most 64 rows name the same one
- expert_gates: bfloat16 [8, 384, 4], P('expert', 'dp'), may hold values from 0.049804688 to 0.59765625
- attention_gain: float32 [2880], replicated, may hold values from 0.25 to 1.75
- joined_weight: bfloat16 [2880, 4, 640], P(None, 'dp'), may hold values from -0.109375 to 0.109375
- sinks: float32 [32], P('dp'), may hold values from 0 to 3
- attention_out_weight: bfloat16 [2048, 2880], P('dp'), may hold values from -0.125 to 0.125
- joined_down_maps: bfloat16 [2880, 128], replicated, may hold values from -0.109375 to 0.109375
- joined_up_maps: bfloat16 [128, 4, 640], P(None, 'dp'), may hold values from -0.375 to 0.375
- output_down_maps: bfloat16 [2048, 128], P('dp'), may hold values from -0.125 to 0.125
- output_up_maps: bfloat16 [128, 2880], P(None, 'dp'), may hold values from -0.75 to 0.75
- expert_norm_gain: float32 [2880], replicated, may hold values from 0.25 to 1.75
- expert_gate_weight: bfloat16 [8, 2880, 2880], P('expert', None, 'dp'), may hold values from -0.109375 to 0.109375
- expert_up_weight: bfloat16 [8, 2880, 2880], P('expert', None, 'dp'), may hold values from -0.109375 to 0.109375
- expert_down_weight: bfloat16 [8, 2880, 2880], P('expert', 'dp'), may hold values from -0.109375 to 0.109375
- closing_gain: float32 [2880], replicated, may hold values from 0.25 to 1.75
- vocabulary_weight: bfloat16 [2880, 25600], P(None, ('dp', 'expert')), may hold values from -0.109375 to 0.109375
Outputs:
- hidden_out: bfloat16 [3072, 2880], P('expert', 'dp')
- logits: float32 [32, 25600], P(None, ('dp', 'expert'))
The draws below stay inside these ranges and needn't reach their ends.
Inputs may be any that keep to these rules, and one draw needn't show every extreme that they name: `segments`: in each column the ids do not fall; each of the 4 requests has 1 to 192 tokens, and one has exactly 192. `routes`: the 4 experts of a token differ. Within the rows of one device (96 consecutive tokens, aligned blocks) no expert is named more than 64 times, and in some blocks one expert is named exactly 64 times.
All inputs are finite; a program needn't handle non-finite values.
Results may differ from the reference program's by a relative error of at most 0.02.
Values may be sent and summed in bfloat16 or wider, within the bound.
No kernel may reach another device: no remote copies, remote signals or barrier semaphores. Data moves between devices by JAX's collectives and lax.ppermute only.
A program may use at most 128 MiB of HBM per device.

```python
import math
import jax
import jax.numpy as jnp
import numpy as np
from jax import lax

MODEL_WIDTH = 2880
HEAD_SIZE = 64
QUERY_GROUP = 8
KEY_VALUE_HEADS = 4
QUERY_HEADS = 32
FF = 2880
EXPERTS = 8
TOP = 4
ADAPTER_RANK = 16
ADAPTER_COUNT = 8
TOK_DEV = 96
TOK_COL = 384
COLUMNS = 8
TOKENS = 3072
REQS = 4
MAX_LEN = 192
CAP = 64
LAST = 32
VOCAB = 25600
N_DP = 4


def plant(drawn, key, low, high):
    longest = drawn.shape.index(max(drawn.shape))
    spots = []
    for shift in (0, 1):
        where = [jax.random.randint(jax.random.fold_in(key, axis), (), 0, length) for axis, length in enumerate(drawn.shape)]
        where[longest] = (where[longest] + shift) % drawn.shape[longest]
        spots.append(tuple(where))
    return drawn.at[spots[0]].set(low).at[spots[1]].set(high)


def steps_of(key, shape, split, smallest, largest):
    def one(dim, shards_of):
        steps = jax.random.uniform(jax.random.fold_in(jax.random.fold_in(key, 6), dim), (shards_of,), jnp.float32, smallest / len(split), largest / len(split))
        return jnp.repeat(jnp.exp(steps), shape[dim] // shards_of).reshape((-1,) + (1,) * (len(shape) - dim - 1))

    factor_of = one(*split[0])
    for cut in split[1:]:
        factor_of = factor_of * one(*cut)
    return factor_of


def length_profile(amount, total, limit, lean):
    weights = [(1 << 20) // math.isqrt(grade ** lean) + 1 for grade in range(2, amount + 1)]
    spare, holding = total - limit - (amount - 1), [1] * (amount - 1)
    while spare > 0:
        free = [i for i in range(amount - 1) if holding[i] < limit]
        mass, budget = sum([weights[i] for i in free]), spare
        for i in free:
            extra = min(limit - holding[i], max(1, budget * weights[i] // mass), spare)
            holding[i] = holding[i] + extra
            spare = spare - extra
    return np.array([limit] + holding)


def ragged_sizes(key, number_of, total, bound, skew):
    if number_of == 2:
        one = jax.random.randint(key, (), max(1, total - bound), min(bound, total - 1) + 1)
        return jnp.stack([one, total - one])
    lengths = jnp.asarray(length_profile(number_of, total, bound, skew), jnp.int32)
    pairs = (number_of - 1) // 2
    giver, receiver = lengths[1:1 + 2 * pairs:2], lengths[2:2 + 2 * pairs:2]
    room = jnp.minimum(giver - 1, bound - receiver)
    moved = jax.random.randint(jax.random.fold_in(key, 1), (pairs,), 0, 1 << 20) % (room + 1)
    lengths = lengths.at[1:1 + 2 * pairs:2].set(giver - moved).at[2:2 + 2 * pairs:2].set(receiver + moved)
    return lengths[jax.random.permutation(jax.random.fold_in(key, 2), number_of)]


def deal_out(stream_key, own, number, rows, count, top, limit, slope):
    sequence = jax.random.permutation(stream_key, count)
    heavy_load, ordinary = portions_of(count, rows * top, limit, slope, True), portions_of(count, rows * top, limit, slope, False)
    places = jnp.arange(count)

    def named(sizes, rotation):
        used = int((sizes > 0).sum())
        fixed = max(1, used // 4)
        shifted = fixed + (places - fixed + rotation * (used - fixed)) % max(1, count - fixed)
        return jnp.zeros((count,), jnp.int32).at[sequence[jnp.where(places < fixed, places, shifted)]].set(jnp.asarray(sizes, jnp.int32))

    sizes = jnp.where(number % 4 == 0, named(heavy_load, number // 4), named(ordinary, number - number // 4 - 1))
    mixed = jax.random.permutation(jax.random.fold_in(own, 3), count)
    giver, receiver = mixed[0:count // 2 * 2:2], mixed[1:count // 2 * 2:2]
    room = jnp.minimum(sizes[giver] - 1, limit - sizes[receiver]) // 2
    room = jnp.where((giver == sequence[0]) | (receiver == sequence[0]) | (sizes[receiver] == 0), 0, jnp.maximum(room, 0))
    shifted = jax.random.randint(jax.random.fold_in(own, 4), (count // 2,), 0, 1 << 20) % (room + 1)
    sizes = sizes.at[giver].add(-shifted).at[receiver].add(shifted)
    labels = jnp.searchsorted(jnp.cumsum(sizes), jnp.arange(rows * top), side="right").astype(jnp.int32)
    listing = labels.reshape(top, rows).T
    listing = listing[jax.random.permutation(jax.random.fold_in(own, 1), rows)]
    rotation = jax.random.randint(jax.random.fold_in(own, 2), (rows, 1), 0, top)
    return jnp.take_along_axis(listing, (jnp.arange(top)[None, :] + rotation) % top, axis=1)


def portions_of(number_of, total, bound, slope, full):
    loads = [(1 << 20) // math.isqrt(rank ** slope) + 1 for rank in range(1, number_of + 1)]
    largest = bound if full else min(bound, max(-(-total // number_of), total * loads[0] // sum(loads)))
    least = 1 if total - largest >= number_of - 1 else 0
    holding, rest = [largest] + [least] * (number_of - 1), total - largest - least * (number_of - 1)
    while rest > 0:
        movable = [i for i in range(1, number_of) if holding[i] < largest] or [i for i in range(1, number_of) if holding[i] < bound]
        pool, budget = sum([loads[i] for i in movable]), rest
        for i in movable:
            extra = min(bound - holding[i], max(1, budget * loads[i] // pool), rest)
            holding[i] = holding[i] + extra
            rest = rest - extra
    return np.array(holding)


def noise(key, dims, scale, reach, split=(), kind=jnp.bfloat16):
    factor_of = steps_of(key, dims, split, -0.22, 0.18) if split else 1.0
    drawn = jax.random.normal(key, dims, jnp.float32) * scale * factor_of
    return jnp.minimum(jnp.maximum(drawn, -reach), reach).astype(kind)


def setup_inputs(seed: int = 0) -> dict:
    arg_keys = jax.random.split(jax.random.key(seed), 20)
    hidden = noise(arg_keys[0], (TOKENS, MODEL_WIDTH), 1.0, 6.0, ((0, 8), (1, 4)))
    segments = jax.vmap(lambda own: jnp.searchsorted(jnp.cumsum(ragged_sizes(own, REQS, TOK_COL, MAX_LEN, 2)), jnp.arange(TOK_COL), side="right"))(jax.random.split(arg_keys[1], COLUMNS)).reshape((COLUMNS, TOK_COL)).astype(jnp.int32)
    request_adapter = plant(jax.random.randint(arg_keys[2], (COLUMNS, REQS), 0, ADAPTER_COUNT), jax.random.fold_in(arg_keys[2], 1), 0, ADAPTER_COUNT - 1).astype(jnp.int32)
    routes_keys = jax.random.split(jax.random.fold_in(arg_keys[3], 1), COLUMNS * TOK_COL // TOK_DEV)
    routes_turns = jax.random.permutation(jax.random.fold_in(arg_keys[3], 3), COLUMNS * TOK_COL // TOK_DEV)
    routes = jax.vmap(lambda own, number: deal_out(jax.random.fold_in(arg_keys[3], 2), own, number, TOK_DEV, EXPERTS, TOP, CAP, 1))(routes_keys, routes_turns).reshape((COLUMNS, TOK_COL, TOP))
    expert_gates = jnp.clip(0.049804688 + 0.54785156 * jax.random.uniform(arg_keys[4], (COLUMNS, TOK_COL, TOP), jnp.float32) ** steps_of(arg_keys[4], (COLUMNS, TOK_COL, TOP), ((0, 8), (1, 4)), -0.2, 0.2), 0.049804688, 0.59765625).astype(jnp.bfloat16)
    attention_gain = jnp.clip(1.0 + 0.15 * jax.random.normal(arg_keys[5], (MODEL_WIDTH,), jnp.float32), 0.25, 1.75)
    joined_weight = noise(arg_keys[6], (MODEL_WIDTH, KEY_VALUE_HEADS, (QUERY_GROUP + 2) * HEAD_SIZE), MODEL_WIDTH ** -0.5, 0.109375, ((1, 4),))
    sinks = jnp.clip(3.0 * jax.random.uniform(arg_keys[7], (QUERY_HEADS,), jnp.float32) ** steps_of(arg_keys[7], (QUERY_HEADS,), ((0, 4),), -0.2, 0.2), 0.0, 3.0)
    attention_out_weight = noise(arg_keys[8], (QUERY_HEADS * HEAD_SIZE, MODEL_WIDTH), (QUERY_HEADS * HEAD_SIZE) ** -0.5, 0.125, ((0, 4),))
    joined_down_maps = noise(arg_keys[9], (MODEL_WIDTH, ADAPTER_COUNT * ADAPTER_RANK), MODEL_WIDTH ** -0.5, 0.109375)
    joined_up_maps = noise(arg_keys[10], (ADAPTER_COUNT * ADAPTER_RANK, KEY_VALUE_HEADS, (QUERY_GROUP + 2) * HEAD_SIZE), (16 * ADAPTER_RANK) ** -0.5, 0.375, ((1, 4),))
    output_down_maps = noise(arg_keys[11], (QUERY_HEADS * HEAD_SIZE, ADAPTER_COUNT * ADAPTER_RANK), (QUERY_HEADS * HEAD_SIZE) ** -0.5, 0.125, ((0, 4),))
    output_up_maps = noise(arg_keys[12], (ADAPTER_COUNT * ADAPTER_RANK, MODEL_WIDTH), (4 * ADAPTER_RANK) ** -0.5, 0.75, ((1, 4),))
    expert_norm_gain = jnp.clip(1.0 + 0.15 * jax.random.normal(arg_keys[13], (MODEL_WIDTH,), jnp.float32), 0.25, 1.75)
    expert_gate_weight = noise(arg_keys[14], (EXPERTS, MODEL_WIDTH, FF), MODEL_WIDTH ** -0.5, 0.109375, ((0, 8), (2, 4)))
    expert_up_weight = noise(arg_keys[15], (EXPERTS, MODEL_WIDTH, FF), MODEL_WIDTH ** -0.5, 0.109375, ((0, 8), (2, 4)))
    expert_down_weight = noise(arg_keys[16], (EXPERTS, FF, MODEL_WIDTH), FF ** -0.5, 0.109375, ((0, 8), (1, 4)))
    closing_gain = jnp.clip(1.0 + 0.15 * jax.random.normal(arg_keys[17], (MODEL_WIDTH,), jnp.float32), 0.25, 1.75)
    vocabulary_weight = noise(arg_keys[18], (MODEL_WIDTH, VOCAB), MODEL_WIDTH ** -0.5, 0.109375, ((1, 32),))
    return dict(hidden=hidden, segments=segments, request_adapter=request_adapter, routes=routes, expert_gates=expert_gates, attention_gain=attention_gain, joined_weight=joined_weight, sinks=sinks, attention_out_weight=attention_out_weight, joined_down_maps=joined_down_maps, joined_up_maps=joined_up_maps, output_down_maps=output_down_maps, output_up_maps=output_up_maps, expert_norm_gain=expert_norm_gain, expert_gate_weight=expert_gate_weight, expert_up_weight=expert_up_weight, expert_down_weight=expert_down_weight, closing_gain=closing_gain, vocabulary_weight=vocabulary_weight)


epsilon = 1e-05
theta_base = 150000.0
adapter_scale = 2.0
glu_alpha = 1.702

def rms_scale(values, gain_row):
    mean_square = lax.optimization_barrier(jnp.mean(values * values, axis=-1, keepdims=True))
    return values * lax.rsqrt(mean_square + epsilon) * gain_row

def positions_of(segment_row):
    counter = jnp.arange(segment_row.shape[0], dtype=jnp.int32)
    starting = jnp.concatenate([jnp.ones((1,), dtype=jnp.bool_), segment_row[1:] != segment_row[:-1]])
    first_index = lax.cummax(jnp.where(starting, counter, 0), axis=0)
    return counter - first_index

def adapter_per_token(segment_row, adapter_row):
    hits = segment_row[:, None] == jnp.arange(adapter_row.shape[0], dtype=jnp.int32)[None, :]
    return lax.optimization_barrier(jnp.sum(jnp.where(hits, adapter_row[None, :], 0), axis=1))

def rotate_heads(values, positions):
    head_dim = values.shape[-1]
    half_dim = head_dim // 2
    frequency = theta_base ** (-2.0 * jnp.arange(half_dim, dtype=jnp.float32) / head_dim)
    angles = positions.astype(jnp.float32)[:, None] * frequency[None, :]
    cosine = jnp.cos(angles)[:, None, :]
    sine_part = jnp.sin(angles)[:, None, :]
    first_half = values[..., :half_dim]
    second_half = values[..., half_dim:]
    return jnp.concatenate([first_half * cosine - second_half * sine_part, second_half * cosine + first_half * sine_part], axis=-1)

def attend_heads(queries, key_heads, value_heads, segment_row, sink_row):
    tokens_now, kv_now, group_now, head_dim = queries.shape
    scores = jnp.einsum('tkgh,skh->kgts', queries.astype(jnp.float32), key_heads.astype(jnp.float32)) * head_dim ** (-0.5)
    counter = jnp.arange(tokens_now, dtype=jnp.int32)
    allowed = (segment_row[:, None] == segment_row[None, :]) & (counter[None, :] <= counter[:, None])
    weights = jnp.where(allowed[None, None], jnp.exp(scores), 0.0)
    totals = lax.optimization_barrier(jnp.sum(weights, axis=-1, keepdims=True)) + jnp.exp(sink_row).reshape(kv_now, group_now, 1, 1)
    probs = lax.optimization_barrier((weights / totals).astype(jnp.bfloat16))
    blended_hidden = jnp.einsum('kgts,skh->tkgh', probs.astype(jnp.float32), value_heads.astype(jnp.float32))
    return blended_hidden.astype(jnp.bfloat16).reshape(tokens_now, kv_now * group_now * head_dim)

def reference(hidden, segments, request_adapter, routes, expert_gates, attention_gain, joined_weight, sinks, attention_out_weight, joined_down_maps, joined_up_maps, output_down_maps, output_up_maps, expert_norm_gain, expert_gate_weight, expert_up_weight, expert_down_weight, closing_gain, vocabulary_weight):
    reduced_every_adapter = ADAPTER_COUNT * ADAPTER_RANK
    rank_owner = jnp.arange(reduced_every_adapter, dtype=jnp.int32) // ADAPTER_RANK

    def column_layer(inputs):
        column_rows, segment_row, adapter_row = inputs
        normalized_hidden = rms_scale(column_rows.astype(jnp.float32), attention_gain).astype(jnp.bfloat16)
        joined_projection = jnp.dot(normalized_hidden, joined_weight.reshape(MODEL_WIDTH, -1), preferred_element_type=jnp.float32)
        reduced_hidden = jnp.dot(normalized_hidden, joined_down_maps, preferred_element_type=jnp.float32).astype(jnp.bfloat16)
        adapter_mask = adapter_per_token(segment_row, adapter_row)[:, None] == rank_owner[None, :]
        selected_reduced = jnp.where(adapter_mask, reduced_hidden, jnp.zeros_like(reduced_hidden))
        joined_projection = joined_projection + adapter_scale * jnp.dot(selected_reduced, joined_up_maps.reshape(reduced_every_adapter, -1), preferred_element_type=jnp.float32)
        joined_projection = joined_projection.reshape(TOK_COL, KEY_VALUE_HEADS, QUERY_GROUP + 2, HEAD_SIZE)
        positions = positions_of(segment_row)
        queries = rotate_heads(joined_projection[:, :, :QUERY_GROUP].reshape(TOK_COL, KEY_VALUE_HEADS * QUERY_GROUP, HEAD_SIZE), positions)
        queries = lax.optimization_barrier(queries.astype(jnp.bfloat16)).reshape(TOK_COL, KEY_VALUE_HEADS, QUERY_GROUP, HEAD_SIZE)
        key_heads = lax.optimization_barrier(rotate_heads(joined_projection[:, :, QUERY_GROUP], positions).astype(jnp.bfloat16))
        value_heads = lax.optimization_barrier(joined_projection[:, :, QUERY_GROUP + 1].astype(jnp.bfloat16))
        blended_hidden = attend_heads(queries, key_heads, value_heads, segment_row, sinks)
        attention_output = jnp.dot(blended_hidden, attention_out_weight, preferred_element_type=jnp.float32)
        output_reduced = jnp.dot(blended_hidden, output_down_maps, preferred_element_type=jnp.float32).astype(jnp.bfloat16)
        selected_output = jnp.where(adapter_mask, output_reduced, jnp.zeros_like(output_reduced))
        attention_output = attention_output + adapter_scale * jnp.dot(selected_output, output_up_maps, preferred_element_type=jnp.float32)
        return (column_rows.astype(jnp.float32) + attention_output).astype(jnp.bfloat16)
    resid = lax.map(column_layer, (hidden.reshape(COLUMNS, TOK_COL, MODEL_WIDTH), segments, request_adapter)).reshape(TOKENS, MODEL_WIDTH)
    resid = lax.optimization_barrier(resid)
    moe_in = rms_scale(resid.astype(jnp.float32), expert_norm_gain).astype(jnp.bfloat16)
    blocks = TOKENS // TOK_DEV
    route_rows = routes.reshape(blocks, TOK_DEV * TOP)
    gate_rows = expert_gates.reshape(blocks, TOK_DEV * TOP).astype(jnp.float32)
    one_hot = (route_rows[:, :, None] == jnp.arange(EXPERTS, dtype=jnp.int32)[None, None, :]).astype(jnp.int32)
    slot_rows = lax.optimization_barrier(jnp.sum((jnp.cumsum(one_hot, axis=1) - one_hot) * one_hot, axis=2))
    block_ids = jnp.broadcast_to(jnp.arange(blocks, dtype=jnp.int32)[:, None], route_rows.shape)
    token_ids = block_ids * TOK_DEV + jnp.arange(TOK_DEV * TOP, dtype=jnp.int32)[None, :] // TOP
    table = jnp.full((EXPERTS, blocks, CAP), TOKENS, jnp.int32).at[route_rows, block_ids, slot_rows].set(token_ids)
    gate_table = jnp.zeros((EXPERTS, blocks, CAP), jnp.float32).at[route_rows, block_ids, slot_rows].set(gate_rows)
    padded = jnp.concatenate([moe_in, jnp.zeros((1, MODEL_WIDTH), jnp.bfloat16)], axis=0)
    quarter_units = FF // N_DP

    def one_expert(running, inputs):
        gate_weight, up_weight, down_weight, rows_index, row_gates = inputs
        flat_index = rows_index.reshape(-1).astype(jnp.int32)
        rows_in = jnp.take(padded, flat_index, axis=0)
        gate_part = jnp.dot(rows_in, gate_weight, preferred_element_type=jnp.float32)
        up_part = jnp.dot(rows_in, up_weight, preferred_element_type=jnp.float32)
        activated = (gate_part * jax.nn.sigmoid(glu_alpha * gate_part) * (up_part + 1.0)).astype(jnp.bfloat16)
        summed = jnp.zeros((flat_index.shape[0], MODEL_WIDTH), jnp.float32)
        for quarter in range(N_DP):
            first_unit = quarter * quarter_units
            piece_out = jnp.dot(activated[:, first_unit:first_unit + quarter_units], down_weight[first_unit:first_unit + quarter_units], preferred_element_type=jnp.float32)
            summed = summed + lax.optimization_barrier(piece_out.astype(jnp.bfloat16)).astype(jnp.float32)
        expert_out = lax.optimization_barrier(summed.astype(jnp.bfloat16)).astype(jnp.float32)
        running = running.at[flat_index].add(row_gates.reshape(-1, 1) * expert_out)
        return (running, None)
    moe_sum, unused = lax.scan(one_expert, jnp.zeros((TOKENS + 1, MODEL_WIDTH), jnp.float32), (expert_gate_weight, expert_up_weight, expert_down_weight, table, gate_table))
    moe = lax.optimization_barrier(moe_sum[:TOKENS].astype(jnp.bfloat16))
    hidden_out = (resid.astype(jnp.float32) + moe.astype(jnp.float32)).astype(jnp.bfloat16)
    column_out = lax.optimization_barrier(hidden_out).reshape(COLUMNS, TOK_COL, MODEL_WIDTH)
    counter = jnp.arange(TOK_COL, dtype=jnp.int32)
    request_ids = jnp.arange(REQS, dtype=jnp.int32)
    last_index = lax.optimization_barrier(jnp.max(jnp.where(segments[:, None, :] == request_ids[None, :, None], counter[None, None, :], -1), axis=2))
    end_rows = jax.vmap(lambda rows, where_at: jnp.take(rows, where_at, axis=0))(column_out, last_index)
    ends = rms_scale(end_rows.astype(jnp.float32), closing_gain).astype(jnp.bfloat16).reshape(LAST, MODEL_WIDTH)
    logits = jnp.dot(ends, vocabulary_weight, preferred_element_type=jnp.float32)
    return (hidden_out, logits)
```

```python
import jax
import jax.numpy as jnp
from jax import lax
from jax.sharding import PartitionSpec as P

HEAD_SIZE = 64
QUERY_GROUP = 8
TOP = 4
ADAPTER_RANK = 16
REQS = 4


epsilon = 1e-05
theta_base = 150000.0
adapter_scale = 2.0
glu_alpha = 1.702


def rms_scale(values, gain_row):
    mean_square = jnp.mean(values * values, axis=-1, keepdims=True)
    return values * lax.rsqrt(mean_square + epsilon) * gain_row


def positions_of(segment_row):
    counter = jnp.arange(segment_row.shape[0], dtype=jnp.int32)
    starting = jnp.concatenate(
        [jnp.ones((1,), dtype=jnp.bool_), segment_row[1:] != segment_row[:-1]]
    )
    first_index = lax.cummax(jnp.where(starting, counter, 0), axis=0)
    return counter - first_index


def adapter_per_token(segment_row, adapter_row):
    hits = segment_row[:, None] == jnp.arange(adapter_row.shape[0], dtype=jnp.int32)[None, :]
    return jnp.sum(jnp.where(hits, adapter_row[None, :], 0), axis=1)


def rotate_heads(values, positions):
    head_dim = values.shape[-1]
    half_dim = head_dim // 2
    frequency = theta_base ** (-2.0 * jnp.arange(half_dim, dtype=jnp.float32) / head_dim)
    angles = positions.astype(jnp.float32)[:, None] * frequency[None, :]
    cosine = jnp.cos(angles)[:, None, :]
    sine_part = jnp.sin(angles)[:, None, :]
    first_half = values[..., :half_dim]
    second_half = values[..., half_dim:]
    return jnp.concatenate(
        [
            first_half * cosine - second_half * sine_part,
            second_half * cosine + first_half * sine_part,
        ],
        axis=-1,
    )


def attend_heads(queries, key_heads, value_heads, segment_row, sink_row):
    tokens_now, kv_now, group_now, head_dim = queries.shape
    scores = jnp.einsum(
        "tkgh,skh->kgts", queries, key_heads, preferred_element_type=jnp.float32
    ) * head_dim ** (-0.5)
    counter = jnp.arange(tokens_now, dtype=jnp.int32)
    allowed = (segment_row[:, None] == segment_row[None, :]) & (
        counter[None, :] <= counter[:, None]
    )
    weights = jnp.where(allowed[None, None], jnp.exp(scores), 0.0)
    totals = jnp.sum(weights, axis=-1, keepdims=True) + jnp.exp(sink_row).reshape(
        kv_now, group_now, 1, 1
    )
    probs = (weights / totals).astype(jnp.bfloat16)
    blended_hidden = jnp.einsum(
        "kgts,skh->tkgh", probs, value_heads, preferred_element_type=jnp.float32
    )
    return blended_hidden.astype(jnp.bfloat16).reshape(tokens_now, kv_now * group_now * head_dim)


def shards(
    hidden,
    segments,
    request_adapter,
    routes,
    expert_gates,
    attention_gain,
    joined_weight,
    sinks,
    attention_out_weight,
    joined_down_maps,
    joined_up_maps,
    output_down_maps,
    output_up_maps,
    expert_norm_gain,
    expert_gate_weight,
    expert_up_weight,
    expert_down_weight,
    closing_gain,
    vocabulary_weight,
):
    groups = lax.axis_size("dp")
    columns = lax.axis_size("expert")
    position_dp = lax.axis_index("dp")
    segment_row = segments[0]
    adapter_row = request_adapter[0]
    col_tokens = segment_row.shape[0]
    gathered_rows = lax.all_gather(hidden, "dp", axis=1, tiled=True)
    width = gathered_rows.shape[1]
    normalized_hidden = rms_scale(gathered_rows.astype(jnp.float32), attention_gain).astype(
        jnp.bfloat16
    )
    joined_projection = jnp.dot(
        normalized_hidden, joined_weight.reshape(width, -1), preferred_element_type=jnp.float32
    )
    reduced_every_adapter = joined_down_maps.shape[1]
    reduced_hidden = jnp.dot(
        normalized_hidden, joined_down_maps, preferred_element_type=jnp.float32
    ).astype(jnp.bfloat16)
    rank_owner = jnp.arange(reduced_every_adapter, dtype=jnp.int32) // ADAPTER_RANK
    adapter_mask = adapter_per_token(segment_row, adapter_row)[:, None] == rank_owner[None, :]
    selected_reduced = jnp.where(adapter_mask, reduced_hidden, jnp.zeros_like(reduced_hidden))
    joined_projection = joined_projection + adapter_scale * jnp.dot(
        selected_reduced,
        joined_up_maps.reshape(reduced_every_adapter, -1),
        preferred_element_type=jnp.float32,
    )
    kv_here = joined_weight.shape[1]
    joined_projection = joined_projection.reshape(col_tokens, kv_here, QUERY_GROUP + 2, HEAD_SIZE)
    positions = positions_of(segment_row)
    queries = rotate_heads(
        joined_projection[:, :, :QUERY_GROUP].reshape(col_tokens, kv_here * QUERY_GROUP, HEAD_SIZE),
        positions,
    )
    queries = queries.astype(jnp.bfloat16).reshape(col_tokens, kv_here, QUERY_GROUP, HEAD_SIZE)
    key_heads = rotate_heads(joined_projection[:, :, QUERY_GROUP], positions).astype(jnp.bfloat16)
    value_heads = joined_projection[:, :, QUERY_GROUP + 1].astype(jnp.bfloat16)
    blended_hidden = attend_heads(queries, key_heads, value_heads, segment_row, sinks)
    partial_out = jnp.dot(blended_hidden, attention_out_weight, preferred_element_type=jnp.float32)
    mine_out = lax.psum_scatter(
        partial_out.astype(jnp.bfloat16), "dp", scatter_dimension=1, tiled=True
    ).astype(jnp.float32)
    output_reduced = lax.psum(
        jnp.dot(blended_hidden, output_down_maps, preferred_element_type=jnp.float32).astype(
            jnp.bfloat16
        ),
        "dp",
    )
    selected_output = jnp.where(adapter_mask, output_reduced, jnp.zeros_like(output_reduced))
    adapter_delta = adapter_scale * jnp.dot(
        selected_output, output_up_maps, preferred_element_type=jnp.float32
    )
    resid = (hidden.astype(jnp.float32) + mine_out + adapter_delta).astype(jnp.bfloat16)
    column_full = lax.all_gather(resid, "dp", axis=1, tiled=True)
    moe_in = rms_scale(column_full.astype(jnp.float32), expert_norm_gain).astype(jnp.bfloat16)
    share = col_tokens // groups
    experts = expert_gate_weight.shape[0] * columns
    capacity = 4 * share * TOP // (3 * experts)
    col_capacity = groups * capacity
    route_col = lax.all_gather(routes[0], "dp", axis=0, tiled=True)
    gates_col = lax.all_gather(expert_gates[0], "dp", axis=0, tiled=True)
    route_flat = route_col.reshape(-1)
    one_hot = (route_flat[:, None] == jnp.arange(experts, dtype=jnp.int32)[None, :]).astype(
        jnp.int32
    )
    slot_rows = jnp.sum((jnp.cumsum(one_hot, axis=0) - one_hot) * one_hot, axis=1)
    target = route_flat * col_capacity + slot_rows
    source_rows = jnp.arange(route_flat.shape[0], dtype=jnp.int32) // TOP
    table = jnp.full((experts * col_capacity,), col_tokens, jnp.int32).at[target].set(source_rows)
    padded = jnp.concatenate([moe_in, jnp.zeros((1, width), jnp.bfloat16)], axis=0)
    outgoing = jnp.take(padded, table, axis=0).reshape(experts, col_capacity, width)
    gate_weight = expert_gate_weight[0]
    up_weight = expert_up_weight[0]
    down_weight = expert_down_weight[0]
    arrived = lax.all_to_all(outgoing, "expert", split_axis=0, concat_axis=0, tiled=True)
    rows_in = arrived.reshape(-1, width)
    gate_part = jnp.dot(rows_in, gate_weight, preferred_element_type=jnp.float32)
    up_part = jnp.dot(rows_in, up_weight, preferred_element_type=jnp.float32)
    activated = (gate_part * jax.nn.sigmoid(glu_alpha * gate_part) * (up_part + 1.0)).astype(
        jnp.bfloat16
    )
    shares_out = (
        jnp.dot(activated, down_weight, preferred_element_type=jnp.float32)
        .astype(jnp.bfloat16)
        .reshape(experts, col_capacity, width)
    )
    answers = lax.all_to_all(shares_out, "expert", split_axis=0, concat_axis=0, tiled=True)
    picked_out = jnp.take(answers.reshape(experts * col_capacity, width), target, axis=0).reshape(
        col_tokens, TOP, width
    )
    mixture = jnp.einsum(
        "tk,tkd->td", gates_col, picked_out, preferred_element_type=jnp.float32
    )
    moe_part = lax.psum_scatter(
        mixture.astype(jnp.bfloat16), "dp", scatter_dimension=1, tiled=True
    )
    moe_rounded = moe_part.astype(jnp.float32).astype(jnp.bfloat16)
    hidden_out = (resid.astype(jnp.float32) + moe_rounded.astype(jnp.float32)).astype(jnp.bfloat16)
    counter = jnp.arange(col_tokens, dtype=jnp.int32)
    request_ids = jnp.arange(REQS, dtype=jnp.int32)
    last_index = jnp.max(
        jnp.where(segment_row[None, :] == request_ids[:, None], counter[None, :], -1), axis=1
    )
    chosen = jnp.take(hidden_out, jnp.clip(last_index, 0, col_tokens - 1), axis=0)
    spread_rows = lax.all_gather(chosen, ("dp", "expert"), axis=0, tiled=True)
    quarter = chosen.shape[1]
    tail_full = (
        spread_rows.reshape(groups, columns * REQS, quarter)
        .transpose(1, 0, 2)
        .reshape(columns * REQS, groups * quarter)
    )
    tail_rows = rms_scale(tail_full.astype(jnp.float32), closing_gain).astype(jnp.bfloat16)
    logits = jnp.dot(tail_rows, vocabulary_weight, preferred_element_type=jnp.float32)
    return (hidden_out, logits)


def solution(mesh):
    in_specs = (
        P("expert", "dp"),
        P("expert", None),
        P("expert", None),
        P("expert", "dp", None),
        P("expert", "dp", None),
        P(),
        P(None, "dp", None),
        P("dp"),
        P("dp", None),
        P(),
        P(None, "dp", None),
        P("dp", None),
        P(None, "dp"),
        P(),
        P("expert", None, "dp"),
        P("expert", None, "dp"),
        P("expert", "dp", None),
        P(),
        P(None, ("dp", "expert")),
    )
    out_specs = (P("expert", "dp"), P(None, ("dp", "expert")))
    return jax.shard_map(shards, mesh=mesh, in_specs=in_specs, out_specs=out_specs, check_vma=False)
```

```python
import jax
import jax.numpy as jnp
from jax import lax
from jax.sharding import PartitionSpec as P

HEAD_SIZE = 64
QUERY_GROUP = 8
TOP = 4
ADAPTER_RANK = 16
REQS = 4


epsilon = 1e-05
theta_base = 150000.0
adapter_scale = 2.0
glu_alpha = 1.702


def rms_scale(values, gain_row):
    mean_square = jnp.mean(values * values, axis=-1, keepdims=True)
    return values * lax.rsqrt(mean_square + epsilon) * gain_row


def positions_of(segment_row):
    counter = jnp.arange(segment_row.shape[0], dtype=jnp.int32)
    starting = jnp.concatenate(
        [jnp.ones((1,), dtype=jnp.bool_), segment_row[1:] != segment_row[:-1]]
    )
    first_index = lax.cummax(jnp.where(starting, counter, 0), axis=0)
    return counter - first_index


def adapter_per_token(segment_row, adapter_row):
    hits = segment_row[:, None] == jnp.arange(adapter_row.shape[0], dtype=jnp.int32)[None, :]
    return jnp.sum(jnp.where(hits, adapter_row[None, :], 0), axis=1)


def rotate_heads(values, positions):
    head_dim = values.shape[-1]
    half_dim = head_dim // 2
    frequency = theta_base ** (-2.0 * jnp.arange(half_dim, dtype=jnp.float32) / head_dim)
    angles = positions.astype(jnp.float32)[:, None] * frequency[None, :]
    cosine = jnp.cos(angles)[:, None, :]
    sine_part = jnp.sin(angles)[:, None, :]
    first_half = values[..., :half_dim]
    second_half = values[..., half_dim:]
    return jnp.concatenate(
        [
            first_half * cosine - second_half * sine_part,
            second_half * cosine + first_half * sine_part,
        ],
        axis=-1,
    )


def attend_heads(queries, key_heads, value_heads, segment_row, sink_row):
    tokens_now, kv_now, group_now, head_dim = queries.shape
    scores = jnp.einsum(
        "tkgh,skh->kgts", queries, key_heads, preferred_element_type=jnp.float32
    ) * head_dim ** (-0.5)
    counter = jnp.arange(tokens_now, dtype=jnp.int32)
    allowed = (segment_row[:, None] == segment_row[None, :]) & (
        counter[None, :] <= counter[:, None]
    )
    weights = jnp.where(allowed[None, None], jnp.exp(scores), 0.0)
    totals = jnp.sum(weights, axis=-1, keepdims=True) + jnp.exp(sink_row).reshape(
        kv_now, group_now, 1, 1
    )
    probs = (weights / totals).astype(jnp.bfloat16)
    blended_hidden = jnp.einsum(
        "kgts,skh->tkgh", probs, value_heads, preferred_element_type=jnp.float32
    )
    return blended_hidden.astype(jnp.bfloat16).reshape(tokens_now, kv_now * group_now * head_dim)


def shards(
    hidden,
    segments,
    request_adapter,
    routes,
    expert_gates,
    attention_gain,
    joined_weight,
    sinks,
    attention_out_weight,
    joined_down_maps,
    joined_up_maps,
    output_down_maps,
    output_up_maps,
    expert_norm_gain,
    expert_gate_weight,
    expert_up_weight,
    expert_down_weight,
    closing_gain,
    vocabulary_weight,
):
    groups = lax.axis_size("dp")
    columns = lax.axis_size("expert")
    position_dp = lax.axis_index("dp")
    segment_row = segments[0]
    adapter_row = request_adapter[0]
    col_tokens = segment_row.shape[0]
    gathered_rows = lax.all_gather(hidden, "dp", axis=1, tiled=True)
    width = gathered_rows.shape[1]
    normalized_hidden = rms_scale(gathered_rows.astype(jnp.float32), attention_gain).astype(
        jnp.bfloat16
    )
    joined_projection = jnp.dot(
        normalized_hidden, joined_weight.reshape(width, -1), preferred_element_type=jnp.float32
    )
    reduced_every_adapter = joined_down_maps.shape[1]
    reduced_hidden = jnp.dot(
        normalized_hidden, joined_down_maps, preferred_element_type=jnp.float32
    ).astype(jnp.bfloat16)
    rank_owner = jnp.arange(reduced_every_adapter, dtype=jnp.int32) // ADAPTER_RANK
    adapter_mask = adapter_per_token(segment_row, adapter_row)[:, None] == rank_owner[None, :]
    selected_reduced = jnp.where(adapter_mask, reduced_hidden, jnp.zeros_like(reduced_hidden))
    joined_projection = joined_projection + adapter_scale * jnp.dot(
        selected_reduced,
        joined_up_maps.reshape(reduced_every_adapter, -1),
        preferred_element_type=jnp.float32,
    )
    kv_here = joined_weight.shape[1]
    joined_projection = joined_projection.reshape(col_tokens, kv_here, QUERY_GROUP + 2, HEAD_SIZE)
    positions = positions_of(segment_row)
    queries = rotate_heads(
        joined_projection[:, :, :QUERY_GROUP].reshape(col_tokens, kv_here * QUERY_GROUP, HEAD_SIZE),
        positions,
    )
    queries = queries.astype(jnp.bfloat16).reshape(col_tokens, kv_here, QUERY_GROUP, HEAD_SIZE)
    key_heads = rotate_heads(joined_projection[:, :, QUERY_GROUP], positions).astype(jnp.bfloat16)
    value_heads = joined_projection[:, :, QUERY_GROUP + 1].astype(jnp.bfloat16)
    blended_hidden = attend_heads(queries, key_heads, value_heads, segment_row, sinks)
    partial_out = jnp.dot(blended_hidden, attention_out_weight, preferred_element_type=jnp.float32)
    mine_out = lax.psum_scatter(
        partial_out.astype(jnp.bfloat16), "dp", scatter_dimension=1, tiled=True
    ).astype(jnp.float32)
    output_reduced = lax.psum(
        jnp.dot(blended_hidden, output_down_maps, preferred_element_type=jnp.float32).astype(
            jnp.bfloat16
        ),
        "dp",
    )
    selected_output = jnp.where(adapter_mask, output_reduced, jnp.zeros_like(output_reduced))
    adapter_delta = adapter_scale * jnp.dot(
        selected_output, output_up_maps, preferred_element_type=jnp.float32
    )
    resid = (hidden.astype(jnp.float32) + mine_out + adapter_delta).astype(jnp.bfloat16)
    column_full = lax.all_gather(resid, "dp", axis=1, tiled=True)
    moe_in = rms_scale(column_full.astype(jnp.float32), expert_norm_gain).astype(jnp.bfloat16)
    share = col_tokens // groups
    experts = expert_gate_weight.shape[0] * columns
    capacity = 4 * share * TOP // (3 * experts)
    col_capacity = groups * capacity
    route_pack = jnp.concatenate(
        [routes[0].astype(jnp.bfloat16), expert_gates[0].astype(jnp.bfloat16)], axis=1
    )
    pack_col = lax.all_gather(route_pack, "dp", axis=0, tiled=True)
    route_col = pack_col[:, :TOP].astype(jnp.int32)
    gates_col = pack_col[:, TOP:]
    route_flat = route_col.reshape(-1)
    one_hot = (route_flat[:, None] == jnp.arange(experts, dtype=jnp.int32)[None, :]).astype(
        jnp.int32
    )
    slot_rows = jnp.sum((jnp.cumsum(one_hot, axis=0) - one_hot) * one_hot, axis=1)
    target = route_flat * col_capacity + slot_rows
    source_rows = jnp.arange(route_flat.shape[0], dtype=jnp.int32) // TOP
    table = jnp.full((experts * col_capacity,), col_tokens, jnp.int32).at[target].set(source_rows)
    dispatch = (table[:, None] == jnp.arange(col_tokens, dtype=jnp.int32)[None, :]).astype(
        jnp.bfloat16
    )
    outgoing = (
        jnp.dot(dispatch, moe_in, preferred_element_type=jnp.float32)
        .astype(jnp.bfloat16)
        .reshape(experts, col_capacity, width)
    )
    gate_weight = expert_gate_weight[0]
    up_weight = expert_up_weight[0]
    down_weight = expert_down_weight[0]
    arrived = lax.all_to_all(outgoing, "expert", split_axis=0, concat_axis=0, tiled=True)
    rows_in = arrived.reshape(-1, width)
    gate_part = jnp.dot(rows_in, gate_weight, preferred_element_type=jnp.float32)
    up_part = jnp.dot(rows_in, up_weight, preferred_element_type=jnp.float32)
    activated = (gate_part * jax.nn.sigmoid(glu_alpha * gate_part) * (up_part + 1.0)).astype(
        jnp.bfloat16
    )
    shares_out = (
        jnp.dot(activated, down_weight, preferred_element_type=jnp.float32)
        .astype(jnp.bfloat16)
        .reshape(experts, col_capacity, width)
    )
    answers = lax.all_to_all(shares_out, "expert", split_axis=0, concat_axis=0, tiled=True)
    slot_ids = jnp.arange(experts * col_capacity, dtype=jnp.int32)
    combine = jnp.sum(
        jnp.where(
            target.reshape(col_tokens, TOP)[:, :, None] == slot_ids[None, None, :],
            gates_col[:, :, None],
            jnp.zeros((), jnp.bfloat16),
        ),
        axis=1,
    ).astype(jnp.bfloat16)
    mixture = jnp.dot(
        combine, answers.reshape(experts * col_capacity, width), preferred_element_type=jnp.float32
    )
    moe_part = lax.psum_scatter(
        mixture.astype(jnp.bfloat16), "dp", scatter_dimension=1, tiled=True
    )
    moe_rounded = moe_part.astype(jnp.float32).astype(jnp.bfloat16)
    hidden_out = (resid.astype(jnp.float32) + moe_rounded.astype(jnp.float32)).astype(jnp.bfloat16)
    counter = jnp.arange(col_tokens, dtype=jnp.int32)
    request_ids = jnp.arange(REQS, dtype=jnp.int32)
    last_index = jnp.max(
        jnp.where(segment_row[None, :] == request_ids[:, None], counter[None, :], -1), axis=1
    )
    chosen = jnp.take(hidden_out, jnp.clip(last_index, 0, col_tokens - 1), axis=0)
    row_full = lax.all_gather(chosen, "dp", axis=1, tiled=True)
    tail_full = lax.all_gather(row_full, "expert", axis=0, tiled=True)
    tail_rows = rms_scale(tail_full.astype(jnp.float32), closing_gain).astype(jnp.bfloat16)
    logits = jnp.dot(tail_rows, vocabulary_weight, preferred_element_type=jnp.float32)
    return (hidden_out, logits)


def solution(mesh):
    in_specs = (
        P("expert", "dp"),
        P("expert", None),
        P("expert", None),
        P("expert", "dp", None),
        P("expert", "dp", None),
        P(),
        P(None, "dp", None),
        P("dp"),
        P("dp", None),
        P(),
        P(None, "dp", None),
        P("dp", None),
        P(None, "dp"),
        P(),
        P("expert", None, "dp"),
        P("expert", None, "dp"),
        P("expert", "dp", None),
        P(),
        P(None, ("dp", "expert")),
    )
    out_specs = (P("expert", "dp"), P(None, ("dp", "expert")))
    return jax.shard_map(shards, mesh=mesh, in_specs=in_specs, out_specs=out_specs, check_vma=False)
```

```python
import jax
import jax.numpy as jnp
from jax import lax
from jax.sharding import PartitionSpec as P

HEAD_SIZE = 64
QUERY_GROUP = 8
TOP = 4
ADAPTER_RANK = 16
REQS = 4


epsilon = 1e-05
theta_base = 150000.0
adapter_scale = 2.0
glu_alpha = 1.702


def rms_scale(values, gain_row):
    mean_square = jnp.mean(values * values, axis=-1, keepdims=True)
    return values * lax.rsqrt(mean_square + epsilon) * gain_row


def positions_of(segment_row):
    counter = jnp.arange(segment_row.shape[0], dtype=jnp.int32)
    starting = jnp.concatenate(
        [jnp.ones((1,), dtype=jnp.bool_), segment_row[1:] != segment_row[:-1]]
    )
    first_index = lax.cummax(jnp.where(starting, counter, 0), axis=0)
    return counter - first_index


def adapter_per_token(segment_row, adapter_row):
    hits = segment_row[:, None] == jnp.arange(adapter_row.shape[0], dtype=jnp.int32)[None, :]
    return jnp.sum(jnp.where(hits, adapter_row[None, :], 0), axis=1)


def rotate_heads(values, positions):
    head_dim = values.shape[-1]
    half_dim = head_dim // 2
    frequency = theta_base ** (-2.0 * jnp.arange(half_dim, dtype=jnp.float32) / head_dim)
    angles = positions.astype(jnp.float32)[:, None] * frequency[None, :]
    cosine = jnp.cos(angles)[:, None, :]
    sine_part = jnp.sin(angles)[:, None, :]
    first_half = values[..., :half_dim]
    second_half = values[..., half_dim:]
    return jnp.concatenate(
        [
            first_half * cosine - second_half * sine_part,
            second_half * cosine + first_half * sine_part,
        ],
        axis=-1,
    )


def attend_heads(queries, key_heads, value_heads, segment_row, sink_row):
    tokens_now, kv_now, group_now, head_dim = queries.shape
    scores = jnp.einsum(
        "tkgh,skh->kgts", queries, key_heads, preferred_element_type=jnp.float32
    ) * head_dim ** (-0.5)
    counter = jnp.arange(tokens_now, dtype=jnp.int32)
    allowed = (segment_row[:, None] == segment_row[None, :]) & (
        counter[None, :] <= counter[:, None]
    )
    weights = jnp.where(allowed[None, None], jnp.exp(scores), 0.0)
    totals = jnp.sum(weights, axis=-1, keepdims=True) + jnp.exp(sink_row).reshape(
        kv_now, group_now, 1, 1
    )
    probs = (weights / totals).astype(jnp.bfloat16)
    blended_hidden = jnp.einsum(
        "kgts,skh->tkgh", probs, value_heads, preferred_element_type=jnp.float32
    )
    return blended_hidden.astype(jnp.bfloat16).reshape(tokens_now, kv_now * group_now * head_dim)


def shards(
    hidden,
    segments,
    request_adapter,
    routes,
    expert_gates,
    attention_gain,
    joined_weight,
    sinks,
    attention_out_weight,
    joined_down_maps,
    joined_up_maps,
    output_down_maps,
    output_up_maps,
    expert_norm_gain,
    expert_gate_weight,
    expert_up_weight,
    expert_down_weight,
    closing_gain,
    vocabulary_weight,
):
    groups = lax.axis_size("dp")
    columns = lax.axis_size("expert")
    position_dp = lax.axis_index("dp")
    segment_row = segments[0]
    adapter_row = request_adapter[0]
    col_tokens = segment_row.shape[0]
    gathered_rows = lax.all_gather(hidden, "dp", axis=1, tiled=True)
    width = gathered_rows.shape[1]
    normalized_hidden = rms_scale(gathered_rows.astype(jnp.float32), attention_gain).astype(
        jnp.bfloat16
    )
    joined_projection = jnp.dot(
        normalized_hidden, joined_weight.reshape(width, -1), preferred_element_type=jnp.float32
    )
    reduced_every_adapter = joined_down_maps.shape[1]
    reduced_hidden = jnp.dot(
        normalized_hidden, joined_down_maps, preferred_element_type=jnp.float32
    ).astype(jnp.bfloat16)
    rank_owner = jnp.arange(reduced_every_adapter, dtype=jnp.int32) // ADAPTER_RANK
    adapter_mask = adapter_per_token(segment_row, adapter_row)[:, None] == rank_owner[None, :]
    selected_reduced = jnp.where(adapter_mask, reduced_hidden, jnp.zeros_like(reduced_hidden))
    joined_projection = joined_projection + adapter_scale * jnp.dot(
        selected_reduced,
        joined_up_maps.reshape(reduced_every_adapter, -1),
        preferred_element_type=jnp.float32,
    )
    kv_here = joined_weight.shape[1]
    joined_projection = joined_projection.reshape(col_tokens, kv_here, QUERY_GROUP + 2, HEAD_SIZE)
    positions = positions_of(segment_row)
    queries = rotate_heads(
        joined_projection[:, :, :QUERY_GROUP].reshape(col_tokens, kv_here * QUERY_GROUP, HEAD_SIZE),
        positions,
    )
    queries = queries.astype(jnp.bfloat16).reshape(col_tokens, kv_here, QUERY_GROUP, HEAD_SIZE)
    key_heads = rotate_heads(joined_projection[:, :, QUERY_GROUP], positions).astype(jnp.bfloat16)
    value_heads = joined_projection[:, :, QUERY_GROUP + 1].astype(jnp.bfloat16)
    blended_hidden = attend_heads(queries, key_heads, value_heads, segment_row, sinks)
    up_full = lax.all_gather(output_up_maps, "dp", axis=1, tiled=True)
    low_local = jnp.dot(blended_hidden, output_down_maps, preferred_element_type=jnp.float32)
    selected_output = jnp.where(adapter_mask, low_local, jnp.zeros_like(low_local))
    partial_out = jnp.dot(
        blended_hidden, attention_out_weight, preferred_element_type=jnp.float32
    ) + adapter_scale * jnp.dot(
        selected_output.astype(jnp.bfloat16), up_full, preferred_element_type=jnp.float32
    )
    mine_out = lax.psum_scatter(
        partial_out.astype(jnp.bfloat16), "dp", scatter_dimension=1, tiled=True
    ).astype(jnp.float32)
    resid = (hidden.astype(jnp.float32) + mine_out).astype(jnp.bfloat16)
    column_full = lax.all_gather(resid, "dp", axis=1, tiled=True)
    moe_in = rms_scale(column_full.astype(jnp.float32), expert_norm_gain).astype(jnp.bfloat16)
    lane_pad = -width % 128
    moe_in = jnp.pad(moe_in, ((0, 0), (0, lane_pad)))
    wide = width + lane_pad
    share = col_tokens // groups
    experts = expert_gate_weight.shape[0] * columns
    capacity = 4 * share * TOP // (3 * experts)
    col_capacity = groups * capacity
    route_pack = jnp.concatenate(
        [routes[0].astype(jnp.bfloat16), expert_gates[0].astype(jnp.bfloat16)], axis=1
    )
    pack_col = lax.all_gather(route_pack, "dp", axis=0, tiled=True)
    route_col = pack_col[:, :TOP].astype(jnp.int32)
    gates_col = pack_col[:, TOP:]
    route_flat = route_col.reshape(-1)
    one_hot = (route_flat[:, None] == jnp.arange(experts, dtype=jnp.int32)[None, :]).astype(
        jnp.int32
    )
    slot_rows = jnp.sum((jnp.cumsum(one_hot, axis=0) - one_hot) * one_hot, axis=1)
    target = route_flat * col_capacity + slot_rows
    source_rows = jnp.arange(route_flat.shape[0], dtype=jnp.int32) // TOP
    table = jnp.full((experts * col_capacity,), col_tokens, jnp.int32).at[target].set(source_rows)
    dispatch = (table[:, None] == jnp.arange(col_tokens, dtype=jnp.int32)[None, :]).astype(
        jnp.bfloat16
    )
    outgoing = (
        jnp.dot(dispatch, moe_in, preferred_element_type=jnp.float32)
        .astype(jnp.bfloat16)
        .reshape(experts, col_capacity, wide)
    )
    gate_weight = expert_gate_weight[0]
    up_weight = expert_up_weight[0]
    down_weight = jnp.pad(expert_down_weight[0], ((0, 0), (0, lane_pad)))
    arrived = lax.all_to_all(outgoing, "expert", split_axis=0, concat_axis=0, tiled=True)
    rows_in = arrived.reshape(-1, wide)[:, :width]
    gate_part = jnp.dot(rows_in, gate_weight, preferred_element_type=jnp.float32)
    up_part = jnp.dot(rows_in, up_weight, preferred_element_type=jnp.float32)
    activated = (gate_part * jax.nn.sigmoid(glu_alpha * gate_part) * (up_part + 1.0)).astype(
        jnp.bfloat16
    )
    shares_out = (
        jnp.dot(activated, down_weight, preferred_element_type=jnp.float32)
        .astype(jnp.bfloat16)
        .reshape(experts, col_capacity, wide)
    )
    answers = lax.all_to_all(shares_out, "expert", split_axis=0, concat_axis=0, tiled=True)
    slot_ids = jnp.arange(experts * col_capacity, dtype=jnp.int32)
    combine = jnp.sum(
        jnp.where(
            target.reshape(col_tokens, TOP)[:, :, None] == slot_ids[None, None, :],
            gates_col[:, :, None],
            jnp.zeros((), jnp.bfloat16),
        ),
        axis=1,
    ).astype(jnp.bfloat16)
    mixture = jnp.dot(
        combine, answers.reshape(experts * col_capacity, wide), preferred_element_type=jnp.float32
    )[:, :width]
    moe_part = lax.psum_scatter(
        mixture.astype(jnp.bfloat16), "dp", scatter_dimension=1, tiled=True
    )
    moe_rounded = moe_part.astype(jnp.float32).astype(jnp.bfloat16)
    hidden_out = (resid.astype(jnp.float32) + moe_rounded.astype(jnp.float32)).astype(jnp.bfloat16)
    counter = jnp.arange(col_tokens, dtype=jnp.int32)
    request_ids = jnp.arange(REQS, dtype=jnp.int32)
    last_index = jnp.max(
        jnp.where(segment_row[None, :] == request_ids[:, None], counter[None, :], -1), axis=1
    )
    chosen = jnp.take(hidden_out, jnp.clip(last_index, 0, col_tokens - 1), axis=0)
    row_full = lax.all_gather(chosen, "dp", axis=1, tiled=True)
    tail_full = lax.all_gather(row_full, "expert", axis=0, tiled=True)
    tail_rows = rms_scale(tail_full.astype(jnp.float32), closing_gain).astype(jnp.bfloat16)
    logits = jnp.dot(tail_rows, vocabulary_weight, preferred_element_type=jnp.float32)
    return (hidden_out, logits)


def solution(mesh):
    in_specs = (
        P("expert", "dp"),
        P("expert", None),
        P("expert", None),
        P("expert", "dp", None),
        P("expert", "dp", None),
        P(),
        P(None, "dp", None),
        P("dp"),
        P("dp", None),
        P(),
        P(None, "dp", None),
        P("dp", None),
        P(None, "dp"),
        P(),
        P("expert", None, "dp"),
        P("expert", None, "dp"),
        P("expert", "dp", None),
        P(),
        P(None, ("dp", "expert")),
    )
    out_specs = (P("expert", "dp"), P(None, ("dp", "expert")))
    return jax.shard_map(shards, mesh=mesh, in_specs=in_specs, out_specs=out_specs, check_vma=False)
```

```python
import jax
import jax.numpy as jnp
from jax import lax
from jax.sharding import PartitionSpec as P

HEAD_SIZE = 64
QUERY_GROUP = 8
TOP = 4
ADAPTER_RANK = 16
REQS = 4


epsilon = 1e-05
theta_base = 150000.0
adapter_scale = 2.0
glu_alpha = 1.702


def rms_scale(values, gain_row):
    mean_square = jnp.mean(values * values, axis=-1, keepdims=True)
    return values * lax.rsqrt(mean_square + epsilon) * gain_row


def positions_of(segment_row):
    counter = jnp.arange(segment_row.shape[0], dtype=jnp.int32)
    starting = jnp.concatenate(
        [jnp.ones((1,), dtype=jnp.bool_), segment_row[1:] != segment_row[:-1]]
    )
    first_index = lax.cummax(jnp.where(starting, counter, 0), axis=0)
    return counter - first_index


def adapter_per_token(segment_row, adapter_row):
    hits = segment_row[:, None] == jnp.arange(adapter_row.shape[0], dtype=jnp.int32)[None, :]
    return jnp.sum(jnp.where(hits, adapter_row[None, :], 0), axis=1)


def rotate_heads(values, positions):
    head_dim = values.shape[-1]
    half_dim = head_dim // 2
    frequency = theta_base ** (-2.0 * jnp.arange(half_dim, dtype=jnp.float32) / head_dim)
    angles = positions.astype(jnp.float32)[:, None] * frequency[None, :]
    cosine = jnp.cos(angles)[:, None, :]
    sine_part = jnp.sin(angles)[:, None, :]
    first_half = values[..., :half_dim]
    second_half = values[..., half_dim:]
    return jnp.concatenate(
        [
            first_half * cosine - second_half * sine_part,
            second_half * cosine + first_half * sine_part,
        ],
        axis=-1,
    )


def attend_heads(queries, key_heads, value_heads, segment_row, sink_row):
    tokens_now, kv_now, group_now, head_dim = queries.shape
    scores = jnp.einsum(
        "tkgh,skh->kgts", queries, key_heads, preferred_element_type=jnp.float32
    ) * head_dim ** (-0.5)
    counter = jnp.arange(tokens_now, dtype=jnp.int32)
    allowed = (segment_row[:, None] == segment_row[None, :]) & (
        counter[None, :] <= counter[:, None]
    )
    weights = jnp.where(allowed[None, None], jnp.exp(scores), 0.0)
    totals = jnp.sum(weights, axis=-1, keepdims=True) + jnp.exp(sink_row).reshape(
        kv_now, group_now, 1, 1
    )
    probs = (weights / totals).astype(jnp.bfloat16)
    blended_hidden = jnp.einsum(
        "kgts,skh->tkgh", probs, value_heads, preferred_element_type=jnp.float32
    )
    return blended_hidden.astype(jnp.bfloat16).reshape(tokens_now, kv_now * group_now * head_dim)


def shards(
    hidden,
    segments,
    request_adapter,
    routes,
    expert_gates,
    attention_gain,
    joined_weight,
    sinks,
    attention_out_weight,
    joined_down_maps,
    joined_up_maps,
    output_down_maps,
    output_up_maps,
    expert_norm_gain,
    expert_gate_weight,
    expert_up_weight,
    expert_down_weight,
    closing_gain,
    vocabulary_weight,
):
    groups = lax.axis_size("dp")
    columns = lax.axis_size("expert")
    position_dp = lax.axis_index("dp")
    segment_row = segments[0]
    adapter_row = request_adapter[0]
    col_tokens = segment_row.shape[0]
    gathered_rows = lax.all_gather(hidden, "dp", axis=1, tiled=True)
    width = gathered_rows.shape[1]
    normalized_hidden = rms_scale(gathered_rows.astype(jnp.float32), attention_gain).astype(
        jnp.bfloat16
    )
    joined_projection = jnp.dot(
        normalized_hidden, joined_weight.reshape(width, -1), preferred_element_type=jnp.float32
    )
    reduced_every_adapter = joined_down_maps.shape[1]
    reduced_hidden = jnp.dot(
        normalized_hidden, joined_down_maps, preferred_element_type=jnp.float32
    ).astype(jnp.bfloat16)
    rank_owner = jnp.arange(reduced_every_adapter, dtype=jnp.int32) // ADAPTER_RANK
    adapter_mask = adapter_per_token(segment_row, adapter_row)[:, None] == rank_owner[None, :]
    selected_reduced = jnp.where(adapter_mask, reduced_hidden, jnp.zeros_like(reduced_hidden))
    joined_projection = joined_projection + adapter_scale * jnp.dot(
        selected_reduced,
        joined_up_maps.reshape(reduced_every_adapter, -1),
        preferred_element_type=jnp.float32,
    )
    kv_here = joined_weight.shape[1]
    joined_projection = joined_projection.reshape(col_tokens, kv_here, QUERY_GROUP + 2, HEAD_SIZE)
    positions = positions_of(segment_row)
    queries = rotate_heads(
        joined_projection[:, :, :QUERY_GROUP].reshape(col_tokens, kv_here * QUERY_GROUP, HEAD_SIZE),
        positions,
    )
    queries = queries.astype(jnp.bfloat16).reshape(col_tokens, kv_here, QUERY_GROUP, HEAD_SIZE)
    key_heads = rotate_heads(joined_projection[:, :, QUERY_GROUP], positions).astype(jnp.bfloat16)
    value_heads = joined_projection[:, :, QUERY_GROUP + 1].astype(jnp.bfloat16)
    blended_hidden = attend_heads(queries, key_heads, value_heads, segment_row, sinks)
    share = col_tokens // groups
    quarter = hidden.shape[1]
    rank_total = output_down_maps.shape[1]
    route_pack = jnp.concatenate(
        [routes[0].astype(jnp.bfloat16), expert_gates[0].astype(jnp.bfloat16)], axis=1
    )
    pack_width = -(quarter + rank_total) % 128 or 128
    route_pack = jnp.pad(route_pack, ((0, 0), (0, pack_width - 2 * TOP)))
    pack_rows = lax.dynamic_update_slice_in_dim(
        jnp.zeros((col_tokens, pack_width), jnp.bfloat16), route_pack, position_dp * share, 0
    )
    partial_out = jnp.dot(blended_hidden, attention_out_weight, preferred_element_type=jnp.float32)
    low_local = jnp.dot(blended_hidden, output_down_maps, preferred_element_type=jnp.float32)
    joined_send = jnp.concatenate(
        [
            partial_out.astype(jnp.bfloat16).reshape(col_tokens, groups, quarter),
            jnp.broadcast_to(
                low_local.astype(jnp.bfloat16)[:, None, :], (col_tokens, groups, rank_total)
            ),
            jnp.broadcast_to(pack_rows[:, None, :], (col_tokens, groups, pack_width)),
        ],
        axis=2,
    ).reshape(col_tokens, -1)
    joined_back = lax.psum_scatter(joined_send, "dp", scatter_dimension=1, tiled=True)
    mine_out = joined_back[:, :quarter].astype(jnp.float32)
    output_reduced = joined_back[:, quarter : quarter + rank_total]
    pack_col = joined_back[:, quarter + rank_total :]
    selected_output = jnp.where(adapter_mask, output_reduced, jnp.zeros_like(output_reduced))
    adapter_delta = adapter_scale * jnp.dot(
        selected_output, output_up_maps, preferred_element_type=jnp.float32
    )
    resid = (hidden.astype(jnp.float32) + mine_out + adapter_delta).astype(jnp.bfloat16)
    column_full = lax.all_gather(resid, "dp", axis=1, tiled=True)
    moe_in = rms_scale(column_full.astype(jnp.float32), expert_norm_gain).astype(jnp.bfloat16)
    lane_pad = -width % 128
    moe_in = jnp.pad(moe_in, ((0, 0), (0, lane_pad)))
    wide = width + lane_pad
    experts = expert_gate_weight.shape[0] * columns
    capacity = 4 * share * TOP // (3 * experts)
    col_capacity = groups * capacity
    route_col = pack_col[:, :TOP].astype(jnp.int32)
    gates_col = pack_col[:, TOP : 2 * TOP]
    route_flat = route_col.reshape(-1)
    one_hot = (route_flat[:, None] == jnp.arange(experts, dtype=jnp.int32)[None, :]).astype(
        jnp.int32
    )
    slot_rows = jnp.sum((jnp.cumsum(one_hot, axis=0) - one_hot) * one_hot, axis=1)
    target = route_flat * col_capacity + slot_rows
    source_rows = jnp.arange(route_flat.shape[0], dtype=jnp.int32) // TOP
    table = jnp.full((experts * col_capacity,), col_tokens, jnp.int32).at[target].set(source_rows)
    table = table.reshape(experts, col_capacity)
    slot_ids = jnp.arange(experts * col_capacity, dtype=jnp.int32).reshape(experts, col_capacity)
    target_tk = target.reshape(col_tokens, TOP)
    gate_weight = expert_gate_weight[0]
    up_weight = expert_up_weight[0]
    down_weight = jnp.pad(expert_down_weight[0], ((0, 0), (0, lane_pad)))
    halves = 2 if col_capacity % 16 == 0 else 1
    piece = col_capacity // halves
    mixture = None
    for h in range(halves):
        table_h = table[:, h * piece : (h + 1) * piece].reshape(-1)
        dispatch = (table_h[:, None] == jnp.arange(col_tokens, dtype=jnp.int32)[None, :]).astype(
            jnp.bfloat16
        )
        outgoing = (
            jnp.dot(dispatch, moe_in, preferred_element_type=jnp.float32)
            .astype(jnp.bfloat16)
            .reshape(experts, piece, wide)
        )
        arrived = lax.all_to_all(outgoing, "expert", split_axis=0, concat_axis=0, tiled=True)
        rows_in = arrived.reshape(-1, wide)[:, :width]
        gate_part = jnp.dot(rows_in, gate_weight, preferred_element_type=jnp.float32)
        up_part = jnp.dot(rows_in, up_weight, preferred_element_type=jnp.float32)
        activated = (gate_part * jax.nn.sigmoid(glu_alpha * gate_part) * (up_part + 1.0)).astype(
            jnp.bfloat16
        )
        shares_out = (
            jnp.dot(activated, down_weight, preferred_element_type=jnp.float32)
            .astype(jnp.bfloat16)
            .reshape(experts, piece, wide)
        )
        answers = lax.all_to_all(shares_out, "expert", split_axis=0, concat_axis=0, tiled=True)
        slots_h = slot_ids[:, h * piece : (h + 1) * piece].reshape(-1)
        combine = jnp.sum(
            jnp.where(
                target_tk[:, :, None] == slots_h[None, None, :],
                gates_col[:, :, None],
                jnp.zeros((), jnp.bfloat16),
            ),
            axis=1,
        ).astype(jnp.bfloat16)
        part = jnp.dot(
            combine, answers.reshape(experts * piece, wide), preferred_element_type=jnp.float32
        )
        mixture = part if mixture is None else mixture + part
    mixture = mixture[:, :width]
    counter = jnp.arange(col_tokens, dtype=jnp.int32)
    request_ids = jnp.arange(REQS, dtype=jnp.int32)
    last_index = jnp.max(
        jnp.where(segment_row[None, :] == request_ids[:, None], counter[None, :], -1), axis=1
    )
    last_index = jnp.clip(last_index, 0, col_tokens - 1)
    last_mix = jnp.take(mixture, last_index, axis=0).reshape(REQS * groups, quarter)
    moe_send = jnp.concatenate(
        [mixture, jnp.tile(last_mix, (1, groups))], axis=0
    ).astype(jnp.bfloat16)
    moe_back = lax.psum_scatter(moe_send, "dp", scatter_dimension=1, tiled=True)
    moe_rounded = moe_back[:col_tokens].astype(jnp.float32).astype(jnp.bfloat16)
    hidden_out = (resid.astype(jnp.float32) + moe_rounded.astype(jnp.float32)).astype(jnp.bfloat16)
    last_moe = moe_back[col_tokens:].reshape(REQS, width)
    last_resid = jnp.take(column_full, last_index, axis=0)
    last_hidden = (last_resid.astype(jnp.float32) + last_moe.astype(jnp.float32)).astype(
        jnp.bfloat16
    )
    ends = rms_scale(last_hidden.astype(jnp.float32), closing_gain).astype(jnp.bfloat16)
    tail_rows = lax.all_gather(ends, "expert", axis=0, tiled=True)
    logits = jnp.dot(tail_rows, vocabulary_weight, preferred_element_type=jnp.float32)
    return (hidden_out, logits)


def solution(mesh):
    in_specs = (
        P("expert", "dp"),
        P("expert", None),
        P("expert", None),
        P("expert", "dp", None),
        P("expert", "dp", None),
        P(),
        P(None, "dp", None),
        P("dp"),
        P("dp", None),
        P(),
        P(None, "dp", None),
        P("dp", None),
        P(None, "dp"),
        P(),
        P("expert", None, "dp"),
        P("expert", None, "dp"),
        P("expert", "dp", None),
        P(),
        P(None, ("dp", "expert")),
    )
    out_specs = (P("expert", "dp"), P(None, ("dp", "expert")))
    return jax.shard_map(shards, mesh=mesh, in_specs=in_specs, out_specs=out_specs, check_vma=False)
```

```python
import jax
import jax.numpy as jnp
from jax import lax
from jax.sharding import PartitionSpec as P

HEAD_SIZE = 64
QUERY_GROUP = 8
TOP = 4
ADAPTER_RANK = 16
REQS = 4


epsilon = 1e-05
theta_base = 150000.0
adapter_scale = 2.0
glu_alpha = 1.702


def rms_scale(values, gain_row):
    mean_square = jnp.mean(values * values, axis=-1, keepdims=True)
    return values * lax.rsqrt(mean_square + epsilon) * gain_row


def positions_of(segment_row):
    counter = jnp.arange(segment_row.shape[0], dtype=jnp.int32)
    starting = jnp.concatenate(
        [jnp.ones((1,), dtype=jnp.bool_), segment_row[1:] != segment_row[:-1]]
    )
    first_index = lax.cummax(jnp.where(starting, counter, 0), axis=0)
    return counter - first_index


def adapter_per_token(segment_row, adapter_row):
    hits = segment_row[:, None] == jnp.arange(adapter_row.shape[0], dtype=jnp.int32)[None, :]
    return jnp.sum(jnp.where(hits, adapter_row[None, :], 0), axis=1)


def rotate_heads(values, positions):
    head_dim = values.shape[-1]
    half_dim = head_dim // 2
    frequency = theta_base ** (-2.0 * jnp.arange(half_dim, dtype=jnp.float32) / head_dim)
    angles = positions.astype(jnp.float32)[:, None] * frequency[None, :]
    cosine = jnp.cos(angles)[:, None, :]
    sine_part = jnp.sin(angles)[:, None, :]
    first_half = values[..., :half_dim]
    second_half = values[..., half_dim:]
    return jnp.concatenate(
        [
            first_half * cosine - second_half * sine_part,
            second_half * cosine + first_half * sine_part,
        ],
        axis=-1,
    )


def attend_heads(queries, key_heads, value_heads, segment_row, sink_row):
    tokens_now, kv_now, group_now, head_dim = queries.shape
    scores = jnp.einsum(
        "tkgh,skh->kgts", queries, key_heads, preferred_element_type=jnp.float32
    ) * head_dim ** (-0.5)
    counter = jnp.arange(tokens_now, dtype=jnp.int32)
    allowed = (segment_row[:, None] == segment_row[None, :]) & (
        counter[None, :] <= counter[:, None]
    )
    weights = jnp.where(allowed[None, None], jnp.exp(scores), 0.0)
    totals = jnp.sum(weights, axis=-1, keepdims=True) + jnp.exp(sink_row).reshape(
        kv_now, group_now, 1, 1
    )
    probs = (weights / totals).astype(jnp.bfloat16)
    blended_hidden = jnp.einsum(
        "kgts,skh->tkgh", probs, value_heads, preferred_element_type=jnp.float32
    )
    return blended_hidden.astype(jnp.bfloat16).reshape(tokens_now, kv_now * group_now * head_dim)


def shards(
    hidden,
    segments,
    request_adapter,
    routes,
    expert_gates,
    attention_gain,
    joined_weight,
    sinks,
    attention_out_weight,
    joined_down_maps,
    joined_up_maps,
    output_down_maps,
    output_up_maps,
    expert_norm_gain,
    expert_gate_weight,
    expert_up_weight,
    expert_down_weight,
    closing_gain,
    vocabulary_weight,
):
    groups = lax.axis_size("dp")
    columns = lax.axis_size("expert")
    position_dp = lax.axis_index("dp")
    segment_row = segments[0]
    adapter_row = request_adapter[0]
    col_tokens = segment_row.shape[0]
    gathered_rows = lax.all_gather(hidden, "dp", axis=1, tiled=True)
    width = gathered_rows.shape[1]
    normalized_hidden = rms_scale(gathered_rows.astype(jnp.float32), attention_gain).astype(
        jnp.bfloat16
    )
    joined_projection = jnp.dot(
        normalized_hidden, joined_weight.reshape(width, -1), preferred_element_type=jnp.float32
    )
    reduced_every_adapter = joined_down_maps.shape[1]
    reduced_hidden = jnp.dot(
        normalized_hidden, joined_down_maps, preferred_element_type=jnp.float32
    ).astype(jnp.bfloat16)
    rank_owner = jnp.arange(reduced_every_adapter, dtype=jnp.int32) // ADAPTER_RANK
    adapter_mask = adapter_per_token(segment_row, adapter_row)[:, None] == rank_owner[None, :]
    selected_reduced = jnp.where(adapter_mask, reduced_hidden, jnp.zeros_like(reduced_hidden))
    joined_projection = joined_projection + adapter_scale * jnp.dot(
        selected_reduced,
        joined_up_maps.reshape(reduced_every_adapter, -1),
        preferred_element_type=jnp.float32,
    )
    kv_here = joined_weight.shape[1]
    joined_projection = joined_projection.reshape(col_tokens, kv_here, QUERY_GROUP + 2, HEAD_SIZE)
    positions = positions_of(segment_row)
    queries = rotate_heads(
        joined_projection[:, :, :QUERY_GROUP].reshape(col_tokens, kv_here * QUERY_GROUP, HEAD_SIZE),
        positions,
    )
    queries = queries.astype(jnp.bfloat16).reshape(col_tokens, kv_here, QUERY_GROUP, HEAD_SIZE)
    key_heads = rotate_heads(joined_projection[:, :, QUERY_GROUP], positions).astype(jnp.bfloat16)
    value_heads = joined_projection[:, :, QUERY_GROUP + 1].astype(jnp.bfloat16)
    blended_hidden = attend_heads(queries, key_heads, value_heads, segment_row, sinks)
    share = col_tokens // groups
    quarter = hidden.shape[1]
    rank_total = output_down_maps.shape[1]
    route_pack = jnp.concatenate(
        [routes[0].astype(jnp.bfloat16), expert_gates[0].astype(jnp.bfloat16)], axis=1
    )
    pack_width = -(quarter + rank_total) % 128 or 128
    route_pack = jnp.pad(route_pack, ((0, 0), (0, pack_width - 2 * TOP)))
    pack_rows = lax.dynamic_update_slice_in_dim(
        jnp.zeros((col_tokens, pack_width), jnp.bfloat16), route_pack, position_dp * share, 0
    )
    partial_out = jnp.dot(blended_hidden, attention_out_weight, preferred_element_type=jnp.float32)
    low_local = jnp.dot(blended_hidden, output_down_maps, preferred_element_type=jnp.float32)
    joined_send = jnp.concatenate(
        [
            partial_out.astype(jnp.bfloat16).reshape(col_tokens, groups, quarter),
            jnp.broadcast_to(
                low_local.astype(jnp.bfloat16)[:, None, :], (col_tokens, groups, rank_total)
            ),
            jnp.broadcast_to(pack_rows[:, None, :], (col_tokens, groups, pack_width)),
        ],
        axis=2,
    ).reshape(col_tokens, -1)
    joined_back = lax.psum_scatter(joined_send, "dp", scatter_dimension=1, tiled=True)
    mine_out = joined_back[:, :quarter].astype(jnp.float32)
    output_reduced = joined_back[:, quarter : quarter + rank_total]
    pack_col = joined_back[:, quarter + rank_total :]
    selected_output = jnp.where(adapter_mask, output_reduced, jnp.zeros_like(output_reduced))
    adapter_delta = adapter_scale * jnp.dot(
        selected_output, output_up_maps, preferred_element_type=jnp.float32
    )
    resid = (hidden.astype(jnp.float32) + mine_out + adapter_delta).astype(jnp.bfloat16)
    lane_pad = -width % 128
    wide = width + lane_pad
    experts = expert_gate_weight.shape[0] * columns
    capacity = 4 * share * TOP // (3 * experts)
    gate_weight = expert_gate_weight[0]
    up_weight = expert_up_weight[0]
    down_weight = jnp.pad(expert_down_weight[0], ((0, 0), (0, lane_pad)))
    halves = 2 if groups % 2 == 0 else 1
    half_tokens = col_tokens // halves
    half_capacity = (groups // halves) * capacity
    counter = jnp.arange(col_tokens, dtype=jnp.int32)
    request_ids = jnp.arange(REQS, dtype=jnp.int32)
    last_index = jnp.max(
        jnp.where(segment_row[None, :] == request_ids[:, None], counter[None, :], -1), axis=1
    )
    last_index = jnp.clip(last_index, 0, col_tokens - 1)
    moe_rows = []
    last_parts = []
    last_resid_parts = []
    held = None
    for h in range(halves):
        lo = h * half_tokens
        resid_h = resid[lo : lo + half_tokens]
        column_h = lax.all_gather(resid_h, "dp", axis=1, tiled=True)
        if held is not None:
            column_h, held = lax.optimization_barrier((column_h, held))
        moe_in = rms_scale(column_h.astype(jnp.float32), expert_norm_gain).astype(jnp.bfloat16)
        moe_in = jnp.pad(moe_in, ((0, 0), (0, lane_pad)))
        pack_h = pack_col[lo : lo + half_tokens]
        route_flat = pack_h[:, :TOP].astype(jnp.int32).reshape(-1)
        gates_h = pack_h[:, TOP : 2 * TOP]
        one_hot = (route_flat[:, None] == jnp.arange(experts, dtype=jnp.int32)[None, :]).astype(
            jnp.int32
        )
        slot_rows = jnp.sum((jnp.cumsum(one_hot, axis=0) - one_hot) * one_hot, axis=1)
        target = route_flat * half_capacity + slot_rows
        source_rows = jnp.arange(route_flat.shape[0], dtype=jnp.int32) // TOP
        table = (
            jnp.full((experts * half_capacity,), half_tokens, jnp.int32)
            .at[target]
            .set(source_rows)
        )
        dispatch = (table[:, None] == jnp.arange(half_tokens, dtype=jnp.int32)[None, :]).astype(
            jnp.bfloat16
        )
        outgoing = (
            jnp.dot(dispatch, moe_in, preferred_element_type=jnp.float32)
            .astype(jnp.bfloat16)
            .reshape(experts, half_capacity, wide)
        )
        arrived = lax.all_to_all(outgoing, "expert", split_axis=0, concat_axis=0, tiled=True)
        if h == 0:
            held = arrived
        else:
            arrived = lax.optimization_barrier((arrived, held))[0]
        rows_in = arrived.reshape(-1, wide)[:, :width]
        gate_part = jnp.dot(rows_in, gate_weight, preferred_element_type=jnp.float32)
        up_part = jnp.dot(rows_in, up_weight, preferred_element_type=jnp.float32)
        activated = (gate_part * jax.nn.sigmoid(glu_alpha * gate_part) * (up_part + 1.0)).astype(
            jnp.bfloat16
        )
        shares_out = (
            jnp.dot(activated, down_weight, preferred_element_type=jnp.float32)
            .astype(jnp.bfloat16)
            .reshape(experts, half_capacity, wide)
        )
        answers = lax.all_to_all(shares_out, "expert", split_axis=0, concat_axis=0, tiled=True)
        slot_ids = jnp.arange(experts * half_capacity, dtype=jnp.int32)
        combine = jnp.sum(
            jnp.where(
                target.reshape(half_tokens, TOP)[:, :, None] == slot_ids[None, None, :],
                gates_h[:, :, None],
                jnp.zeros((), jnp.bfloat16),
            ),
            axis=1,
        ).astype(jnp.bfloat16)
        mixture = jnp.dot(
            combine,
            answers.reshape(experts * half_capacity, wide),
            preferred_element_type=jnp.float32,
        )[:, :width]
        local_last = jnp.clip(last_index - lo, 0, half_tokens - 1)
        inside = ((last_index >= lo) & (last_index < lo + half_tokens))[:, None]
        last_parts.append(
            jnp.where(inside, jnp.take(mixture, local_last, axis=0), jnp.zeros((), jnp.float32))
        )
        last_resid_parts.append(
            jnp.where(inside, jnp.take(column_h, local_last, axis=0), jnp.zeros((), jnp.bfloat16))
        )
        if h < halves - 1:
            moe_send = mixture.astype(jnp.bfloat16)
        else:
            last_mix = sum(last_parts).reshape(REQS * groups, quarter)
            moe_send = jnp.concatenate(
                [mixture, jnp.tile(last_mix, (1, groups))], axis=0
            ).astype(jnp.bfloat16)
        moe_rows.append(lax.psum_scatter(moe_send, "dp", scatter_dimension=1, tiled=True))
    moe_back = jnp.concatenate(moe_rows, axis=0)
    moe_rounded = moe_back[:col_tokens].astype(jnp.float32).astype(jnp.bfloat16)
    hidden_out = (resid.astype(jnp.float32) + moe_rounded.astype(jnp.float32)).astype(jnp.bfloat16)
    last_moe = moe_back[col_tokens:].reshape(REQS, width)
    last_resid = sum(part.astype(jnp.float32) for part in last_resid_parts)
    last_hidden = (last_resid + last_moe.astype(jnp.float32)).astype(jnp.bfloat16)
    ends = rms_scale(last_hidden.astype(jnp.float32), closing_gain).astype(jnp.bfloat16)
    tail_rows = lax.all_gather(ends, "expert", axis=0, tiled=True)
    logits = jnp.dot(tail_rows, vocabulary_weight, preferred_element_type=jnp.float32)
    return (hidden_out, logits)


def solution(mesh):
    in_specs = (
        P("expert", "dp"),
        P("expert", None),
        P("expert", None),
        P("expert", "dp", None),
        P("expert", "dp", None),
        P(),
        P(None, "dp", None),
        P("dp"),
        P("dp", None),
        P(),
        P(None, "dp", None),
        P("dp", None),
        P(None, "dp"),
        P(),
        P("expert", None, "dp"),
        P("expert", None, "dp"),
        P("expert", "dp", None),
        P(),
        P(None, ("dp", "expert")),
    )
    out_specs = (P("expert", "dp"), P(None, ("dp", "expert")))
    return jax.shard_map(shards, mesh=mesh, in_specs=in_specs, out_specs=out_specs, check_vma=False)
```

```python
import jax
import jax.numpy as jnp
from jax import lax
from jax.sharding import PartitionSpec as P

HEAD_SIZE = 64
QUERY_GROUP = 8
TOP = 4
ADAPTER_RANK = 16
REQS = 4


epsilon = 1e-05
theta_base = 150000.0
adapter_scale = 2.0
glu_alpha = 1.702


def rms_scale(values, gain_row):
    mean_square = jnp.mean(values * values, axis=-1, keepdims=True)
    return values * lax.rsqrt(mean_square + epsilon) * gain_row


def positions_of(segment_row):
    counter = jnp.arange(segment_row.shape[0], dtype=jnp.int32)
    starting = jnp.concatenate(
        [jnp.ones((1,), dtype=jnp.bool_), segment_row[1:] != segment_row[:-1]]
    )
    first_index = lax.cummax(jnp.where(starting, counter, 0), axis=0)
    return counter - first_index


def adapter_per_token(segment_row, adapter_row):
    hits = segment_row[:, None] == jnp.arange(adapter_row.shape[0], dtype=jnp.int32)[None, :]
    return jnp.sum(jnp.where(hits, adapter_row[None, :], 0), axis=1)


def rotate_heads(values, positions):
    head_dim = values.shape[-1]
    half_dim = head_dim // 2
    frequency = theta_base ** (-2.0 * jnp.arange(half_dim, dtype=jnp.float32) / head_dim)
    angles = positions.astype(jnp.float32)[:, None] * frequency[None, :]
    cosine = jnp.cos(angles)[:, None, :]
    sine_part = jnp.sin(angles)[:, None, :]
    first_half = values[..., :half_dim]
    second_half = values[..., half_dim:]
    return jnp.concatenate(
        [
            first_half * cosine - second_half * sine_part,
            second_half * cosine + first_half * sine_part,
        ],
        axis=-1,
    )


def attend_heads(queries, key_heads, value_heads, segment_row, sink_row):
    tokens_now, kv_now, group_now, head_dim = queries.shape
    scores = jnp.einsum(
        "tkgh,skh->kgts", queries, key_heads, preferred_element_type=jnp.float32
    ) * head_dim ** (-0.5)
    counter = jnp.arange(tokens_now, dtype=jnp.int32)
    allowed = (segment_row[:, None] == segment_row[None, :]) & (
        counter[None, :] <= counter[:, None]
    )
    weights = jnp.where(allowed[None, None], jnp.exp(scores), 0.0)
    totals = jnp.sum(weights, axis=-1, keepdims=True) + jnp.exp(sink_row).reshape(
        kv_now, group_now, 1, 1
    )
    probs = (weights / totals).astype(jnp.bfloat16)
    blended_hidden = jnp.einsum(
        "kgts,skh->tkgh", probs, value_heads, preferred_element_type=jnp.float32
    )
    return blended_hidden.astype(jnp.bfloat16).reshape(tokens_now, kv_now * group_now * head_dim)


def shards(
    hidden,
    segments,
    request_adapter,
    routes,
    expert_gates,
    attention_gain,
    joined_weight,
    sinks,
    attention_out_weight,
    joined_down_maps,
    joined_up_maps,
    output_down_maps,
    output_up_maps,
    expert_norm_gain,
    expert_gate_weight,
    expert_up_weight,
    expert_down_weight,
    closing_gain,
    vocabulary_weight,
):
    groups = lax.axis_size("dp")
    columns = lax.axis_size("expert")
    position_dp = lax.axis_index("dp")
    segment_row = segments[0]
    adapter_row = request_adapter[0]
    col_tokens = segment_row.shape[0]
    gathered_rows = lax.all_gather(hidden, "dp", axis=1, tiled=True)
    width = gathered_rows.shape[1]
    normalized_hidden = rms_scale(gathered_rows.astype(jnp.float32), attention_gain).astype(
        jnp.bfloat16
    )
    joined_projection = jnp.dot(
        normalized_hidden, joined_weight.reshape(width, -1), preferred_element_type=jnp.float32
    )
    reduced_every_adapter = joined_down_maps.shape[1]
    reduced_hidden = jnp.dot(
        normalized_hidden, joined_down_maps, preferred_element_type=jnp.float32
    ).astype(jnp.bfloat16)
    rank_owner = jnp.arange(reduced_every_adapter, dtype=jnp.int32) // ADAPTER_RANK
    adapter_mask = adapter_per_token(segment_row, adapter_row)[:, None] == rank_owner[None, :]
    selected_reduced = jnp.where(adapter_mask, reduced_hidden, jnp.zeros_like(reduced_hidden))
    joined_projection = joined_projection + adapter_scale * jnp.dot(
        selected_reduced,
        joined_up_maps.reshape(reduced_every_adapter, -1),
        preferred_element_type=jnp.float32,
    )
    kv_here = joined_weight.shape[1]
    joined_projection = joined_projection.reshape(col_tokens, kv_here, QUERY_GROUP + 2, HEAD_SIZE)
    positions = positions_of(segment_row)
    queries = rotate_heads(
        joined_projection[:, :, :QUERY_GROUP].reshape(col_tokens, kv_here * QUERY_GROUP, HEAD_SIZE),
        positions,
    )
    queries = queries.astype(jnp.bfloat16).reshape(col_tokens, kv_here, QUERY_GROUP, HEAD_SIZE)
    key_heads = rotate_heads(joined_projection[:, :, QUERY_GROUP], positions).astype(jnp.bfloat16)
    value_heads = joined_projection[:, :, QUERY_GROUP + 1].astype(jnp.bfloat16)
    blended_hidden = attend_heads(queries, key_heads, value_heads, segment_row, sinks)
    share = col_tokens // groups
    quarter = hidden.shape[1]
    rank_total = output_down_maps.shape[1]
    route_pack = jnp.concatenate(
        [routes[0].astype(jnp.bfloat16), expert_gates[0].astype(jnp.bfloat16)], axis=1
    )
    pack_width = -(quarter + rank_total) % 128 or 128
    route_pack = jnp.pad(route_pack, ((0, 0), (0, pack_width - 2 * TOP)))
    pack_rows = lax.dynamic_update_slice_in_dim(
        jnp.zeros((col_tokens, pack_width), jnp.bfloat16), route_pack, position_dp * share, 0
    )
    partial_out = jnp.dot(blended_hidden, attention_out_weight, preferred_element_type=jnp.float32)
    low_local = jnp.dot(blended_hidden, output_down_maps, preferred_element_type=jnp.float32)
    joined_send = jnp.concatenate(
        [
            partial_out.astype(jnp.bfloat16).reshape(col_tokens, groups, quarter),
            jnp.broadcast_to(
                low_local.astype(jnp.bfloat16)[:, None, :], (col_tokens, groups, rank_total)
            ),
            jnp.broadcast_to(pack_rows[:, None, :], (col_tokens, groups, pack_width)),
        ],
        axis=2,
    ).reshape(col_tokens, -1)
    reduced_parts = []

    def reduce_rows(lo, rows):
        joined_back = lax.psum_scatter(
            joined_send[lo : lo + rows], "dp", scatter_dimension=1, tiled=True
        )
        return joined_back

    def resid_rows(joined_back, lo, rows):
        mine_out = joined_back[:, :quarter].astype(jnp.float32)
        output_reduced = joined_back[:, quarter : quarter + rank_total]
        selected_output = jnp.where(
            adapter_mask[lo : lo + rows], output_reduced, jnp.zeros_like(output_reduced)
        )
        adapter_delta = adapter_scale * jnp.dot(
            selected_output, output_up_maps, preferred_element_type=jnp.float32
        )
        resid_part = (
            hidden[lo : lo + rows].astype(jnp.float32) + mine_out + adapter_delta
        ).astype(jnp.bfloat16)
        return resid_part, joined_back[:, quarter + rank_total :]

    lane_pad = -width % 128
    wide = width + lane_pad
    experts = expert_gate_weight.shape[0] * columns
    capacity = 4 * share * TOP // (3 * experts)
    gate_weight = expert_gate_weight[0]
    up_weight = expert_up_weight[0]
    down_weight = jnp.pad(expert_down_weight[0], ((0, 0), (0, lane_pad)))
    halves = 2 if groups % 2 == 0 else 1
    half_tokens = col_tokens // halves
    half_capacity = (groups // halves) * capacity
    counter = jnp.arange(col_tokens, dtype=jnp.int32)
    request_ids = jnp.arange(REQS, dtype=jnp.int32)
    last_index = jnp.max(
        jnp.where(segment_row[None, :] == request_ids[:, None], counter[None, :], -1), axis=1
    )
    last_index = jnp.clip(last_index, 0, col_tokens - 1)
    moe_rows = []
    last_parts = []
    last_resid_parts = []
    held = None
    pending = None
    for h in range(halves):
        lo = h * half_tokens
        joined_h = reduce_rows(lo, half_tokens)
        if held is not None:
            joined_h, held = lax.optimization_barrier((joined_h, held))
        resid_h, pack_h = resid_rows(joined_h, lo, half_tokens)
        reduced_parts.append(resid_h)
        column_h = lax.all_gather(resid_h, "dp", axis=1, tiled=True)
        if held is not None:
            column_h, held = lax.optimization_barrier((column_h, held))
        moe_in = rms_scale(column_h.astype(jnp.float32), expert_norm_gain).astype(jnp.bfloat16)
        moe_in = jnp.pad(moe_in, ((0, 0), (0, lane_pad)))
        route_flat = pack_h[:, :TOP].astype(jnp.int32).reshape(-1)
        gates_h = pack_h[:, TOP : 2 * TOP]
        one_hot = (route_flat[:, None] == jnp.arange(experts, dtype=jnp.int32)[None, :]).astype(
            jnp.int32
        )
        slot_rows = jnp.sum((jnp.cumsum(one_hot, axis=0) - one_hot) * one_hot, axis=1)
        target = route_flat * half_capacity + slot_rows
        source_rows = jnp.arange(route_flat.shape[0], dtype=jnp.int32) // TOP
        table = (
            jnp.full((experts * half_capacity,), half_tokens, jnp.int32)
            .at[target]
            .set(source_rows)
        )
        dispatch = (table[:, None] == jnp.arange(half_tokens, dtype=jnp.int32)[None, :]).astype(
            jnp.bfloat16
        )
        outgoing = (
            jnp.dot(dispatch, moe_in, preferred_element_type=jnp.float32)
            .astype(jnp.bfloat16)
            .reshape(experts, half_capacity, wide)
        )
        arrived = lax.all_to_all(outgoing, "expert", split_axis=0, concat_axis=0, tiled=True)
        if h == 0:
            held = arrived
        else:
            arrived = lax.optimization_barrier((arrived, held))[0]
        rows_in = arrived.reshape(-1, wide)[:, :width]
        gate_part = jnp.dot(rows_in, gate_weight, preferred_element_type=jnp.float32)
        up_part = jnp.dot(rows_in, up_weight, preferred_element_type=jnp.float32)
        activated = (gate_part * jax.nn.sigmoid(glu_alpha * gate_part) * (up_part + 1.0)).astype(
            jnp.bfloat16
        )
        shares_out = (
            jnp.dot(activated, down_weight, preferred_element_type=jnp.float32)
            .astype(jnp.bfloat16)
            .reshape(experts, half_capacity, wide)
        )
        if pending is not None:
            shares_out, pending = lax.optimization_barrier((shares_out, pending))
            moe_rows.append(lax.psum_scatter(pending, "dp", scatter_dimension=1, tiled=True))
            pending = None
        answers = lax.all_to_all(shares_out, "expert", split_axis=0, concat_axis=0, tiled=True)
        slot_ids = jnp.arange(experts * half_capacity, dtype=jnp.int32)
        combine = jnp.sum(
            jnp.where(
                target.reshape(half_tokens, TOP)[:, :, None] == slot_ids[None, None, :],
                gates_h[:, :, None],
                jnp.zeros((), jnp.bfloat16),
            ),
            axis=1,
        ).astype(jnp.bfloat16)
        mixture = jnp.dot(
            combine,
            answers.reshape(experts * half_capacity, wide),
            preferred_element_type=jnp.float32,
        )[:, :width]
        local_last = jnp.clip(last_index - lo, 0, half_tokens - 1)
        inside = ((last_index >= lo) & (last_index < lo + half_tokens))[:, None]
        last_parts.append(
            jnp.where(inside, jnp.take(mixture, local_last, axis=0), jnp.zeros((), jnp.float32))
        )
        last_resid_parts.append(
            jnp.where(inside, jnp.take(column_h, local_last, axis=0), jnp.zeros((), jnp.bfloat16))
        )
        if h < halves - 1:
            pending = mixture.astype(jnp.bfloat16)
        else:
            last_mix = sum(last_parts).reshape(REQS * groups, quarter)
            moe_send = jnp.concatenate(
                [mixture, jnp.tile(last_mix, (1, groups))], axis=0
            ).astype(jnp.bfloat16)
            moe_rows.append(lax.psum_scatter(moe_send, "dp", scatter_dimension=1, tiled=True))
    moe_back = jnp.concatenate(moe_rows, axis=0)
    moe_rounded = moe_back[:col_tokens].astype(jnp.float32).astype(jnp.bfloat16)
    resid = jnp.concatenate(reduced_parts, axis=0)
    hidden_out = (resid.astype(jnp.float32) + moe_rounded.astype(jnp.float32)).astype(jnp.bfloat16)
    last_moe = moe_back[col_tokens:].reshape(REQS, width)
    last_resid = sum(part.astype(jnp.float32) for part in last_resid_parts)
    last_hidden = (last_resid + last_moe.astype(jnp.float32)).astype(jnp.bfloat16)
    ends = rms_scale(last_hidden.astype(jnp.float32), closing_gain).astype(jnp.bfloat16)
    tail_rows = lax.all_gather(ends, "expert", axis=0, tiled=True)
    logits = jnp.dot(tail_rows, vocabulary_weight, preferred_element_type=jnp.float32)
    return (hidden_out, logits)


def solution(mesh):
    in_specs = (
        P("expert", "dp"),
        P("expert", None),
        P("expert", None),
        P("expert", "dp", None),
        P("expert", "dp", None),
        P(),
        P(None, "dp", None),
        P("dp"),
        P("dp", None),
        P(),
        P(None, "dp", None),
        P("dp", None),
        P(None, "dp"),
        P(),
        P("expert", None, "dp"),
        P("expert", None, "dp"),
        P("expert", "dp", None),
        P(),
        P(None, ("dp", "expert")),
    )
    out_specs = (P("expert", "dp"), P(None, ("dp", "expert")))
    return jax.shard_map(shards, mesh=mesh, in_specs=in_specs, out_specs=out_specs, check_vma=False)
```

```python
import jax
import jax.numpy as jnp
from jax import lax
from jax.sharding import PartitionSpec as P

HEAD_SIZE = 64
QUERY_GROUP = 8
TOP = 4
ADAPTER_RANK = 16
REQS = 4


epsilon = 1e-05
theta_base = 150000.0
adapter_scale = 2.0
glu_alpha = 1.702


def rms_scale(values, gain_row):
    mean_square = jnp.mean(values * values, axis=-1, keepdims=True)
    return values * lax.rsqrt(mean_square + epsilon) * gain_row


def positions_of(segment_row):
    counter = jnp.arange(segment_row.shape[0], dtype=jnp.int32)
    starting = jnp.concatenate(
        [jnp.ones((1,), dtype=jnp.bool_), segment_row[1:] != segment_row[:-1]]
    )
    first_index = lax.cummax(jnp.where(starting, counter, 0), axis=0)
    return counter - first_index


def adapter_per_token(segment_row, adapter_row):
    hits = segment_row[:, None] == jnp.arange(adapter_row.shape[0], dtype=jnp.int32)[None, :]
    return jnp.sum(jnp.where(hits, adapter_row[None, :], 0), axis=1)


def rotate_heads(values, positions):
    head_dim = values.shape[-1]
    half_dim = head_dim // 2
    frequency = theta_base ** (-2.0 * jnp.arange(half_dim, dtype=jnp.float32) / head_dim)
    angles = positions.astype(jnp.float32)[:, None] * frequency[None, :]
    cosine = jnp.cos(angles)[:, None, :]
    sine_part = jnp.sin(angles)[:, None, :]
    first_half = values[..., :half_dim]
    second_half = values[..., half_dim:]
    return jnp.concatenate(
        [
            first_half * cosine - second_half * sine_part,
            second_half * cosine + first_half * sine_part,
        ],
        axis=-1,
    )


def attend_heads(queries, key_heads, value_heads, segment_row, sink_row):
    tokens_now, kv_now, group_now, head_dim = queries.shape
    scores = jnp.einsum(
        "tkgh,skh->kgts", queries, key_heads, preferred_element_type=jnp.float32
    ) * head_dim ** (-0.5)
    counter = jnp.arange(tokens_now, dtype=jnp.int32)
    allowed = (segment_row[:, None] == segment_row[None, :]) & (
        counter[None, :] <= counter[:, None]
    )
    weights = jnp.where(allowed[None, None], jnp.exp(scores), 0.0)
    totals = jnp.sum(weights, axis=-1, keepdims=True) + jnp.exp(sink_row).reshape(
        kv_now, group_now, 1, 1
    )
    probs = (weights / totals).astype(jnp.bfloat16)
    blended_hidden = jnp.einsum(
        "kgts,skh->tkgh", probs, value_heads, preferred_element_type=jnp.float32
    )
    return blended_hidden.astype(jnp.bfloat16).reshape(tokens_now, kv_now * group_now * head_dim)


def shards(
    hidden,
    segments,
    request_adapter,
    routes,
    expert_gates,
    attention_gain,
    joined_weight,
    sinks,
    attention_out_weight,
    joined_down_maps,
    joined_up_maps,
    output_down_maps,
    output_up_maps,
    expert_norm_gain,
    expert_gate_weight,
    expert_up_weight,
    expert_down_weight,
    closing_gain,
    vocabulary_weight,
):
    groups = lax.axis_size("dp")
    columns = lax.axis_size("expert")
    position_dp = lax.axis_index("dp")
    segment_row = segments[0]
    adapter_row = request_adapter[0]
    col_tokens = segment_row.shape[0]
    gathered_rows = lax.all_gather(hidden, "dp", axis=1, tiled=True)
    width = gathered_rows.shape[1]
    normalized_hidden = rms_scale(gathered_rows.astype(jnp.float32), attention_gain).astype(
        jnp.bfloat16
    )
    joined_projection = jnp.dot(
        normalized_hidden, joined_weight.reshape(width, -1), preferred_element_type=jnp.float32
    )
    reduced_every_adapter = joined_down_maps.shape[1]
    reduced_hidden = jnp.dot(
        normalized_hidden, joined_down_maps, preferred_element_type=jnp.float32
    ).astype(jnp.bfloat16)
    rank_owner = jnp.arange(reduced_every_adapter, dtype=jnp.int32) // ADAPTER_RANK
    adapter_mask = adapter_per_token(segment_row, adapter_row)[:, None] == rank_owner[None, :]
    selected_reduced = jnp.where(adapter_mask, reduced_hidden, jnp.zeros_like(reduced_hidden))
    joined_projection = joined_projection + adapter_scale * jnp.dot(
        selected_reduced,
        joined_up_maps.reshape(reduced_every_adapter, -1),
        preferred_element_type=jnp.float32,
    )
    kv_here = joined_weight.shape[1]
    joined_projection = joined_projection.reshape(col_tokens, kv_here, QUERY_GROUP + 2, HEAD_SIZE)
    positions = positions_of(segment_row)
    queries = rotate_heads(
        joined_projection[:, :, :QUERY_GROUP].reshape(col_tokens, kv_here * QUERY_GROUP, HEAD_SIZE),
        positions,
    )
    queries = queries.astype(jnp.bfloat16).reshape(col_tokens, kv_here, QUERY_GROUP, HEAD_SIZE)
    key_heads = rotate_heads(joined_projection[:, :, QUERY_GROUP], positions).astype(jnp.bfloat16)
    value_heads = joined_projection[:, :, QUERY_GROUP + 1].astype(jnp.bfloat16)
    blended_hidden = attend_heads(queries, key_heads, value_heads, segment_row, sinks)
    share = col_tokens // groups
    quarter = hidden.shape[1]
    rank_total = output_down_maps.shape[1]
    route_pack = jnp.concatenate(
        [routes[0].astype(jnp.bfloat16), expert_gates[0].astype(jnp.bfloat16)], axis=1
    )
    pack_width = -(quarter + rank_total) % 128 or 128
    route_pack = jnp.pad(route_pack, ((0, 0), (0, pack_width - 2 * TOP)))
    pack_rows = lax.dynamic_update_slice_in_dim(
        jnp.zeros((col_tokens, pack_width), jnp.bfloat16), route_pack, position_dp * share, 0
    )
    partial_out = jnp.dot(blended_hidden, attention_out_weight, preferred_element_type=jnp.float32)
    low_local = jnp.dot(blended_hidden, output_down_maps, preferred_element_type=jnp.float32)
    joined_send = jnp.concatenate(
        [
            partial_out.astype(jnp.bfloat16).reshape(col_tokens, groups, quarter),
            jnp.broadcast_to(
                low_local.astype(jnp.bfloat16)[:, None, :], (col_tokens, groups, rank_total)
            ),
            jnp.broadcast_to(pack_rows[:, None, :], (col_tokens, groups, pack_width)),
        ],
        axis=2,
    ).reshape(col_tokens, -1)
    reduced_parts = []

    def reduce_rows(lo, rows):
        joined_back = lax.psum_scatter(
            joined_send[lo : lo + rows], "dp", scatter_dimension=1, tiled=True
        )
        return joined_back

    def resid_rows(joined_back, lo, rows):
        mine_out = joined_back[:, :quarter].astype(jnp.float32)
        output_reduced = joined_back[:, quarter : quarter + rank_total]
        selected_output = jnp.where(
            adapter_mask[lo : lo + rows], output_reduced, jnp.zeros_like(output_reduced)
        )
        adapter_delta = adapter_scale * jnp.dot(
            selected_output, output_up_maps, preferred_element_type=jnp.float32
        )
        resid_part = (
            hidden[lo : lo + rows].astype(jnp.float32) + mine_out + adapter_delta
        ).astype(jnp.bfloat16)
        return resid_part, joined_back[:, quarter + rank_total :]

    lane_pad = -width % 128
    wide = width + lane_pad
    experts = expert_gate_weight.shape[0] * columns
    capacity = 4 * share * TOP // (3 * experts)
    gate_weight = expert_gate_weight[0]
    up_weight = expert_up_weight[0]
    down_weight = jnp.pad(expert_down_weight[0], ((0, 0), (0, lane_pad)))
    halves = 2 if groups % 2 == 0 else 1
    half_tokens = col_tokens // halves
    half_capacity = (groups // halves) * capacity
    counter = jnp.arange(col_tokens, dtype=jnp.int32)
    request_ids = jnp.arange(REQS, dtype=jnp.int32)
    last_index = jnp.max(
        jnp.where(segment_row[None, :] == request_ids[:, None], counter[None, :], -1), axis=1
    )
    last_index = jnp.clip(last_index, 0, col_tokens - 1)
    moe_rows = []
    last_parts = []
    last_resid_parts = []
    held = None
    pending = None
    for h in range(halves):
        lo = h * half_tokens
        joined_h = reduce_rows(lo, half_tokens)
        resid_h, pack_h = resid_rows(joined_h, lo, half_tokens)
        reduced_parts.append(resid_h)
        column_h = lax.all_gather(resid_h, "dp", axis=1, tiled=True)
        if held is not None:
            column_h, held = lax.optimization_barrier((column_h, held))
        moe_in = rms_scale(column_h.astype(jnp.float32), expert_norm_gain).astype(jnp.bfloat16)
        moe_in = jnp.pad(moe_in, ((0, 0), (0, lane_pad)))
        route_flat = pack_h[:, :TOP].astype(jnp.int32).reshape(-1)
        gates_h = pack_h[:, TOP : 2 * TOP]
        one_hot = (route_flat[:, None] == jnp.arange(experts, dtype=jnp.int32)[None, :]).astype(
            jnp.int32
        )
        slot_rows = jnp.sum((jnp.cumsum(one_hot, axis=0) - one_hot) * one_hot, axis=1)
        target = route_flat * half_capacity + slot_rows
        source_rows = jnp.arange(route_flat.shape[0], dtype=jnp.int32) // TOP
        table = (
            jnp.full((experts * half_capacity,), half_tokens, jnp.int32)
            .at[target]
            .set(source_rows)
        )
        dispatch = (table[:, None] == jnp.arange(half_tokens, dtype=jnp.int32)[None, :]).astype(
            jnp.bfloat16
        )
        outgoing = (
            jnp.dot(dispatch, moe_in, preferred_element_type=jnp.float32)
            .astype(jnp.bfloat16)
            .reshape(experts, half_capacity, wide)
        )
        arrived = lax.all_to_all(outgoing, "expert", split_axis=0, concat_axis=0, tiled=True)
        if h == 0:
            held = arrived
        else:
            arrived = lax.optimization_barrier((arrived, held))[0]
        rows_in = arrived.reshape(-1, wide)[:, :width]
        gate_part = jnp.dot(rows_in, gate_weight, preferred_element_type=jnp.float32)
        up_part = jnp.dot(rows_in, up_weight, preferred_element_type=jnp.float32)
        activated = (gate_part * jax.nn.sigmoid(glu_alpha * gate_part) * (up_part + 1.0)).astype(
            jnp.bfloat16
        )
        shares_out = (
            jnp.dot(activated, down_weight, preferred_element_type=jnp.float32)
            .astype(jnp.bfloat16)
            .reshape(experts, half_capacity, wide)
        )
        if pending is not None:
            shares_out, pending = lax.optimization_barrier((shares_out, pending))
            moe_rows.append(lax.psum_scatter(pending, "dp", scatter_dimension=1, tiled=True))
            pending = None
        answers = lax.all_to_all(shares_out, "expert", split_axis=0, concat_axis=0, tiled=True)
        slot_ids = jnp.arange(experts * half_capacity, dtype=jnp.int32)
        combine = jnp.sum(
            jnp.where(
                target.reshape(half_tokens, TOP)[:, :, None] == slot_ids[None, None, :],
                gates_h[:, :, None],
                jnp.zeros((), jnp.bfloat16),
            ),
            axis=1,
        ).astype(jnp.bfloat16)
        mixture = jnp.dot(
            combine,
            answers.reshape(experts * half_capacity, wide),
            preferred_element_type=jnp.float32,
        )[:, :width]
        local_last = jnp.clip(last_index - lo, 0, half_tokens - 1)
        inside = ((last_index >= lo) & (last_index < lo + half_tokens))[:, None]
        last_parts.append(
            jnp.where(inside, jnp.take(mixture, local_last, axis=0), jnp.zeros((), jnp.float32))
        )
        last_resid_parts.append(
            jnp.where(inside, jnp.take(column_h, local_last, axis=0), jnp.zeros((), jnp.bfloat16))
        )
        if h < halves - 1:
            pending = mixture.astype(jnp.bfloat16)
        else:
            last_mix = sum(last_parts).reshape(REQS * groups, quarter)
            moe_send = jnp.concatenate(
                [mixture, jnp.tile(last_mix, (1, groups))], axis=0
            ).astype(jnp.bfloat16)
            moe_rows.append(lax.psum_scatter(moe_send, "dp", scatter_dimension=1, tiled=True))
    moe_back = jnp.concatenate(moe_rows, axis=0)
    moe_rounded = moe_back[:col_tokens].astype(jnp.float32).astype(jnp.bfloat16)
    resid = jnp.concatenate(reduced_parts, axis=0)
    hidden_out = (resid.astype(jnp.float32) + moe_rounded.astype(jnp.float32)).astype(jnp.bfloat16)
    last_moe = moe_back[col_tokens:].reshape(REQS, width)
    last_resid = sum(part.astype(jnp.float32) for part in last_resid_parts)
    last_hidden = (last_resid + last_moe.astype(jnp.float32)).astype(jnp.bfloat16)
    ends = rms_scale(last_hidden.astype(jnp.float32), closing_gain).astype(jnp.bfloat16)
    tail_rows = lax.all_gather(ends, "expert", axis=0, tiled=True)
    logits = jnp.dot(tail_rows, vocabulary_weight, preferred_element_type=jnp.float32)
    return (hidden_out, logits)


def solution(mesh):
    in_specs = (
        P("expert", "dp"),
        P("expert", None),
        P("expert", None),
        P("expert", "dp", None),
        P("expert", "dp", None),
        P(),
        P(None, "dp", None),
        P("dp"),
        P("dp", None),
        P(),
        P(None, "dp", None),
        P("dp", None),
        P(None, "dp"),
        P(),
        P("expert", None, "dp"),
        P("expert", None, "dp"),
        P("expert", "dp", None),
        P(),
        P(None, ("dp", "expert")),
    )
    out_specs = (P("expert", "dp"), P(None, ("dp", "expert")))
    return jax.shard_map(shards, mesh=mesh, in_specs=in_specs, out_specs=out_specs, check_vma=False)
```

```python
import jax
import jax.numpy as jnp
from jax import lax
from jax.sharding import PartitionSpec as P

HEAD_SIZE = 64
QUERY_GROUP = 8
TOP = 4
ADAPTER_RANK = 16
REQS = 4


epsilon = 1e-05
theta_base = 150000.0
adapter_scale = 2.0
glu_alpha = 1.702


def rms_scale(values, gain_row):
    mean_square = jnp.mean(values * values, axis=-1, keepdims=True)
    return values * lax.rsqrt(mean_square + epsilon) * gain_row


def positions_of(segment_row):
    counter = jnp.arange(segment_row.shape[0], dtype=jnp.int32)
    starting = jnp.concatenate(
        [jnp.ones((1,), dtype=jnp.bool_), segment_row[1:] != segment_row[:-1]]
    )
    first_index = lax.cummax(jnp.where(starting, counter, 0), axis=0)
    return counter - first_index


def adapter_per_token(segment_row, adapter_row):
    hits = segment_row[:, None] == jnp.arange(adapter_row.shape[0], dtype=jnp.int32)[None, :]
    return jnp.sum(jnp.where(hits, adapter_row[None, :], 0), axis=1)


def rotate_heads(values, positions):
    head_dim = values.shape[-1]
    half_dim = head_dim // 2
    frequency = theta_base ** (-2.0 * jnp.arange(half_dim, dtype=jnp.float32) / head_dim)
    angles = positions.astype(jnp.float32)[:, None] * frequency[None, :]
    cosine = jnp.cos(angles)[:, None, :]
    sine_part = jnp.sin(angles)[:, None, :]
    first_half = values[..., :half_dim]
    second_half = values[..., half_dim:]
    return jnp.concatenate(
        [
            first_half * cosine - second_half * sine_part,
            second_half * cosine + first_half * sine_part,
        ],
        axis=-1,
    )


def attend_heads(queries, key_heads, value_heads, segment_row, sink_row):
    tokens_now, kv_now, group_now, head_dim = queries.shape
    scores = jnp.einsum(
        "tkgh,skh->kgts", queries, key_heads, preferred_element_type=jnp.float32
    ) * head_dim ** (-0.5)
    counter = jnp.arange(tokens_now, dtype=jnp.int32)
    allowed = (segment_row[:, None] == segment_row[None, :]) & (
        counter[None, :] <= counter[:, None]
    )
    weights = jnp.where(allowed[None, None], jnp.exp(scores), 0.0)
    totals = jnp.sum(weights, axis=-1, keepdims=True) + jnp.exp(sink_row).reshape(
        kv_now, group_now, 1, 1
    )
    probs = (weights / totals).astype(jnp.bfloat16)
    blended_hidden = jnp.einsum(
        "kgts,skh->tkgh", probs, value_heads, preferred_element_type=jnp.float32
    )
    return blended_hidden.astype(jnp.bfloat16).reshape(tokens_now, kv_now * group_now * head_dim)


def shards(
    hidden,
    segments,
    request_adapter,
    routes,
    expert_gates,
    attention_gain,
    joined_weight,
    sinks,
    attention_out_weight,
    joined_down_maps,
    joined_up_maps,
    output_down_maps,
    output_up_maps,
    expert_norm_gain,
    expert_gate_weight,
    expert_up_weight,
    expert_down_weight,
    closing_gain,
    vocabulary_weight,
):
    groups = lax.axis_size("dp")
    columns = lax.axis_size("expert")
    position_dp = lax.axis_index("dp")
    segment_row = segments[0]
    adapter_row = request_adapter[0]
    col_tokens = segment_row.shape[0]
    gathered_rows = lax.all_gather(hidden, "dp", axis=1, tiled=True)
    width = gathered_rows.shape[1]
    normalized_hidden = rms_scale(gathered_rows.astype(jnp.float32), attention_gain).astype(
        jnp.bfloat16
    )
    joined_projection = jnp.dot(
        normalized_hidden, joined_weight.reshape(width, -1), preferred_element_type=jnp.float32
    )
    reduced_every_adapter = joined_down_maps.shape[1]
    reduced_hidden = jnp.dot(
        normalized_hidden, joined_down_maps, preferred_element_type=jnp.float32
    ).astype(jnp.bfloat16)
    rank_owner = jnp.arange(reduced_every_adapter, dtype=jnp.int32) // ADAPTER_RANK
    adapter_mask = adapter_per_token(segment_row, adapter_row)[:, None] == rank_owner[None, :]
    selected_reduced = jnp.where(adapter_mask, reduced_hidden, jnp.zeros_like(reduced_hidden))
    joined_projection = joined_projection + adapter_scale * jnp.dot(
        selected_reduced,
        joined_up_maps.reshape(reduced_every_adapter, -1),
        preferred_element_type=jnp.float32,
    )
    kv_here = joined_weight.shape[1]
    joined_projection = joined_projection.reshape(col_tokens, kv_here, QUERY_GROUP + 2, HEAD_SIZE)
    positions = positions_of(segment_row)
    queries = rotate_heads(
        joined_projection[:, :, :QUERY_GROUP].reshape(col_tokens, kv_here * QUERY_GROUP, HEAD_SIZE),
        positions,
    )
    queries = queries.astype(jnp.bfloat16).reshape(col_tokens, kv_here, QUERY_GROUP, HEAD_SIZE)
    key_heads = rotate_heads(joined_projection[:, :, QUERY_GROUP], positions).astype(jnp.bfloat16)
    value_heads = joined_projection[:, :, QUERY_GROUP + 1].astype(jnp.bfloat16)
    blended_hidden = attend_heads(queries, key_heads, value_heads, segment_row, sinks)
    share = col_tokens // groups
    quarter = hidden.shape[1]
    rank_total = output_down_maps.shape[1]
    route_pack = jnp.concatenate(
        [routes[0].astype(jnp.bfloat16), expert_gates[0].astype(jnp.bfloat16)], axis=1
    )
    pack_width = -(quarter + rank_total) % 128 or 128
    route_pack = jnp.pad(route_pack, ((0, 0), (0, pack_width - 2 * TOP)))
    pack_rows = lax.dynamic_update_slice_in_dim(
        jnp.zeros((col_tokens, pack_width), jnp.bfloat16), route_pack, position_dp * share, 0
    )
    partial_out = jnp.dot(blended_hidden, attention_out_weight, preferred_element_type=jnp.float32)
    low_local = jnp.dot(blended_hidden, output_down_maps, preferred_element_type=jnp.float32)
    joined_send = jnp.concatenate(
        [
            partial_out.astype(jnp.bfloat16).reshape(col_tokens, groups, quarter),
            jnp.broadcast_to(
                low_local.astype(jnp.bfloat16)[:, None, :], (col_tokens, groups, rank_total)
            ),
            jnp.broadcast_to(pack_rows[:, None, :], (col_tokens, groups, pack_width)),
        ],
        axis=2,
    ).reshape(col_tokens, -1)
    reduced_parts = []

    def reduce_rows(lo, rows):
        joined_back = lax.psum_scatter(
            joined_send[lo : lo + rows], "dp", scatter_dimension=1, tiled=True
        )
        return joined_back

    def resid_rows(joined_back, lo, rows):
        mine_out = joined_back[:, :quarter].astype(jnp.float32)
        output_reduced = joined_back[:, quarter : quarter + rank_total]
        selected_output = jnp.where(
            adapter_mask[lo : lo + rows], output_reduced, jnp.zeros_like(output_reduced)
        )
        adapter_delta = adapter_scale * jnp.dot(
            selected_output, output_up_maps, preferred_element_type=jnp.float32
        )
        resid_part = (
            hidden[lo : lo + rows].astype(jnp.float32) + mine_out + adapter_delta
        ).astype(jnp.bfloat16)
        return resid_part, joined_back[:, quarter + rank_total :]

    lane_pad = -width % 128
    wide = width + lane_pad
    experts = expert_gate_weight.shape[0] * columns
    capacity = 4 * share * TOP // (3 * experts)
    gate_weight = expert_gate_weight[0]
    up_weight = expert_up_weight[0]
    down_weight = jnp.pad(expert_down_weight[0], ((0, 0), (0, lane_pad)))
    halves = groups
    half_tokens = col_tokens // halves
    half_capacity = (groups // halves) * capacity
    counter = jnp.arange(col_tokens, dtype=jnp.int32)
    request_ids = jnp.arange(REQS, dtype=jnp.int32)
    last_index = jnp.max(
        jnp.where(segment_row[None, :] == request_ids[:, None], counter[None, :], -1), axis=1
    )
    last_index = jnp.clip(last_index, 0, col_tokens - 1)
    moe_rows = []
    last_parts = []
    last_resid_parts = []
    held = None
    pending = None
    for h in range(halves):
        lo = h * half_tokens
        joined_h = reduce_rows(lo, half_tokens)
        resid_h, pack_h = resid_rows(joined_h, lo, half_tokens)
        reduced_parts.append(resid_h)
        column_h = lax.all_gather(resid_h, "dp", axis=1, tiled=True)
        if held is not None:
            column_h, held = lax.optimization_barrier((column_h, held))
        moe_in = rms_scale(column_h.astype(jnp.float32), expert_norm_gain).astype(jnp.bfloat16)
        moe_in = jnp.pad(moe_in, ((0, 0), (0, lane_pad)))
        route_flat = pack_h[:, :TOP].astype(jnp.int32).reshape(-1)
        gates_h = pack_h[:, TOP : 2 * TOP]
        one_hot = (route_flat[:, None] == jnp.arange(experts, dtype=jnp.int32)[None, :]).astype(
            jnp.int32
        )
        slot_rows = jnp.sum((jnp.cumsum(one_hot, axis=0) - one_hot) * one_hot, axis=1)
        target = route_flat * half_capacity + slot_rows
        source_rows = jnp.arange(route_flat.shape[0], dtype=jnp.int32) // TOP
        table = (
            jnp.full((experts * half_capacity,), half_tokens, jnp.int32)
            .at[target]
            .set(source_rows)
        )
        dispatch = (table[:, None] == jnp.arange(half_tokens, dtype=jnp.int32)[None, :]).astype(
            jnp.bfloat16
        )
        outgoing = (
            jnp.dot(dispatch, moe_in, preferred_element_type=jnp.float32)
            .astype(jnp.bfloat16)
            .reshape(experts, half_capacity, wide)
        )
        arrived = lax.all_to_all(outgoing, "expert", split_axis=0, concat_axis=0, tiled=True)
        held = arrived
        rows_in = arrived.reshape(-1, wide)[:, :width]
        gate_part = jnp.dot(rows_in, gate_weight, preferred_element_type=jnp.float32)
        up_part = jnp.dot(rows_in, up_weight, preferred_element_type=jnp.float32)
        activated = (gate_part * jax.nn.sigmoid(glu_alpha * gate_part) * (up_part + 1.0)).astype(
            jnp.bfloat16
        )
        shares_out = (
            jnp.dot(activated, down_weight, preferred_element_type=jnp.float32)
            .astype(jnp.bfloat16)
            .reshape(experts, half_capacity, wide)
        )
        if pending is not None:
            shares_out, pending = lax.optimization_barrier((shares_out, pending))
            moe_rows.append(lax.psum_scatter(pending, "dp", scatter_dimension=1, tiled=True))
            pending = None
        answers = lax.all_to_all(shares_out, "expert", split_axis=0, concat_axis=0, tiled=True)
        slot_ids = jnp.arange(experts * half_capacity, dtype=jnp.int32)
        combine = jnp.sum(
            jnp.where(
                target.reshape(half_tokens, TOP)[:, :, None] == slot_ids[None, None, :],
                gates_h[:, :, None],
                jnp.zeros((), jnp.bfloat16),
            ),
            axis=1,
        ).astype(jnp.bfloat16)
        mixture = jnp.dot(
            combine,
            answers.reshape(experts * half_capacity, wide),
            preferred_element_type=jnp.float32,
        )[:, :width]
        local_last = jnp.clip(last_index - lo, 0, half_tokens - 1)
        inside = ((last_index >= lo) & (last_index < lo + half_tokens))[:, None]
        last_parts.append(
            jnp.where(inside, jnp.take(mixture, local_last, axis=0), jnp.zeros((), jnp.float32))
        )
        last_resid_parts.append(
            jnp.where(inside, jnp.take(column_h, local_last, axis=0), jnp.zeros((), jnp.bfloat16))
        )
        if h < halves - 1:
            pending = mixture.astype(jnp.bfloat16)
        else:
            last_mix = sum(last_parts).reshape(REQS * groups, quarter)
            moe_send = jnp.concatenate(
                [mixture, jnp.tile(last_mix, (1, groups))], axis=0
            ).astype(jnp.bfloat16)
            moe_rows.append(lax.psum_scatter(moe_send, "dp", scatter_dimension=1, tiled=True))
    moe_back = jnp.concatenate(moe_rows, axis=0)
    moe_rounded = moe_back[:col_tokens].astype(jnp.float32).astype(jnp.bfloat16)
    resid = jnp.concatenate(reduced_parts, axis=0)
    hidden_out = (resid.astype(jnp.float32) + moe_rounded.astype(jnp.float32)).astype(jnp.bfloat16)
    last_moe = moe_back[col_tokens:].reshape(REQS, width)
    last_resid = sum(part.astype(jnp.float32) for part in last_resid_parts)
    last_hidden = (last_resid + last_moe.astype(jnp.float32)).astype(jnp.bfloat16)
    ends = rms_scale(last_hidden.astype(jnp.float32), closing_gain).astype(jnp.bfloat16)
    tail_rows = lax.all_gather(ends, "expert", axis=0, tiled=True)
    logits = jnp.dot(tail_rows, vocabulary_weight, preferred_element_type=jnp.float32)
    return (hidden_out, logits)


def solution(mesh):
    in_specs = (
        P("expert", "dp"),
        P("expert", None),
        P("expert", None),
        P("expert", "dp", None),
        P("expert", "dp", None),
        P(),
        P(None, "dp", None),
        P("dp"),
        P("dp", None),
        P(),
        P(None, "dp", None),
        P("dp", None),
        P(None, "dp"),
        P(),
        P("expert", None, "dp"),
        P("expert", None, "dp"),
        P("expert", "dp", None),
        P(),
        P(None, ("dp", "expert")),
    )
    out_specs = (P("expert", "dp"), P(None, ("dp", "expert")))
    return jax.shard_map(shards, mesh=mesh, in_specs=in_specs, out_specs=out_specs, check_vma=False)
```

```python
import jax
import jax.numpy as jnp
from jax import lax
from jax.sharding import PartitionSpec as P

HEAD_SIZE = 64
QUERY_GROUP = 8
TOP = 4
ADAPTER_RANK = 16
REQS = 4


epsilon = 1e-05
theta_base = 150000.0
adapter_scale = 2.0
glu_alpha = 1.702


def rms_scale(values, gain_row):
    mean_square = jnp.mean(values * values, axis=-1, keepdims=True)
    return values * lax.rsqrt(mean_square + epsilon) * gain_row


def positions_of(segment_row):
    counter = jnp.arange(segment_row.shape[0], dtype=jnp.int32)
    starting = jnp.concatenate(
        [jnp.ones((1,), dtype=jnp.bool_), segment_row[1:] != segment_row[:-1]]
    )
    first_index = lax.cummax(jnp.where(starting, counter, 0), axis=0)
    return counter - first_index


def adapter_per_token(segment_row, adapter_row):
    hits = segment_row[:, None] == jnp.arange(adapter_row.shape[0], dtype=jnp.int32)[None, :]
    return jnp.sum(jnp.where(hits, adapter_row[None, :], 0), axis=1)


def rotate_heads(values, positions):
    head_dim = values.shape[-1]
    half_dim = head_dim // 2
    frequency = theta_base ** (-2.0 * jnp.arange(half_dim, dtype=jnp.float32) / head_dim)
    angles = positions.astype(jnp.float32)[:, None] * frequency[None, :]
    cosine = jnp.cos(angles)[:, None, :]
    sine_part = jnp.sin(angles)[:, None, :]
    first_half = values[..., :half_dim]
    second_half = values[..., half_dim:]
    return jnp.concatenate(
        [
            first_half * cosine - second_half * sine_part,
            second_half * cosine + first_half * sine_part,
        ],
        axis=-1,
    )


def attend_heads(queries, key_heads, value_heads, segment_row, sink_row, offset):
    tokens_now, kv_now, group_now, head_dim = queries.shape
    keys_now = key_heads.shape[0]
    scores = jnp.einsum(
        "tkgh,skh->kgts", queries, key_heads, preferred_element_type=jnp.float32
    ) * head_dim ** (-0.5)
    query_index = offset + jnp.arange(tokens_now, dtype=jnp.int32)
    key_index = jnp.arange(keys_now, dtype=jnp.int32)
    allowed = (segment_row[offset : offset + tokens_now, None] == segment_row[None, :keys_now]) & (
        key_index[None, :] <= query_index[:, None]
    )
    weights = jnp.where(allowed[None, None], jnp.exp(scores), 0.0)
    totals = jnp.sum(weights, axis=-1, keepdims=True) + jnp.exp(sink_row).reshape(
        kv_now, group_now, 1, 1
    )
    probs = (weights / totals).astype(jnp.bfloat16)
    blended_hidden = jnp.einsum(
        "kgts,skh->tkgh", probs, value_heads, preferred_element_type=jnp.float32
    )
    return blended_hidden.astype(jnp.bfloat16).reshape(tokens_now, kv_now * group_now * head_dim)


def shards(
    hidden,
    segments,
    request_adapter,
    routes,
    expert_gates,
    attention_gain,
    joined_weight,
    sinks,
    attention_out_weight,
    joined_down_maps,
    joined_up_maps,
    output_down_maps,
    output_up_maps,
    expert_norm_gain,
    expert_gate_weight,
    expert_up_weight,
    expert_down_weight,
    closing_gain,
    vocabulary_weight,
):
    groups = lax.axis_size("dp")
    columns = lax.axis_size("expert")
    position_dp = lax.axis_index("dp")
    segment_row = segments[0]
    adapter_row = request_adapter[0]
    col_tokens = segment_row.shape[0]
    gathered_rows = lax.all_gather(hidden, "dp", axis=1, tiled=True)
    width = gathered_rows.shape[1]
    normalized_hidden = rms_scale(gathered_rows.astype(jnp.float32), attention_gain).astype(
        jnp.bfloat16
    )
    joined_projection = jnp.dot(
        normalized_hidden, joined_weight.reshape(width, -1), preferred_element_type=jnp.float32
    )
    reduced_every_adapter = joined_down_maps.shape[1]
    reduced_hidden = jnp.dot(
        normalized_hidden, joined_down_maps, preferred_element_type=jnp.float32
    ).astype(jnp.bfloat16)
    rank_owner = jnp.arange(reduced_every_adapter, dtype=jnp.int32) // ADAPTER_RANK
    adapter_mask = adapter_per_token(segment_row, adapter_row)[:, None] == rank_owner[None, :]
    selected_reduced = jnp.where(adapter_mask, reduced_hidden, jnp.zeros_like(reduced_hidden))
    joined_projection = joined_projection + adapter_scale * jnp.dot(
        selected_reduced,
        joined_up_maps.reshape(reduced_every_adapter, -1),
        preferred_element_type=jnp.float32,
    )
    kv_here = joined_weight.shape[1]
    joined_projection = joined_projection.reshape(col_tokens, kv_here, QUERY_GROUP + 2, HEAD_SIZE)
    positions = positions_of(segment_row)
    queries = rotate_heads(
        joined_projection[:, :, :QUERY_GROUP].reshape(col_tokens, kv_here * QUERY_GROUP, HEAD_SIZE),
        positions,
    )
    queries = queries.astype(jnp.bfloat16).reshape(col_tokens, kv_here, QUERY_GROUP, HEAD_SIZE)
    key_heads = rotate_heads(joined_projection[:, :, QUERY_GROUP], positions).astype(jnp.bfloat16)
    value_heads = joined_projection[:, :, QUERY_GROUP + 1].astype(jnp.bfloat16)
    share = col_tokens // groups
    quarter = hidden.shape[1]
    rank_total = output_down_maps.shape[1]
    route_pack = jnp.concatenate(
        [routes[0].astype(jnp.bfloat16), expert_gates[0].astype(jnp.bfloat16)], axis=1
    )
    pack_width = -(quarter + rank_total) % 128 or 128
    route_pack = jnp.pad(route_pack, ((0, 0), (0, pack_width - 2 * TOP)))
    pack_rows = lax.dynamic_update_slice_in_dim(
        jnp.zeros((col_tokens, pack_width), jnp.bfloat16), route_pack, position_dp * share, 0
    )
    halves = 2 if groups % 2 == 0 else 1
    half_tokens = col_tokens // halves
    joined_parts = []
    for h in range(halves):
        lo = h * half_tokens
        hi = lo + half_tokens
        blended_hidden = attend_heads(
            queries[lo:hi], key_heads[:hi], value_heads[:hi], segment_row, sinks, lo
        )
        partial_out = jnp.dot(
            blended_hidden, attention_out_weight, preferred_element_type=jnp.float32
        )
        low_local = jnp.dot(blended_hidden, output_down_maps, preferred_element_type=jnp.float32)
        joined_parts.append(
            jnp.concatenate(
                [
                    partial_out.astype(jnp.bfloat16).reshape(half_tokens, groups, quarter),
                    jnp.broadcast_to(
                        low_local.astype(jnp.bfloat16)[:, None, :],
                        (half_tokens, groups, rank_total),
                    ),
                    jnp.broadcast_to(
                        pack_rows[lo:hi, None, :], (half_tokens, groups, pack_width)
                    ),
                ],
                axis=2,
            ).reshape(half_tokens, -1)
        )
    reduced_parts = []

    def reduce_rows(lo, rows):
        joined_back = lax.psum_scatter(
            joined_parts[lo // rows], "dp", scatter_dimension=1, tiled=True
        )
        return joined_back

    def resid_rows(joined_back, lo, rows):
        mine_out = joined_back[:, :quarter].astype(jnp.float32)
        output_reduced = joined_back[:, quarter : quarter + rank_total]
        selected_output = jnp.where(
            adapter_mask[lo : lo + rows], output_reduced, jnp.zeros_like(output_reduced)
        )
        adapter_delta = adapter_scale * jnp.dot(
            selected_output, output_up_maps, preferred_element_type=jnp.float32
        )
        resid_part = (
            hidden[lo : lo + rows].astype(jnp.float32) + mine_out + adapter_delta
        ).astype(jnp.bfloat16)
        return resid_part, joined_back[:, quarter + rank_total :]

    lane_pad = -width % 128
    wide = width + lane_pad
    experts = expert_gate_weight.shape[0] * columns
    capacity = 4 * share * TOP // (3 * experts)
    gate_weight = expert_gate_weight[0]
    up_weight = expert_up_weight[0]
    down_weight = jnp.pad(expert_down_weight[0], ((0, 0), (0, lane_pad)))
    half_capacity = (groups // halves) * capacity
    counter = jnp.arange(col_tokens, dtype=jnp.int32)
    request_ids = jnp.arange(REQS, dtype=jnp.int32)
    last_index = jnp.max(
        jnp.where(segment_row[None, :] == request_ids[:, None], counter[None, :], -1), axis=1
    )
    last_index = jnp.clip(last_index, 0, col_tokens - 1)
    moe_rows = []
    last_parts = []
    last_resid_parts = []
    held = None
    pending = None
    for h in range(halves):
        lo = h * half_tokens
        joined_h = reduce_rows(lo, half_tokens)
        resid_h, pack_h = resid_rows(joined_h, lo, half_tokens)
        reduced_parts.append(resid_h)
        column_h = lax.all_gather(resid_h, "dp", axis=1, tiled=True)
        if held is not None:
            column_h, held = lax.optimization_barrier((column_h, held))
        moe_in = rms_scale(column_h.astype(jnp.float32), expert_norm_gain).astype(jnp.bfloat16)
        moe_in = jnp.pad(moe_in, ((0, 0), (0, lane_pad)))
        route_flat = pack_h[:, :TOP].astype(jnp.int32).reshape(-1)
        gates_h = pack_h[:, TOP : 2 * TOP]
        one_hot = (route_flat[:, None] == jnp.arange(experts, dtype=jnp.int32)[None, :]).astype(
            jnp.int32
        )
        slot_rows = jnp.sum((jnp.cumsum(one_hot, axis=0) - one_hot) * one_hot, axis=1)
        target = route_flat * half_capacity + slot_rows
        source_rows = jnp.arange(route_flat.shape[0], dtype=jnp.int32) // TOP
        table = (
            jnp.full((experts * half_capacity,), half_tokens, jnp.int32)
            .at[target]
            .set(source_rows)
        )
        dispatch = (table[:, None] == jnp.arange(half_tokens, dtype=jnp.int32)[None, :]).astype(
            jnp.bfloat16
        )
        outgoing = (
            jnp.dot(dispatch, moe_in, preferred_element_type=jnp.float32)
            .astype(jnp.bfloat16)
            .reshape(experts, half_capacity, wide)
        )
        arrived = lax.all_to_all(outgoing, "expert", split_axis=0, concat_axis=0, tiled=True)
        if h == 0:
            held = arrived
        else:
            arrived = lax.optimization_barrier((arrived, held))[0]
        rows_in = arrived.reshape(-1, wide)[:, :width]
        gate_part = jnp.dot(rows_in, gate_weight, preferred_element_type=jnp.float32)
        up_part = jnp.dot(rows_in, up_weight, preferred_element_type=jnp.float32)
        activated = (gate_part * jax.nn.sigmoid(glu_alpha * gate_part) * (up_part + 1.0)).astype(
            jnp.bfloat16
        )
        shares_out = (
            jnp.dot(activated, down_weight, preferred_element_type=jnp.float32)
            .astype(jnp.bfloat16)
            .reshape(experts, half_capacity, wide)
        )
        if pending is not None:
            shares_out, pending = lax.optimization_barrier((shares_out, pending))
            moe_rows.append(lax.psum_scatter(pending, "dp", scatter_dimension=1, tiled=True))
            pending = None
        answers = lax.all_to_all(shares_out, "expert", split_axis=0, concat_axis=0, tiled=True)
        slot_ids = jnp.arange(experts * half_capacity, dtype=jnp.int32)
        combine = jnp.sum(
            jnp.where(
                target.reshape(half_tokens, TOP)[:, :, None] == slot_ids[None, None, :],
                gates_h[:, :, None],
                jnp.zeros((), jnp.bfloat16),
            ),
            axis=1,
        ).astype(jnp.bfloat16)
        mixture = jnp.dot(
            combine,
            answers.reshape(experts * half_capacity, wide),
            preferred_element_type=jnp.float32,
        )[:, :width]
        local_last = jnp.clip(last_index - lo, 0, half_tokens - 1)
        inside = ((last_index >= lo) & (last_index < lo + half_tokens))[:, None]
        last_parts.append(
            jnp.where(inside, jnp.take(mixture, local_last, axis=0), jnp.zeros((), jnp.float32))
        )
        last_resid_parts.append(
            jnp.where(inside, jnp.take(column_h, local_last, axis=0), jnp.zeros((), jnp.bfloat16))
        )
        if h < halves - 1:
            pending = mixture.astype(jnp.bfloat16)
        else:
            last_mix = sum(last_parts).reshape(REQS * groups, quarter)
            moe_send = jnp.concatenate(
                [mixture, jnp.tile(last_mix, (1, groups))], axis=0
            ).astype(jnp.bfloat16)
            moe_rows.append(lax.psum_scatter(moe_send, "dp", scatter_dimension=1, tiled=True))
    moe_back = jnp.concatenate(moe_rows, axis=0)
    moe_rounded = moe_back[:col_tokens].astype(jnp.float32).astype(jnp.bfloat16)
    resid = jnp.concatenate(reduced_parts, axis=0)
    hidden_out = (resid.astype(jnp.float32) + moe_rounded.astype(jnp.float32)).astype(jnp.bfloat16)
    last_moe = moe_back[col_tokens:].reshape(REQS, width)
    last_resid = sum(part.astype(jnp.float32) for part in last_resid_parts)
    last_hidden = (last_resid + last_moe.astype(jnp.float32)).astype(jnp.bfloat16)
    ends = rms_scale(last_hidden.astype(jnp.float32), closing_gain).astype(jnp.bfloat16)
    tail_rows = lax.all_gather(ends, "expert", axis=0, tiled=True)
    logits = jnp.dot(tail_rows, vocabulary_weight, preferred_element_type=jnp.float32)
    return (hidden_out, logits)


def solution(mesh):
    in_specs = (
        P("expert", "dp"),
        P("expert", None),
        P("expert", None),
        P("expert", "dp", None),
        P("expert", "dp", None),
        P(),
        P(None, "dp", None),
        P("dp"),
        P("dp", None),
        P(),
        P(None, "dp", None),
        P("dp", None),
        P(None, "dp"),
        P(),
        P("expert", None, "dp"),
        P("expert", None, "dp"),
        P("expert", "dp", None),
        P(),
        P(None, ("dp", "expert")),
    )
    out_specs = (P("expert", "dp"), P(None, ("dp", "expert")))
    return jax.shard_map(shards, mesh=mesh, in_specs=in_specs, out_specs=out_specs, check_vma=False)
```

```python
import jax
import jax.numpy as jnp
from jax import lax
from jax.sharding import PartitionSpec as P

HEAD_SIZE = 64
QUERY_GROUP = 8
TOP = 4
ADAPTER_RANK = 16
REQS = 4


epsilon = 1e-05
theta_base = 150000.0
adapter_scale = 2.0
glu_alpha = 1.702


def rms_scale(values, gain_row):
    mean_square = jnp.mean(values * values, axis=-1, keepdims=True)
    return values * lax.rsqrt(mean_square + epsilon) * gain_row


def positions_of(segment_row):
    counter = jnp.arange(segment_row.shape[0], dtype=jnp.int32)
    starting = jnp.concatenate(
        [jnp.ones((1,), dtype=jnp.bool_), segment_row[1:] != segment_row[:-1]]
    )
    first_index = lax.cummax(jnp.where(starting, counter, 0), axis=0)
    return counter - first_index


def adapter_per_token(segment_row, adapter_row):
    hits = segment_row[:, None] == jnp.arange(adapter_row.shape[0], dtype=jnp.int32)[None, :]
    return jnp.sum(jnp.where(hits, adapter_row[None, :], 0), axis=1)


def rotate_heads(values, positions):
    head_dim = values.shape[-1]
    half_dim = head_dim // 2
    frequency = theta_base ** (-2.0 * jnp.arange(half_dim, dtype=jnp.float32) / head_dim)
    angles = positions.astype(jnp.float32)[:, None] * frequency[None, :]
    cosine = jnp.cos(angles)[:, None, :]
    sine_part = jnp.sin(angles)[:, None, :]
    first_half = values[..., :half_dim]
    second_half = values[..., half_dim:]
    return jnp.concatenate(
        [
            first_half * cosine - second_half * sine_part,
            second_half * cosine + first_half * sine_part,
        ],
        axis=-1,
    )


def attend_heads(queries, key_heads, value_heads, segment_row, sink_row):
    tokens_now, kv_now, group_now, head_dim = queries.shape
    scores = jnp.einsum(
        "tkgh,skh->kgts", queries, key_heads, preferred_element_type=jnp.float32
    ) * head_dim ** (-0.5)
    counter = jnp.arange(tokens_now, dtype=jnp.int32)
    allowed = (segment_row[:, None] == segment_row[None, :]) & (
        counter[None, :] <= counter[:, None]
    )
    weights = jnp.where(allowed[None, None], jnp.exp(scores), 0.0)
    totals = jnp.sum(weights, axis=-1, keepdims=True) + jnp.exp(sink_row).reshape(
        kv_now, group_now, 1, 1
    )
    probs = (weights / totals).astype(jnp.bfloat16)
    blended_hidden = jnp.einsum(
        "kgts,skh->tkgh", probs, value_heads, preferred_element_type=jnp.float32
    )
    return blended_hidden.astype(jnp.bfloat16).reshape(tokens_now, kv_now * group_now * head_dim)


def shards(
    hidden,
    segments,
    request_adapter,
    routes,
    expert_gates,
    attention_gain,
    joined_weight,
    sinks,
    attention_out_weight,
    joined_down_maps,
    joined_up_maps,
    output_down_maps,
    output_up_maps,
    expert_norm_gain,
    expert_gate_weight,
    expert_up_weight,
    expert_down_weight,
    closing_gain,
    vocabulary_weight,
):
    groups = lax.axis_size("dp")
    columns = lax.axis_size("expert")
    position_dp = lax.axis_index("dp")
    segment_row = segments[0]
    adapter_row = request_adapter[0]
    col_tokens = segment_row.shape[0]
    gathered_rows = lax.all_gather(hidden, "dp", axis=1, tiled=True)
    width = gathered_rows.shape[1]
    normalized_hidden = rms_scale(gathered_rows.astype(jnp.float32), attention_gain).astype(
        jnp.bfloat16
    )
    joined_projection = jnp.dot(
        normalized_hidden, joined_weight.reshape(width, -1), preferred_element_type=jnp.float32
    )
    reduced_every_adapter = joined_down_maps.shape[1]
    reduced_hidden = jnp.dot(
        normalized_hidden, joined_down_maps, preferred_element_type=jnp.float32
    ).astype(jnp.bfloat16)
    rank_owner = jnp.arange(reduced_every_adapter, dtype=jnp.int32) // ADAPTER_RANK
    adapter_mask = adapter_per_token(segment_row, adapter_row)[:, None] == rank_owner[None, :]
    selected_reduced = jnp.where(adapter_mask, reduced_hidden, jnp.zeros_like(reduced_hidden))
    joined_projection = joined_projection + adapter_scale * jnp.dot(
        selected_reduced,
        joined_up_maps.reshape(reduced_every_adapter, -1),
        preferred_element_type=jnp.float32,
    )
    kv_here = joined_weight.shape[1]
    joined_projection = joined_projection.reshape(col_tokens, kv_here, QUERY_GROUP + 2, HEAD_SIZE)
    positions = positions_of(segment_row)
    queries = rotate_heads(
        joined_projection[:, :, :QUERY_GROUP].reshape(col_tokens, kv_here * QUERY_GROUP, HEAD_SIZE),
        positions,
    )
    queries = queries.astype(jnp.bfloat16).reshape(col_tokens, kv_here, QUERY_GROUP, HEAD_SIZE)
    key_heads = rotate_heads(joined_projection[:, :, QUERY_GROUP], positions).astype(jnp.bfloat16)
    value_heads = joined_projection[:, :, QUERY_GROUP + 1].astype(jnp.bfloat16)
    blended_hidden = attend_heads(queries, key_heads, value_heads, segment_row, sinks)
    share = col_tokens // groups
    quarter = hidden.shape[1]
    rank_total = output_down_maps.shape[1]
    route_pack = jnp.concatenate(
        [routes[0].astype(jnp.bfloat16), expert_gates[0].astype(jnp.bfloat16)], axis=1
    )
    pack_width = -(quarter + rank_total) % 128 or 128
    route_pack = jnp.pad(route_pack, ((0, 0), (0, pack_width - 2 * TOP)))
    pack_rows = lax.dynamic_update_slice_in_dim(
        jnp.zeros((col_tokens, pack_width), jnp.bfloat16), route_pack, position_dp * share, 0
    )
    partial_out = jnp.dot(blended_hidden, attention_out_weight, preferred_element_type=jnp.float32)
    low_local = jnp.dot(blended_hidden, output_down_maps, preferred_element_type=jnp.float32)
    joined_send = jnp.concatenate(
        [
            partial_out.astype(jnp.bfloat16).reshape(col_tokens, groups, quarter),
            jnp.broadcast_to(
                low_local.astype(jnp.bfloat16)[:, None, :], (col_tokens, groups, rank_total)
            ),
            jnp.broadcast_to(pack_rows[:, None, :], (col_tokens, groups, pack_width)),
        ],
        axis=2,
    ).reshape(col_tokens, -1)
    reduced_parts = []

    def reduce_rows(lo, rows):
        pieces = joined_send[lo : lo + rows].reshape(rows, groups, -1).transpose(1, 0, 2)
        swapped = lax.all_to_all(pieces, "dp", split_axis=0, concat_axis=0, tiled=True)
        return jnp.sum(swapped.astype(jnp.float32), axis=0).astype(jnp.bfloat16)

    def resid_rows(joined_back, lo, rows):
        mine_out = joined_back[:, :quarter].astype(jnp.float32)
        output_reduced = joined_back[:, quarter : quarter + rank_total]
        selected_output = jnp.where(
            adapter_mask[lo : lo + rows], output_reduced, jnp.zeros_like(output_reduced)
        )
        adapter_delta = adapter_scale * jnp.dot(
            selected_output, output_up_maps, preferred_element_type=jnp.float32
        )
        resid_part = (
            hidden[lo : lo + rows].astype(jnp.float32) + mine_out + adapter_delta
        ).astype(jnp.bfloat16)
        return resid_part, joined_back[:, quarter + rank_total :]

    lane_pad = -width % 128
    wide = width + lane_pad
    experts = expert_gate_weight.shape[0] * columns
    capacity = 4 * share * TOP // (3 * experts)
    gate_weight = expert_gate_weight[0]
    up_weight = expert_up_weight[0]
    down_weight = jnp.pad(expert_down_weight[0], ((0, 0), (0, lane_pad)))
    halves = 2 if groups % 2 == 0 else 1
    half_tokens = col_tokens // halves
    half_capacity = (groups // halves) * capacity
    counter = jnp.arange(col_tokens, dtype=jnp.int32)
    request_ids = jnp.arange(REQS, dtype=jnp.int32)
    last_index = jnp.max(
        jnp.where(segment_row[None, :] == request_ids[:, None], counter[None, :], -1), axis=1
    )
    last_index = jnp.clip(last_index, 0, col_tokens - 1)
    moe_rows = []
    last_parts = []
    last_resid_parts = []
    held = None
    pending = None
    for h in range(halves):
        lo = h * half_tokens
        joined_h = reduce_rows(lo, half_tokens)
        resid_h, pack_h = resid_rows(joined_h, lo, half_tokens)
        reduced_parts.append(resid_h)
        column_h = lax.all_gather(resid_h, "dp", axis=1, tiled=True)
        if held is not None:
            column_h, held = lax.optimization_barrier((column_h, held))
        moe_in = rms_scale(column_h.astype(jnp.float32), expert_norm_gain).astype(jnp.bfloat16)
        moe_in = jnp.pad(moe_in, ((0, 0), (0, lane_pad)))
        route_flat = pack_h[:, :TOP].astype(jnp.int32).reshape(-1)
        gates_h = pack_h[:, TOP : 2 * TOP]
        one_hot = (route_flat[:, None] == jnp.arange(experts, dtype=jnp.int32)[None, :]).astype(
            jnp.int32
        )
        slot_rows = jnp.sum((jnp.cumsum(one_hot, axis=0) - one_hot) * one_hot, axis=1)
        target = route_flat * half_capacity + slot_rows
        source_rows = jnp.arange(route_flat.shape[0], dtype=jnp.int32) // TOP
        table = (
            jnp.full((experts * half_capacity,), half_tokens, jnp.int32)
            .at[target]
            .set(source_rows)
        )
        dispatch = (table[:, None] == jnp.arange(half_tokens, dtype=jnp.int32)[None, :]).astype(
            jnp.bfloat16
        )
        outgoing = (
            jnp.dot(dispatch, moe_in, preferred_element_type=jnp.float32)
            .astype(jnp.bfloat16)
            .reshape(experts, half_capacity, wide)
        )
        arrived = lax.all_to_all(outgoing, "expert", split_axis=0, concat_axis=0, tiled=True)
        if h == 0:
            held = arrived
        else:
            arrived = lax.optimization_barrier((arrived, held))[0]
        rows_in = arrived.reshape(-1, wide)[:, :width]
        gate_part = jnp.dot(rows_in, gate_weight, preferred_element_type=jnp.float32)
        up_part = jnp.dot(rows_in, up_weight, preferred_element_type=jnp.float32)
        activated = (gate_part * jax.nn.sigmoid(glu_alpha * gate_part) * (up_part + 1.0)).astype(
            jnp.bfloat16
        )
        shares_out = (
            jnp.dot(activated, down_weight, preferred_element_type=jnp.float32)
            .astype(jnp.bfloat16)
            .reshape(experts, half_capacity, wide)
        )
        if pending is not None:
            shares_out, pending = lax.optimization_barrier((shares_out, pending))
            moe_rows.append(lax.psum_scatter(pending, "dp", scatter_dimension=1, tiled=True))
            pending = None
        answers = lax.all_to_all(shares_out, "expert", split_axis=0, concat_axis=0, tiled=True)
        slot_ids = jnp.arange(experts * half_capacity, dtype=jnp.int32)
        combine = jnp.sum(
            jnp.where(
                target.reshape(half_tokens, TOP)[:, :, None] == slot_ids[None, None, :],
                gates_h[:, :, None],
                jnp.zeros((), jnp.bfloat16),
            ),
            axis=1,
        ).astype(jnp.bfloat16)
        mixture = jnp.dot(
            combine,
            answers.reshape(experts * half_capacity, wide),
            preferred_element_type=jnp.float32,
        )[:, :width]
        local_last = jnp.clip(last_index - lo, 0, half_tokens - 1)
        inside = ((last_index >= lo) & (last_index < lo + half_tokens))[:, None]
        last_parts.append(
            jnp.where(inside, jnp.take(mixture, local_last, axis=0), jnp.zeros((), jnp.float32))
        )
        last_resid_parts.append(
            jnp.where(inside, jnp.take(column_h, local_last, axis=0), jnp.zeros((), jnp.bfloat16))
        )
        if h < halves - 1:
            pending = mixture.astype(jnp.bfloat16)
        else:
            last_mix = sum(last_parts).reshape(REQS * groups, quarter)
            moe_send = jnp.concatenate(
                [mixture, jnp.tile(last_mix, (1, groups))], axis=0
            ).astype(jnp.bfloat16)
            moe_rows.append(lax.psum_scatter(moe_send, "dp", scatter_dimension=1, tiled=True))
    moe_back = jnp.concatenate(moe_rows, axis=0)
    moe_rounded = moe_back[:col_tokens].astype(jnp.float32).astype(jnp.bfloat16)
    resid = jnp.concatenate(reduced_parts, axis=0)
    hidden_out = (resid.astype(jnp.float32) + moe_rounded.astype(jnp.float32)).astype(jnp.bfloat16)
    last_moe = moe_back[col_tokens:].reshape(REQS, width)
    last_resid = sum(part.astype(jnp.float32) for part in last_resid_parts)
    last_hidden = (last_resid + last_moe.astype(jnp.float32)).astype(jnp.bfloat16)
    ends = rms_scale(last_hidden.astype(jnp.float32), closing_gain).astype(jnp.bfloat16)
    tail_rows = lax.all_gather(ends, "expert", axis=0, tiled=True)
    logits = jnp.dot(tail_rows, vocabulary_weight, preferred_element_type=jnp.float32)
    return (hidden_out, logits)


def solution(mesh):
    in_specs = (
        P("expert", "dp"),
        P("expert", None),
        P("expert", None),
        P("expert", "dp", None),
        P("expert", "dp", None),
        P(),
        P(None, "dp", None),
        P("dp"),
        P("dp", None),
        P(),
        P(None, "dp", None),
        P("dp", None),
        P(None, "dp"),
        P(),
        P("expert", None, "dp"),
        P("expert", None, "dp"),
        P("expert", "dp", None),
        P(),
        P(None, ("dp", "expert")),
    )
    out_specs = (P("expert", "dp"), P(None, ("dp", "expert")))
    return jax.shard_map(shards, mesh=mesh, in_specs=in_specs, out_specs=out_specs, check_vma=False)
```

```python
import jax
import jax.numpy as jnp
from jax import lax
from jax.sharding import PartitionSpec as P

HEAD_SIZE = 64
QUERY_GROUP = 8
TOP = 4
ADAPTER_RANK = 16
REQS = 4


epsilon = 1e-05
theta_base = 150000.0
adapter_scale = 2.0
glu_alpha = 1.702


def rms_scale(values, gain_row):
    mean_square = jnp.mean(values * values, axis=-1, keepdims=True)
    return values * lax.rsqrt(mean_square + epsilon) * gain_row


def positions_of(segment_row):
    counter = jnp.arange(segment_row.shape[0], dtype=jnp.int32)
    starting = jnp.concatenate(
        [jnp.ones((1,), dtype=jnp.bool_), segment_row[1:] != segment_row[:-1]]
    )
    first_index = lax.cummax(jnp.where(starting, counter, 0), axis=0)
    return counter - first_index


def adapter_per_token(segment_row, adapter_row):
    hits = segment_row[:, None] == jnp.arange(adapter_row.shape[0], dtype=jnp.int32)[None, :]
    return jnp.sum(jnp.where(hits, adapter_row[None, :], 0), axis=1)


def rotate_heads(values, positions):
    head_dim = values.shape[-1]
    half_dim = head_dim // 2
    frequency = theta_base ** (-2.0 * jnp.arange(half_dim, dtype=jnp.float32) / head_dim)
    angles = positions.astype(jnp.float32)[:, None] * frequency[None, :]
    cosine = jnp.cos(angles)[:, None, :]
    sine_part = jnp.sin(angles)[:, None, :]
    first_half = values[..., :half_dim]
    second_half = values[..., half_dim:]
    return jnp.concatenate(
        [
            first_half * cosine - second_half * sine_part,
            second_half * cosine + first_half * sine_part,
        ],
        axis=-1,
    )


def attend_heads(queries, key_heads, value_heads, segment_row, sink_row):
    tokens_now, kv_now, group_now, head_dim = queries.shape
    scores = jnp.einsum(
        "tkgh,skh->kgts", queries, key_heads, preferred_element_type=jnp.float32
    ) * head_dim ** (-0.5)
    counter = jnp.arange(tokens_now, dtype=jnp.int32)
    allowed = (segment_row[:, None] == segment_row[None, :]) & (
        counter[None, :] <= counter[:, None]
    )
    weights = jnp.where(allowed[None, None], jnp.exp(scores), 0.0)
    totals = jnp.sum(weights, axis=-1, keepdims=True) + jnp.exp(sink_row).reshape(
        kv_now, group_now, 1, 1
    )
    probs = (weights / totals).astype(jnp.bfloat16)
    blended_hidden = jnp.einsum(
        "kgts,skh->tkgh", probs, value_heads, preferred_element_type=jnp.float32
    )
    return blended_hidden.astype(jnp.bfloat16).reshape(tokens_now, kv_now * group_now * head_dim)


def shards(
    hidden,
    segments,
    request_adapter,
    routes,
    expert_gates,
    attention_gain,
    joined_weight,
    sinks,
    attention_out_weight,
    joined_down_maps,
    joined_up_maps,
    output_down_maps,
    output_up_maps,
    expert_norm_gain,
    expert_gate_weight,
    expert_up_weight,
    expert_down_weight,
    closing_gain,
    vocabulary_weight,
):
    groups = lax.axis_size("dp")
    columns = lax.axis_size("expert")
    position_dp = lax.axis_index("dp")
    segment_row = segments[0]
    adapter_row = request_adapter[0]
    col_tokens = segment_row.shape[0]
    gathered_rows = lax.all_gather(hidden, "dp", axis=1, tiled=True)
    width = gathered_rows.shape[1]
    normalized_hidden = rms_scale(gathered_rows.astype(jnp.float32), attention_gain).astype(
        jnp.bfloat16
    )
    joined_projection = jnp.dot(
        normalized_hidden, joined_weight.reshape(width, -1), preferred_element_type=jnp.float32
    )
    reduced_every_adapter = joined_down_maps.shape[1]
    reduced_hidden = jnp.dot(
        normalized_hidden, joined_down_maps, preferred_element_type=jnp.float32
    ).astype(jnp.bfloat16)
    rank_owner = jnp.arange(reduced_every_adapter, dtype=jnp.int32) // ADAPTER_RANK
    adapter_mask = adapter_per_token(segment_row, adapter_row)[:, None] == rank_owner[None, :]
    selected_reduced = jnp.where(adapter_mask, reduced_hidden, jnp.zeros_like(reduced_hidden))
    joined_projection = joined_projection + adapter_scale * jnp.dot(
        selected_reduced,
        joined_up_maps.reshape(reduced_every_adapter, -1),
        preferred_element_type=jnp.float32,
    )
    kv_here = joined_weight.shape[1]
    joined_projection = joined_projection.reshape(col_tokens, kv_here, QUERY_GROUP + 2, HEAD_SIZE)
    positions = positions_of(segment_row)
    queries = rotate_heads(
        joined_projection[:, :, :QUERY_GROUP].reshape(col_tokens, kv_here * QUERY_GROUP, HEAD_SIZE),
        positions,
    )
    queries = queries.astype(jnp.bfloat16).reshape(col_tokens, kv_here, QUERY_GROUP, HEAD_SIZE)
    key_heads = rotate_heads(joined_projection[:, :, QUERY_GROUP], positions).astype(jnp.bfloat16)
    value_heads = joined_projection[:, :, QUERY_GROUP + 1].astype(jnp.bfloat16)
    blended_hidden = attend_heads(queries, key_heads, value_heads, segment_row, sinks)
    share = col_tokens // groups
    quarter = hidden.shape[1]
    rank_total = output_down_maps.shape[1]
    route_pack = jnp.concatenate(
        [routes[0].astype(jnp.bfloat16), expert_gates[0].astype(jnp.bfloat16)], axis=1
    )
    pack_width = -(quarter + rank_total) % 128 or 128
    route_pack = jnp.pad(route_pack, ((0, 0), (0, pack_width - 2 * TOP)))
    pack_rows = lax.dynamic_update_slice_in_dim(
        jnp.zeros((col_tokens, pack_width), jnp.bfloat16), route_pack, position_dp * share, 0
    )
    partial_out = jnp.dot(blended_hidden, attention_out_weight, preferred_element_type=jnp.float32)
    low_local = jnp.dot(blended_hidden, output_down_maps, preferred_element_type=jnp.float32)
    joined_send = jnp.concatenate(
        [
            partial_out.astype(jnp.bfloat16).reshape(col_tokens, groups, quarter),
            jnp.broadcast_to(
                low_local.astype(jnp.bfloat16)[:, None, :], (col_tokens, groups, rank_total)
            ),
            jnp.broadcast_to(pack_rows[:, None, :], (col_tokens, groups, pack_width)),
        ],
        axis=2,
    ).reshape(col_tokens, -1)
    reduced_parts = []

    def reduce_rows(lo, rows):
        joined_back = lax.psum_scatter(
            joined_send[lo : lo + rows], "dp", scatter_dimension=1, tiled=True
        )
        return joined_back

    def resid_rows(joined_back, lo, rows):
        mine_out = joined_back[:, :quarter].astype(jnp.float32)
        output_reduced = joined_back[:, quarter : quarter + rank_total]
        selected_output = jnp.where(
            adapter_mask[lo : lo + rows], output_reduced, jnp.zeros_like(output_reduced)
        )
        adapter_delta = adapter_scale * jnp.dot(
            selected_output, output_up_maps, preferred_element_type=jnp.float32
        )
        resid_part = (
            hidden[lo : lo + rows].astype(jnp.float32) + mine_out + adapter_delta
        ).astype(jnp.bfloat16)
        return resid_part, joined_back[:, quarter + rank_total :]

    lane_pad = -width % 128
    wide = width + lane_pad
    experts = expert_gate_weight.shape[0] * columns
    capacity = 4 * share * TOP // (3 * experts)
    gate_weight = expert_gate_weight[0]
    up_weight = expert_up_weight[0]
    down_weight = jnp.pad(expert_down_weight[0], ((0, 0), (0, lane_pad)))
    chunk_blocks = [groups - groups // 2] + [1] * (groups // 2)
    halves = len(chunk_blocks)
    counter = jnp.arange(col_tokens, dtype=jnp.int32)
    request_ids = jnp.arange(REQS, dtype=jnp.int32)
    last_index = jnp.max(
        jnp.where(segment_row[None, :] == request_ids[:, None], counter[None, :], -1), axis=1
    )
    last_index = jnp.clip(last_index, 0, col_tokens - 1)
    moe_rows = []
    last_parts = []
    last_resid_parts = []
    held = None
    pending = None
    for h in range(halves):
        lo = sum(chunk_blocks[:h]) * share
        half_tokens = chunk_blocks[h] * share
        half_capacity = chunk_blocks[h] * capacity
        joined_h = reduce_rows(lo, half_tokens)
        resid_h, pack_h = resid_rows(joined_h, lo, half_tokens)
        reduced_parts.append(resid_h)
        column_h = lax.all_gather(resid_h, "dp", axis=1, tiled=True)
        if held is not None:
            column_h, held = lax.optimization_barrier((column_h, held))
        moe_in = rms_scale(column_h.astype(jnp.float32), expert_norm_gain).astype(jnp.bfloat16)
        moe_in = jnp.pad(moe_in, ((0, 0), (0, lane_pad)))
        route_flat = pack_h[:, :TOP].astype(jnp.int32).reshape(-1)
        gates_h = pack_h[:, TOP : 2 * TOP]
        one_hot = (route_flat[:, None] == jnp.arange(experts, dtype=jnp.int32)[None, :]).astype(
            jnp.int32
        )
        slot_rows = jnp.sum((jnp.cumsum(one_hot, axis=0) - one_hot) * one_hot, axis=1)
        target = route_flat * half_capacity + slot_rows
        source_rows = jnp.arange(route_flat.shape[0], dtype=jnp.int32) // TOP
        table = (
            jnp.full((experts * half_capacity,), half_tokens, jnp.int32)
            .at[target]
            .set(source_rows)
        )
        dispatch = (table[:, None] == jnp.arange(half_tokens, dtype=jnp.int32)[None, :]).astype(
            jnp.bfloat16
        )
        outgoing = (
            jnp.dot(dispatch, moe_in, preferred_element_type=jnp.float32)
            .astype(jnp.bfloat16)
            .reshape(experts, half_capacity, wide)
        )
        arrived = lax.all_to_all(outgoing, "expert", split_axis=0, concat_axis=0, tiled=True)
        if h == 0:
            held = arrived
        else:
            arrived = lax.optimization_barrier((arrived, held))[0]
        rows_in = arrived.reshape(-1, wide)[:, :width]
        gate_part = jnp.dot(rows_in, gate_weight, preferred_element_type=jnp.float32)
        up_part = jnp.dot(rows_in, up_weight, preferred_element_type=jnp.float32)
        activated = (gate_part * jax.nn.sigmoid(glu_alpha * gate_part) * (up_part + 1.0)).astype(
            jnp.bfloat16
        )
        shares_out = (
            jnp.dot(activated, down_weight, preferred_element_type=jnp.float32)
            .astype(jnp.bfloat16)
            .reshape(experts, half_capacity, wide)
        )
        if pending is not None:
            shares_out, pending = lax.optimization_barrier((shares_out, pending))
            moe_rows.append(lax.psum_scatter(pending, "dp", scatter_dimension=1, tiled=True))
            pending = None
        answers = lax.all_to_all(shares_out, "expert", split_axis=0, concat_axis=0, tiled=True)
        slot_ids = jnp.arange(experts * half_capacity, dtype=jnp.int32)
        combine = jnp.sum(
            jnp.where(
                target.reshape(half_tokens, TOP)[:, :, None] == slot_ids[None, None, :],
                gates_h[:, :, None],
                jnp.zeros((), jnp.bfloat16),
            ),
            axis=1,
        ).astype(jnp.bfloat16)
        mixture = jnp.dot(
            combine,
            answers.reshape(experts * half_capacity, wide),
            preferred_element_type=jnp.float32,
        )[:, :width]
        local_last = jnp.clip(last_index - lo, 0, half_tokens - 1)
        inside = ((last_index >= lo) & (last_index < lo + half_tokens))[:, None]
        last_parts.append(
            jnp.where(inside, jnp.take(mixture, local_last, axis=0), jnp.zeros((), jnp.float32))
        )
        last_resid_parts.append(
            jnp.where(inside, jnp.take(column_h, local_last, axis=0), jnp.zeros((), jnp.bfloat16))
        )
        if h < halves - 1:
            pending = mixture.astype(jnp.bfloat16)
        else:
            last_mix = sum(last_parts).reshape(REQS * groups, quarter)
            moe_send = jnp.concatenate(
                [mixture, jnp.tile(last_mix, (1, groups))], axis=0
            ).astype(jnp.bfloat16)
            moe_rows.append(lax.psum_scatter(moe_send, "dp", scatter_dimension=1, tiled=True))
    moe_back = jnp.concatenate(moe_rows, axis=0)
    moe_rounded = moe_back[:col_tokens].astype(jnp.float32).astype(jnp.bfloat16)
    resid = jnp.concatenate(reduced_parts, axis=0)
    hidden_out = (resid.astype(jnp.float32) + moe_rounded.astype(jnp.float32)).astype(jnp.bfloat16)
    last_moe = moe_back[col_tokens:].reshape(REQS, width)
    last_resid = sum(part.astype(jnp.float32) for part in last_resid_parts)
    last_hidden = (last_resid + last_moe.astype(jnp.float32)).astype(jnp.bfloat16)
    ends = rms_scale(last_hidden.astype(jnp.float32), closing_gain).astype(jnp.bfloat16)
    tail_rows = lax.all_gather(ends, "expert", axis=0, tiled=True)
    logits = jnp.dot(tail_rows, vocabulary_weight, preferred_element_type=jnp.float32)
    return (hidden_out, logits)


def solution(mesh):
    in_specs = (
        P("expert", "dp"),
        P("expert", None),
        P("expert", None),
        P("expert", "dp", None),
        P("expert", "dp", None),
        P(),
        P(None, "dp", None),
        P("dp"),
        P("dp", None),
        P(),
        P(None, "dp", None),
        P("dp", None),
        P(None, "dp"),
        P(),
        P("expert", None, "dp"),
        P("expert", None, "dp"),
        P("expert", "dp", None),
        P(),
        P(None, ("dp", "expert")),
    )
    out_specs = (P("expert", "dp"), P(None, ("dp", "expert")))
    return jax.shard_map(shards, mesh=mesh, in_specs=in_specs, out_specs=out_specs, check_vma=False)
```

```python
import jax
import jax.numpy as jnp
from jax import lax
from jax.sharding import PartitionSpec as P

HEAD_SIZE = 64
QUERY_GROUP = 8
TOP = 4
ADAPTER_RANK = 16
REQS = 4


epsilon = 1e-05
theta_base = 150000.0
adapter_scale = 2.0
glu_alpha = 1.702


def rms_scale(values, gain_row):
    mean_square = jnp.mean(values * values, axis=-1, keepdims=True)
    return values * lax.rsqrt(mean_square + epsilon) * gain_row


def positions_of(segment_row):
    counter = jnp.arange(segment_row.shape[0], dtype=jnp.int32)
    starting = jnp.concatenate(
        [jnp.ones((1,), dtype=jnp.bool_), segment_row[1:] != segment_row[:-1]]
    )
    first_index = lax.cummax(jnp.where(starting, counter, 0), axis=0)
    return counter - first_index


def adapter_per_token(segment_row, adapter_row):
    hits = segment_row[:, None] == jnp.arange(adapter_row.shape[0], dtype=jnp.int32)[None, :]
    return jnp.sum(jnp.where(hits, adapter_row[None, :], 0), axis=1)


def rotate_heads(values, positions):
    head_dim = values.shape[-1]
    half_dim = head_dim // 2
    frequency = theta_base ** (-2.0 * jnp.arange(half_dim, dtype=jnp.float32) / head_dim)
    angles = positions.astype(jnp.float32)[:, None] * frequency[None, :]
    cosine = jnp.cos(angles)[:, None, :]
    sine_part = jnp.sin(angles)[:, None, :]
    first_half = values[..., :half_dim]
    second_half = values[..., half_dim:]
    return jnp.concatenate(
        [
            first_half * cosine - second_half * sine_part,
            second_half * cosine + first_half * sine_part,
        ],
        axis=-1,
    )


def attend_heads(queries, key_heads, value_heads, segment_row, sink_row):
    tokens_now, kv_now, group_now, head_dim = queries.shape
    scores = jnp.einsum(
        "tkgh,skh->kgts", queries, key_heads, preferred_element_type=jnp.float32
    ) * head_dim ** (-0.5)
    counter = jnp.arange(tokens_now, dtype=jnp.int32)
    allowed = (segment_row[:, None] == segment_row[None, :]) & (
        counter[None, :] <= counter[:, None]
    )
    weights = jnp.where(allowed[None, None], jnp.exp(scores), 0.0)
    totals = jnp.sum(weights, axis=-1, keepdims=True) + jnp.exp(sink_row).reshape(
        kv_now, group_now, 1, 1
    )
    probs = (weights / totals).astype(jnp.bfloat16)
    blended_hidden = jnp.einsum(
        "kgts,skh->tkgh", probs, value_heads, preferred_element_type=jnp.float32
    )
    return blended_hidden.astype(jnp.bfloat16).reshape(tokens_now, kv_now * group_now * head_dim)


def shards(
    hidden,
    segments,
    request_adapter,
    routes,
    expert_gates,
    attention_gain,
    joined_weight,
    sinks,
    attention_out_weight,
    joined_down_maps,
    joined_up_maps,
    output_down_maps,
    output_up_maps,
    expert_norm_gain,
    expert_gate_weight,
    expert_up_weight,
    expert_down_weight,
    closing_gain,
    vocabulary_weight,
):
    groups = lax.axis_size("dp")
    columns = lax.axis_size("expert")
    position_dp = lax.axis_index("dp")
    segment_row = segments[0]
    adapter_row = request_adapter[0]
    col_tokens = segment_row.shape[0]
    gathered_rows = lax.all_gather(hidden, "dp", axis=1, tiled=True)
    width = gathered_rows.shape[1]
    normalized_hidden = rms_scale(gathered_rows.astype(jnp.float32), attention_gain).astype(
        jnp.bfloat16
    )
    joined_projection = jnp.dot(
        normalized_hidden, joined_weight.reshape(width, -1), preferred_element_type=jnp.float32
    )
    reduced_every_adapter = joined_down_maps.shape[1]
    reduced_hidden = jnp.dot(
        normalized_hidden, joined_down_maps, preferred_element_type=jnp.float32
    ).astype(jnp.bfloat16)
    rank_owner = jnp.arange(reduced_every_adapter, dtype=jnp.int32) // ADAPTER_RANK
    adapter_mask = adapter_per_token(segment_row, adapter_row)[:, None] == rank_owner[None, :]
    selected_reduced = jnp.where(adapter_mask, reduced_hidden, jnp.zeros_like(reduced_hidden))
    joined_projection = joined_projection + adapter_scale * jnp.dot(
        selected_reduced,
        joined_up_maps.reshape(reduced_every_adapter, -1),
        preferred_element_type=jnp.float32,
    )
    kv_here = joined_weight.shape[1]
    joined_projection = joined_projection.reshape(col_tokens, kv_here, QUERY_GROUP + 2, HEAD_SIZE)
    positions = positions_of(segment_row)
    queries = rotate_heads(
        joined_projection[:, :, :QUERY_GROUP].reshape(col_tokens, kv_here * QUERY_GROUP, HEAD_SIZE),
        positions,
    )
    queries = queries.astype(jnp.bfloat16).reshape(col_tokens, kv_here, QUERY_GROUP, HEAD_SIZE)
    key_heads = rotate_heads(joined_projection[:, :, QUERY_GROUP], positions).astype(jnp.bfloat16)
    value_heads = joined_projection[:, :, QUERY_GROUP + 1].astype(jnp.bfloat16)
    blended_hidden = attend_heads(queries, key_heads, value_heads, segment_row, sinks)
    share = col_tokens // groups
    quarter = hidden.shape[1]
    rank_total = output_down_maps.shape[1]
    route_pack = jnp.concatenate(
        [routes[0].astype(jnp.bfloat16), expert_gates[0].astype(jnp.bfloat16)], axis=1
    )
    pack_width = -(quarter + rank_total) % 128 or 128
    route_pack = jnp.pad(route_pack, ((0, 0), (0, pack_width - 2 * TOP)))
    pack_rows = lax.dynamic_update_slice_in_dim(
        jnp.zeros((col_tokens, pack_width), jnp.bfloat16), route_pack, position_dp * share, 0
    )
    partial_out = jnp.dot(blended_hidden, attention_out_weight, preferred_element_type=jnp.float32)
    low_local = jnp.dot(blended_hidden, output_down_maps, preferred_element_type=jnp.float32)
    joined_send = jnp.concatenate(
        [
            partial_out.astype(jnp.bfloat16).reshape(col_tokens, groups, quarter),
            jnp.broadcast_to(
                low_local.astype(jnp.bfloat16)[:, None, :], (col_tokens, groups, rank_total)
            ),
            jnp.broadcast_to(pack_rows[:, None, :], (col_tokens, groups, pack_width)),
        ],
        axis=2,
    ).reshape(col_tokens, -1)
    reduced_parts = []

    def reduce_rows(lo, rows):
        joined_back = lax.psum_scatter(
            joined_send[lo : lo + rows], "dp", scatter_dimension=1, tiled=True
        )
        return joined_back

    def resid_rows(joined_back, lo, rows):
        mine_out = joined_back[:, :quarter].astype(jnp.float32)
        output_reduced = joined_back[:, quarter : quarter + rank_total]
        selected_output = jnp.where(
            adapter_mask[lo : lo + rows], output_reduced, jnp.zeros_like(output_reduced)
        )
        adapter_delta = adapter_scale * jnp.dot(
            selected_output, output_up_maps, preferred_element_type=jnp.float32
        )
        resid_part = (
            hidden[lo : lo + rows].astype(jnp.float32) + mine_out + adapter_delta
        ).astype(jnp.bfloat16)
        return resid_part, joined_back[:, quarter + rank_total :]

    lane_pad = -width % 128
    wide = width + lane_pad
    experts = expert_gate_weight.shape[0] * columns
    capacity = 4 * share * TOP // (3 * experts)
    gate_weight = expert_gate_weight[0]
    up_weight = expert_up_weight[0]
    down_weight = jnp.pad(expert_down_weight[0], ((0, 0), (0, lane_pad)))
    halves = 2 if groups % 2 == 0 else 1
    half_tokens = col_tokens // halves
    half_capacity = (groups // halves) * capacity
    counter = jnp.arange(col_tokens, dtype=jnp.int32)
    request_ids = jnp.arange(REQS, dtype=jnp.int32)
    last_index = jnp.max(
        jnp.where(segment_row[None, :] == request_ids[:, None], counter[None, :], -1), axis=1
    )
    last_index = jnp.clip(last_index, 0, col_tokens - 1)
    moe_rows = []
    last_parts = []
    last_resid_parts = []
    held = None
    pending = None
    for h in range(halves):
        lo = h * half_tokens
        joined_h = reduce_rows(lo, half_tokens)
        resid_h, pack_h = resid_rows(joined_h, lo, half_tokens)
        reduced_parts.append(resid_h)
        column_h = lax.all_gather(resid_h, "dp", axis=1, tiled=True)
        if held is not None:
            column_h, held = lax.optimization_barrier((column_h, held))
        moe_in = rms_scale(column_h.astype(jnp.float32), expert_norm_gain).astype(jnp.bfloat16)
        moe_in = jnp.pad(moe_in, ((0, 0), (0, lane_pad)))
        route_flat = pack_h[:, :TOP].astype(jnp.int32).reshape(-1)
        gates_h = pack_h[:, TOP : 2 * TOP]
        one_hot = (route_flat[:, None] == jnp.arange(experts, dtype=jnp.int32)[None, :]).astype(
            jnp.int32
        )
        slot_rows = jnp.sum((jnp.cumsum(one_hot, axis=0) - one_hot) * one_hot, axis=1)
        target = route_flat * half_capacity + slot_rows
        source_rows = jnp.arange(route_flat.shape[0], dtype=jnp.int32) // TOP
        table = (
            jnp.full((experts * half_capacity,), half_tokens, jnp.int32)
            .at[target]
            .set(source_rows)
        )
        dispatch = (table[:, None] == jnp.arange(half_tokens, dtype=jnp.int32)[None, :]).astype(
            jnp.bfloat16
        )
        outgoing = (
            jnp.dot(dispatch, moe_in, preferred_element_type=jnp.float32)
            .astype(jnp.bfloat16)
            .reshape(experts, half_capacity, wide)
        )
        arrived = lax.all_to_all(outgoing, "expert", split_axis=0, concat_axis=0, tiled=True)
        if h == 0:
            held = arrived
        else:
            arrived = lax.optimization_barrier((arrived, held))[0]
        rows_in = arrived.reshape(-1, wide)[:, :width]
        gate_part = jnp.dot(rows_in, gate_weight, preferred_element_type=jnp.float32)
        up_part = jnp.dot(rows_in, up_weight, preferred_element_type=jnp.float32)
        activated = (gate_part * jax.nn.sigmoid(glu_alpha * gate_part) * (up_part + 1.0)).astype(
            jnp.bfloat16
        )
        shares_out = (
            jnp.dot(activated, down_weight, preferred_element_type=jnp.float32)
            .astype(jnp.bfloat16)
            .reshape(experts, half_capacity, wide)
        )
        if pending is not None:
            shares_out, pending = lax.optimization_barrier((shares_out, pending))
            moe_rows.append(lax.psum_scatter(pending, "dp", scatter_dimension=1, tiled=True))
            pending = None
        answers = lax.all_to_all(shares_out, "expert", split_axis=0, concat_axis=0, tiled=True)
        if moe_rows:
            answers, moe_rows[-1] = lax.optimization_barrier((answers, moe_rows[-1]))
        slot_ids = jnp.arange(experts * half_capacity, dtype=jnp.int32)
        combine = jnp.sum(
            jnp.where(
                target.reshape(half_tokens, TOP)[:, :, None] == slot_ids[None, None, :],
                gates_h[:, :, None],
                jnp.zeros((), jnp.bfloat16),
            ),
            axis=1,
        ).astype(jnp.bfloat16)
        mixture = jnp.dot(
            combine,
            answers.reshape(experts * half_capacity, wide),
            preferred_element_type=jnp.float32,
        )[:, :width]
        local_last = jnp.clip(last_index - lo, 0, half_tokens - 1)
        inside = ((last_index >= lo) & (last_index < lo + half_tokens))[:, None]
        last_parts.append(
            jnp.where(inside, jnp.take(mixture, local_last, axis=0), jnp.zeros((), jnp.float32))
        )
        last_resid_parts.append(
            jnp.where(inside, jnp.take(column_h, local_last, axis=0), jnp.zeros((), jnp.bfloat16))
        )
        if h < halves - 1:
            pending = mixture.astype(jnp.bfloat16)
        else:
            last_mix = sum(last_parts).reshape(REQS * groups, quarter)
            extra_back = lax.psum_scatter(
                jnp.tile(last_mix, (1, groups)).astype(jnp.bfloat16),
                "dp",
                scatter_dimension=1,
                tiled=True,
            )
            moe_send, extra_back = lax.optimization_barrier(
                (mixture.astype(jnp.bfloat16), extra_back)
            )
            moe_rows.append(lax.psum_scatter(moe_send, "dp", scatter_dimension=1, tiled=True))
    moe_back = jnp.concatenate(moe_rows, axis=0)
    moe_rounded = moe_back.astype(jnp.float32).astype(jnp.bfloat16)
    resid = jnp.concatenate(reduced_parts, axis=0)
    hidden_out = (resid.astype(jnp.float32) + moe_rounded.astype(jnp.float32)).astype(jnp.bfloat16)
    last_moe = extra_back.reshape(REQS, width)
    last_resid = sum(part.astype(jnp.float32) for part in last_resid_parts)
    last_hidden = (last_resid + last_moe.astype(jnp.float32)).astype(jnp.bfloat16)
    ends = rms_scale(last_hidden.astype(jnp.float32), closing_gain).astype(jnp.bfloat16)
    tail_rows = lax.all_gather(ends, "expert", axis=0, tiled=True)
    logits = jnp.dot(tail_rows, vocabulary_weight, preferred_element_type=jnp.float32)
    return (hidden_out, logits)


def solution(mesh):
    in_specs = (
        P("expert", "dp"),
        P("expert", None),
        P("expert", None),
        P("expert", "dp", None),
        P("expert", "dp", None),
        P(),
        P(None, "dp", None),
        P("dp"),
        P("dp", None),
        P(),
        P(None, "dp", None),
        P("dp", None),
        P(None, "dp"),
        P(),
        P("expert", None, "dp"),
        P("expert", None, "dp"),
        P("expert", "dp", None),
        P(),
        P(None, ("dp", "expert")),
    )
    out_specs = (P("expert", "dp"), P(None, ("dp", "expert")))
    return jax.shard_map(shards, mesh=mesh, in_specs=in_specs, out_specs=out_specs, check_vma=False)
```

```python
import jax
import jax.numpy as jnp
from jax import lax
from jax.sharding import PartitionSpec as P

HEAD_SIZE = 64
QUERY_GROUP = 8
TOP = 4
ADAPTER_RANK = 16
REQS = 4


epsilon = 1e-05
theta_base = 150000.0
adapter_scale = 2.0
glu_alpha = 1.702


def rms_scale(values, gain_row):
    mean_square = jnp.mean(values * values, axis=-1, keepdims=True)
    return values * lax.rsqrt(mean_square + epsilon) * gain_row


def positions_of(segment_row):
    counter = jnp.arange(segment_row.shape[0], dtype=jnp.int32)
    starting = jnp.concatenate(
        [jnp.ones((1,), dtype=jnp.bool_), segment_row[1:] != segment_row[:-1]]
    )
    first_index = lax.cummax(jnp.where(starting, counter, 0), axis=0)
    return counter - first_index


def adapter_per_token(segment_row, adapter_row):
    hits = segment_row[:, None] == jnp.arange(adapter_row.shape[0], dtype=jnp.int32)[None, :]
    return jnp.sum(jnp.where(hits, adapter_row[None, :], 0), axis=1)


def rotate_heads(values, positions):
    head_dim = values.shape[-1]
    half_dim = head_dim // 2
    frequency = theta_base ** (-2.0 * jnp.arange(half_dim, dtype=jnp.float32) / head_dim)
    angles = positions.astype(jnp.float32)[:, None] * frequency[None, :]
    cosine = jnp.cos(angles)[:, None, :]
    sine_part = jnp.sin(angles)[:, None, :]
    first_half = values[..., :half_dim]
    second_half = values[..., half_dim:]
    return jnp.concatenate(
        [
            first_half * cosine - second_half * sine_part,
            second_half * cosine + first_half * sine_part,
        ],
        axis=-1,
    )


def attend_heads(queries, key_heads, value_heads, segment_row, sink_row):
    tokens_now, kv_now, group_now, head_dim = queries.shape
    scores = jnp.einsum(
        "tkgh,skh->kgts", queries, key_heads, preferred_element_type=jnp.float32
    ) * head_dim ** (-0.5)
    counter = jnp.arange(tokens_now, dtype=jnp.int32)
    allowed = (segment_row[:, None] == segment_row[None, :]) & (
        counter[None, :] <= counter[:, None]
    )
    weights = jnp.where(allowed[None, None], jnp.exp(scores), 0.0)
    totals = jnp.sum(weights, axis=-1, keepdims=True) + jnp.exp(sink_row).reshape(
        kv_now, group_now, 1, 1
    )
    probs = (weights / totals).astype(jnp.bfloat16)
    blended_hidden = jnp.einsum(
        "kgts,skh->tkgh", probs, value_heads, preferred_element_type=jnp.float32
    )
    return blended_hidden.astype(jnp.bfloat16).reshape(tokens_now, kv_now * group_now * head_dim)


def shards(
    hidden,
    segments,
    request_adapter,
    routes,
    expert_gates,
    attention_gain,
    joined_weight,
    sinks,
    attention_out_weight,
    joined_down_maps,
    joined_up_maps,
    output_down_maps,
    output_up_maps,
    expert_norm_gain,
    expert_gate_weight,
    expert_up_weight,
    expert_down_weight,
    closing_gain,
    vocabulary_weight,
):
    groups = lax.axis_size("dp")
    columns = lax.axis_size("expert")
    position_dp = lax.axis_index("dp")
    segment_row = segments[0]
    adapter_row = request_adapter[0]
    col_tokens = segment_row.shape[0]
    gathered_rows = lax.all_gather(hidden, "dp", axis=1, tiled=True)
    width = gathered_rows.shape[1]
    normalized_hidden = rms_scale(gathered_rows.astype(jnp.float32), attention_gain).astype(
        jnp.bfloat16
    )
    joined_projection = jnp.dot(
        normalized_hidden, joined_weight.reshape(width, -1), preferred_element_type=jnp.float32
    )
    reduced_every_adapter = joined_down_maps.shape[1]
    reduced_hidden = jnp.dot(
        normalized_hidden, joined_down_maps, preferred_element_type=jnp.float32
    ).astype(jnp.bfloat16)
    rank_owner = jnp.arange(reduced_every_adapter, dtype=jnp.int32) // ADAPTER_RANK
    adapter_mask = adapter_per_token(segment_row, adapter_row)[:, None] == rank_owner[None, :]
    selected_reduced = jnp.where(adapter_mask, reduced_hidden, jnp.zeros_like(reduced_hidden))
    joined_projection = joined_projection + adapter_scale * jnp.dot(
        selected_reduced,
        joined_up_maps.reshape(reduced_every_adapter, -1),
        preferred_element_type=jnp.float32,
    )
    kv_here = joined_weight.shape[1]
    joined_projection = joined_projection.reshape(col_tokens, kv_here, QUERY_GROUP + 2, HEAD_SIZE)
    positions = positions_of(segment_row)
    queries = rotate_heads(
        joined_projection[:, :, :QUERY_GROUP].reshape(col_tokens, kv_here * QUERY_GROUP, HEAD_SIZE),
        positions,
    )
    queries = queries.astype(jnp.bfloat16).reshape(col_tokens, kv_here, QUERY_GROUP, HEAD_SIZE)
    key_heads = rotate_heads(joined_projection[:, :, QUERY_GROUP], positions).astype(jnp.bfloat16)
    value_heads = joined_projection[:, :, QUERY_GROUP + 1].astype(jnp.bfloat16)
    blended_hidden = attend_heads(queries, key_heads, value_heads, segment_row, sinks)
    share = col_tokens // groups
    quarter = hidden.shape[1]
    rank_total = output_down_maps.shape[1]
    route_pack = jnp.concatenate(
        [routes[0].astype(jnp.bfloat16), expert_gates[0].astype(jnp.bfloat16)], axis=1
    )
    pack_width = -(quarter + rank_total) % 128 or 128
    route_pack = jnp.pad(route_pack, ((0, 0), (0, pack_width - 2 * TOP)))
    pack_rows = lax.dynamic_update_slice_in_dim(
        jnp.zeros((col_tokens, pack_width), jnp.bfloat16), route_pack, position_dp * share, 0
    )
    partial_out = jnp.dot(blended_hidden, attention_out_weight, preferred_element_type=jnp.float32)
    low_local = jnp.dot(blended_hidden, output_down_maps, preferred_element_type=jnp.float32)
    joined_send = jnp.concatenate(
        [
            partial_out.astype(jnp.bfloat16).reshape(col_tokens, groups, quarter),
            jnp.broadcast_to(
                low_local.astype(jnp.bfloat16)[:, None, :], (col_tokens, groups, rank_total)
            ),
            jnp.broadcast_to(pack_rows[:, None, :], (col_tokens, groups, pack_width)),
        ],
        axis=2,
    ).reshape(col_tokens, -1)
    reduced_parts = []

    def reduce_rows(lo, rows):
        joined_back = lax.psum_scatter(
            joined_send[lo : lo + rows], "dp", scatter_dimension=1, tiled=True
        )
        return joined_back

    def resid_rows(joined_back, lo, rows):
        mine_out = joined_back[:, :quarter].astype(jnp.float32)
        output_reduced = joined_back[:, quarter : quarter + rank_total]
        selected_output = jnp.where(
            adapter_mask[lo : lo + rows], output_reduced, jnp.zeros_like(output_reduced)
        )
        adapter_delta = adapter_scale * jnp.dot(
            selected_output, output_up_maps, preferred_element_type=jnp.float32
        )
        resid_part = (
            hidden[lo : lo + rows].astype(jnp.float32) + mine_out + adapter_delta
        ).astype(jnp.bfloat16)
        return resid_part, joined_back[:, quarter + rank_total :]

    lane_pad = -width % 128
    wide = width + lane_pad
    experts = expert_gate_weight.shape[0] * columns
    capacity = 4 * share * TOP // (3 * experts)
    gate_weight = expert_gate_weight[0]
    up_weight = expert_up_weight[0]
    down_weight = jnp.pad(expert_down_weight[0], ((0, 0), (0, lane_pad)))
    halves = 2 if groups % 2 == 0 else 1
    half_tokens = col_tokens // halves
    half_capacity = (groups // halves) * capacity
    counter = jnp.arange(col_tokens, dtype=jnp.int32)
    request_ids = jnp.arange(REQS, dtype=jnp.int32)
    last_index = jnp.max(
        jnp.where(segment_row[None, :] == request_ids[:, None], counter[None, :], -1), axis=1
    )
    last_index = jnp.clip(last_index, 0, col_tokens - 1)
    moe_rows = []
    last_parts = []
    last_resid_parts = []
    held = None
    pending = None
    for h in range(halves):
        lo = h * half_tokens
        joined_h = reduce_rows(lo, half_tokens)
        resid_h, pack_h = resid_rows(joined_h, lo, half_tokens)
        reduced_parts.append(resid_h)
        column_h = (
            lax.all_gather(resid_h, "dp", axis=0, tiled=False)
            .transpose(1, 0, 2)
            .reshape(half_tokens, groups * quarter)
        )
        if held is not None:
            column_h, held = lax.optimization_barrier((column_h, held))
        moe_in = rms_scale(column_h.astype(jnp.float32), expert_norm_gain).astype(jnp.bfloat16)
        moe_in = jnp.pad(moe_in, ((0, 0), (0, lane_pad)))
        route_flat = pack_h[:, :TOP].astype(jnp.int32).reshape(-1)
        gates_h = pack_h[:, TOP : 2 * TOP]
        one_hot = (route_flat[:, None] == jnp.arange(experts, dtype=jnp.int32)[None, :]).astype(
            jnp.int32
        )
        slot_rows = jnp.sum((jnp.cumsum(one_hot, axis=0) - one_hot) * one_hot, axis=1)
        target = route_flat * half_capacity + slot_rows
        source_rows = jnp.arange(route_flat.shape[0], dtype=jnp.int32) // TOP
        table = (
            jnp.full((experts * half_capacity,), half_tokens, jnp.int32)
            .at[target]
            .set(source_rows)
        )
        dispatch = (table[:, None] == jnp.arange(half_tokens, dtype=jnp.int32)[None, :]).astype(
            jnp.bfloat16
        )
        outgoing = (
            jnp.dot(dispatch, moe_in, preferred_element_type=jnp.float32)
            .astype(jnp.bfloat16)
            .reshape(experts, half_capacity, wide)
        )
        arrived = lax.all_to_all(outgoing, "expert", split_axis=0, concat_axis=0, tiled=True)
        if h == 0:
            held = arrived
        else:
            arrived = lax.optimization_barrier((arrived, held))[0]
        rows_in = arrived.reshape(-1, wide)[:, :width]
        gate_part = jnp.dot(rows_in, gate_weight, preferred_element_type=jnp.float32)
        up_part = jnp.dot(rows_in, up_weight, preferred_element_type=jnp.float32)
        activated = (gate_part * jax.nn.sigmoid(glu_alpha * gate_part) * (up_part + 1.0)).astype(
            jnp.bfloat16
        )
        shares_out = (
            jnp.dot(activated, down_weight, preferred_element_type=jnp.float32)
            .astype(jnp.bfloat16)
            .reshape(experts, half_capacity, wide)
        )
        if pending is not None:
            shares_out, pending = lax.optimization_barrier((shares_out, pending))
            moe_rows.append(lax.psum_scatter(pending, "dp", scatter_dimension=1, tiled=True))
            pending = None
        answers = lax.all_to_all(shares_out, "expert", split_axis=0, concat_axis=0, tiled=True)
        slot_ids = jnp.arange(experts * half_capacity, dtype=jnp.int32)
        combine = jnp.sum(
            jnp.where(
                target.reshape(half_tokens, TOP)[:, :, None] == slot_ids[None, None, :],
                gates_h[:, :, None],
                jnp.zeros((), jnp.bfloat16),
            ),
            axis=1,
        ).astype(jnp.bfloat16)
        mixture = jnp.dot(
            combine,
            answers.reshape(experts * half_capacity, wide),
            preferred_element_type=jnp.float32,
        )[:, :width]
        local_last = jnp.clip(last_index - lo, 0, half_tokens - 1)
        inside = ((last_index >= lo) & (last_index < lo + half_tokens))[:, None]
        last_parts.append(
            jnp.where(inside, jnp.take(mixture, local_last, axis=0), jnp.zeros((), jnp.float32))
        )
        last_resid_parts.append(
            jnp.where(inside, jnp.take(column_h, local_last, axis=0), jnp.zeros((), jnp.bfloat16))
        )
        if h < halves - 1:
            pending = mixture.astype(jnp.bfloat16)
        else:
            last_mix = sum(last_parts).reshape(REQS * groups, quarter)
            moe_send = jnp.concatenate(
                [mixture, jnp.tile(last_mix, (1, groups))], axis=0
            ).astype(jnp.bfloat16)
            moe_rows.append(lax.psum_scatter(moe_send, "dp", scatter_dimension=1, tiled=True))
    moe_back = jnp.concatenate(moe_rows, axis=0)
    moe_rounded = moe_back[:col_tokens].astype(jnp.float32).astype(jnp.bfloat16)
    resid = jnp.concatenate(reduced_parts, axis=0)
    hidden_out = (resid.astype(jnp.float32) + moe_rounded.astype(jnp.float32)).astype(jnp.bfloat16)
    last_moe = moe_back[col_tokens:].reshape(REQS, width)
    last_resid = sum(part.astype(jnp.float32) for part in last_resid_parts)
    last_hidden = (last_resid + last_moe.astype(jnp.float32)).astype(jnp.bfloat16)
    ends = rms_scale(last_hidden.astype(jnp.float32), closing_gain).astype(jnp.bfloat16)
    tail_rows = lax.all_gather(ends, "expert", axis=0, tiled=True)
    logits = jnp.dot(tail_rows, vocabulary_weight, preferred_element_type=jnp.float32)
    return (hidden_out, logits)


def solution(mesh):
    in_specs = (
        P("expert", "dp"),
        P("expert", None),
        P("expert", None),
        P("expert", "dp", None),
        P("expert", "dp", None),
        P(),
        P(None, "dp", None),
        P("dp"),
        P("dp", None),
        P(),
        P(None, "dp", None),
        P("dp", None),
        P(None, "dp"),
        P(),
        P("expert", None, "dp"),
        P("expert", None, "dp"),
        P("expert", "dp", None),
        P(),
        P(None, ("dp", "expert")),
    )
    out_specs = (P("expert", "dp"), P(None, ("dp", "expert")))
    return jax.shard_map(shards, mesh=mesh, in_specs=in_specs, out_specs=out_specs, check_vma=False)
```

```python
import jax
import jax.numpy as jnp
from jax import lax
from jax.sharding import PartitionSpec as P

HEAD_SIZE = 64
QUERY_GROUP = 8
TOP = 4
ADAPTER_RANK = 16
REQS = 4


epsilon = 1e-05
theta_base = 150000.0
adapter_scale = 2.0
glu_alpha = 1.702


def rms_scale(values, gain_row):
    mean_square = jnp.mean(values * values, axis=-1, keepdims=True)
    return values * lax.rsqrt(mean_square + epsilon) * gain_row


def positions_of(segment_row):
    counter = jnp.arange(segment_row.shape[0], dtype=jnp.int32)
    starting = jnp.concatenate(
        [jnp.ones((1,), dtype=jnp.bool_), segment_row[1:] != segment_row[:-1]]
    )
    first_index = lax.cummax(jnp.where(starting, counter, 0), axis=0)
    return counter - first_index


def adapter_per_token(segment_row, adapter_row):
    hits = segment_row[:, None] == jnp.arange(adapter_row.shape[0], dtype=jnp.int32)[None, :]
    return jnp.sum(jnp.where(hits, adapter_row[None, :], 0), axis=1)


def rotate_heads(values, positions):
    head_dim = values.shape[-1]
    half_dim = head_dim // 2
    frequency = theta_base ** (-2.0 * jnp.arange(half_dim, dtype=jnp.float32) / head_dim)
    angles = positions.astype(jnp.float32)[:, None] * frequency[None, :]
    cosine = jnp.cos(angles)[:, None, :]
    sine_part = jnp.sin(angles)[:, None, :]
    first_half = values[..., :half_dim]
    second_half = values[..., half_dim:]
    return jnp.concatenate(
        [
            first_half * cosine - second_half * sine_part,
            second_half * cosine + first_half * sine_part,
        ],
        axis=-1,
    )


def attend_heads(queries, key_heads, value_heads, segment_row, sink_row):
    tokens_now, kv_now, group_now, head_dim = queries.shape
    scores = jnp.einsum(
        "tkgh,skh->kgts", queries, key_heads, preferred_element_type=jnp.float32
    ) * head_dim ** (-0.5)
    counter = jnp.arange(tokens_now, dtype=jnp.int32)
    allowed = (segment_row[:, None] == segment_row[None, :]) & (
        counter[None, :] <= counter[:, None]
    )
    weights = jnp.where(allowed[None, None], jnp.exp(scores), 0.0)
    totals = jnp.sum(weights, axis=-1, keepdims=True) + jnp.exp(sink_row).reshape(
        kv_now, group_now, 1, 1
    )
    probs = (weights / totals).astype(jnp.bfloat16)
    blended_hidden = jnp.einsum(
        "kgts,skh->tkgh", probs, value_heads, preferred_element_type=jnp.float32
    )
    return blended_hidden.astype(jnp.bfloat16).reshape(tokens_now, kv_now * group_now * head_dim)


def shards(
    hidden,
    segments,
    request_adapter,
    routes,
    expert_gates,
    attention_gain,
    joined_weight,
    sinks,
    attention_out_weight,
    joined_down_maps,
    joined_up_maps,
    output_down_maps,
    output_up_maps,
    expert_norm_gain,
    expert_gate_weight,
    expert_up_weight,
    expert_down_weight,
    closing_gain,
    vocabulary_weight,
):
    groups = lax.axis_size("dp")
    columns = lax.axis_size("expert")
    position_dp = lax.axis_index("dp")
    segment_row = segments[0]
    adapter_row = request_adapter[0]
    col_tokens = segment_row.shape[0]
    gathered_rows = lax.all_gather(hidden, "dp", axis=1, tiled=True)
    width = gathered_rows.shape[1]
    normalized_hidden = rms_scale(gathered_rows.astype(jnp.float32), attention_gain).astype(
        jnp.bfloat16
    )
    joined_projection = jnp.dot(
        normalized_hidden, joined_weight.reshape(width, -1), preferred_element_type=jnp.float32
    )
    reduced_every_adapter = joined_down_maps.shape[1]
    reduced_hidden = jnp.dot(
        normalized_hidden, joined_down_maps, preferred_element_type=jnp.float32
    ).astype(jnp.bfloat16)
    rank_owner = jnp.arange(reduced_every_adapter, dtype=jnp.int32) // ADAPTER_RANK
    adapter_mask = adapter_per_token(segment_row, adapter_row)[:, None] == rank_owner[None, :]
    selected_reduced = jnp.where(adapter_mask, reduced_hidden, jnp.zeros_like(reduced_hidden))
    joined_projection = joined_projection + adapter_scale * jnp.dot(
        selected_reduced,
        joined_up_maps.reshape(reduced_every_adapter, -1),
        preferred_element_type=jnp.float32,
    )
    kv_here = joined_weight.shape[1]
    joined_projection = joined_projection.reshape(col_tokens, kv_here, QUERY_GROUP + 2, HEAD_SIZE)
    positions = positions_of(segment_row)
    queries = rotate_heads(
        joined_projection[:, :, :QUERY_GROUP].reshape(col_tokens, kv_here * QUERY_GROUP, HEAD_SIZE),
        positions,
    )
    queries = queries.astype(jnp.bfloat16).reshape(col_tokens, kv_here, QUERY_GROUP, HEAD_SIZE)
    key_heads = rotate_heads(joined_projection[:, :, QUERY_GROUP], positions).astype(jnp.bfloat16)
    value_heads = joined_projection[:, :, QUERY_GROUP + 1].astype(jnp.bfloat16)
    blended_hidden = attend_heads(queries, key_heads, value_heads, segment_row, sinks)
    share = col_tokens // groups
    quarter = hidden.shape[1]
    rank_total = output_down_maps.shape[1]
    route_pack = jnp.concatenate(
        [routes[0].astype(jnp.bfloat16), expert_gates[0].astype(jnp.bfloat16)], axis=1
    )
    pack_width = -(quarter + rank_total) % 128 or 128
    route_pack = jnp.pad(route_pack, ((0, 0), (0, pack_width - 2 * TOP)))
    pack_rows = lax.dynamic_update_slice_in_dim(
        jnp.zeros((col_tokens, pack_width), jnp.bfloat16), route_pack, position_dp * share, 0
    )
    partial_out = jnp.dot(blended_hidden, attention_out_weight, preferred_element_type=jnp.float32)
    low_local = jnp.dot(blended_hidden, output_down_maps, preferred_element_type=jnp.float32)
    joined_send = jnp.concatenate(
        [
            partial_out.astype(jnp.bfloat16).reshape(col_tokens, groups, quarter),
            jnp.broadcast_to(
                low_local.astype(jnp.bfloat16)[:, None, :], (col_tokens, groups, rank_total)
            ),
            jnp.broadcast_to(pack_rows[:, None, :], (col_tokens, groups, pack_width)),
        ],
        axis=2,
    ).reshape(col_tokens, -1)
    reduced_parts = []

    def reduce_rows(lo, rows):
        joined_back = lax.psum_scatter(
            joined_send[lo : lo + rows], "dp", scatter_dimension=1, tiled=True
        )
        return joined_back

    def resid_rows(joined_back, lo, rows):
        mine_out = joined_back[:, :quarter].astype(jnp.float32)
        output_reduced = joined_back[:, quarter : quarter + rank_total]
        selected_output = jnp.where(
            adapter_mask[lo : lo + rows], output_reduced, jnp.zeros_like(output_reduced)
        )
        adapter_delta = adapter_scale * jnp.dot(
            selected_output, output_up_maps, preferred_element_type=jnp.float32
        )
        resid_part = (
            hidden[lo : lo + rows].astype(jnp.float32) + mine_out + adapter_delta
        ).astype(jnp.bfloat16)
        return resid_part, joined_back[:, quarter + rank_total :]

    lane_pad = -width % 128
    wide = width + lane_pad
    experts = expert_gate_weight.shape[0] * columns
    capacity = 4 * share * TOP // (3 * experts)
    gate_weight = expert_gate_weight[0]
    up_weight = expert_up_weight[0]
    down_weight = jnp.pad(expert_down_weight[0], ((0, 0), (0, lane_pad)))
    halves = 2 if groups % 2 == 0 else 1
    half_tokens = col_tokens // halves
    half_capacity = (groups // halves) * capacity
    counter = jnp.arange(col_tokens, dtype=jnp.int32)
    request_ids = jnp.arange(REQS, dtype=jnp.int32)
    last_index = jnp.max(
        jnp.where(segment_row[None, :] == request_ids[:, None], counter[None, :], -1), axis=1
    )
    last_index = jnp.clip(last_index, 0, col_tokens - 1)
    moe_rows = []
    last_parts = []
    last_resid_parts = []
    held = None
    pending = None
    for h in range(halves):
        lo = h * half_tokens
        joined_h = reduce_rows(lo, half_tokens)
        resid_h, pack_h = resid_rows(joined_h, lo, half_tokens)
        reduced_parts.append(resid_h)
        column_h = lax.all_gather(resid_h, "dp", axis=1, tiled=True)
        if held is not None:
            column_h, held = lax.optimization_barrier((column_h, held))
        moe_in = rms_scale(column_h.astype(jnp.float32), expert_norm_gain).astype(jnp.bfloat16)
        moe_in = jnp.pad(moe_in, ((0, 0), (0, lane_pad)))
        route_flat = pack_h[:, :TOP].astype(jnp.int32).reshape(-1)
        gates_h = pack_h[:, TOP : 2 * TOP]
        one_hot = (route_flat[:, None] == jnp.arange(experts, dtype=jnp.int32)[None, :]).astype(
            jnp.int32
        )
        slot_rows = jnp.sum((jnp.cumsum(one_hot, axis=0) - one_hot) * one_hot, axis=1)
        target = route_flat * half_capacity + slot_rows
        source_rows = jnp.arange(route_flat.shape[0], dtype=jnp.int32) // TOP
        table = (
            jnp.full((experts * half_capacity,), half_tokens, jnp.int32)
            .at[target]
            .set(source_rows)
        )
        dispatch = (table[:, None] == jnp.arange(half_tokens, dtype=jnp.int32)[None, :]).astype(
            jnp.bfloat16
        )
        outgoing = (
            jnp.dot(dispatch, moe_in, preferred_element_type=jnp.float32)
            .astype(jnp.bfloat16)
            .reshape(experts, half_capacity, wide)
        )
        arrived = lax.all_to_all(outgoing, "expert", split_axis=0, concat_axis=0, tiled=True)
        if h == 0:
            held = arrived
        else:
            arrived = lax.optimization_barrier((arrived, held))[0]
        rows_in = arrived.reshape(-1, wide)[:, :width]
        gate_part = jnp.dot(rows_in, gate_weight, preferred_element_type=jnp.float32)
        up_part = jnp.dot(rows_in, up_weight, preferred_element_type=jnp.float32)
        activated = (gate_part * jax.nn.sigmoid(glu_alpha * gate_part) * (up_part + 1.0)).astype(
            jnp.bfloat16
        )
        shares_out = (
            jnp.dot(activated, down_weight, preferred_element_type=jnp.float32)
            .astype(jnp.bfloat16)
            .reshape(experts, half_capacity, wide)
        )
        answers = lax.all_to_all(shares_out, "expert", split_axis=0, concat_axis=0, tiled=True)
        if pending is not None:
            moe_rows.append(lax.psum_scatter(pending, "dp", scatter_dimension=1, tiled=True))
            answers, moe_rows[-1] = lax.optimization_barrier((answers, moe_rows[-1]))
            pending = None
        slot_ids = jnp.arange(experts * half_capacity, dtype=jnp.int32)
        combine = jnp.sum(
            jnp.where(
                target.reshape(half_tokens, TOP)[:, :, None] == slot_ids[None, None, :],
                gates_h[:, :, None],
                jnp.zeros((), jnp.bfloat16),
            ),
            axis=1,
        ).astype(jnp.bfloat16)
        mixture = jnp.dot(
            combine,
            answers.reshape(experts * half_capacity, wide),
            preferred_element_type=jnp.float32,
        )[:, :width]
        local_last = jnp.clip(last_index - lo, 0, half_tokens - 1)
        inside = ((last_index >= lo) & (last_index < lo + half_tokens))[:, None]
        last_parts.append(
            jnp.where(inside, jnp.take(mixture, local_last, axis=0), jnp.zeros((), jnp.float32))
        )
        last_resid_parts.append(
            jnp.where(inside, jnp.take(column_h, local_last, axis=0), jnp.zeros((), jnp.bfloat16))
        )
        if h < halves - 1:
            pending = mixture.astype(jnp.bfloat16)
        else:
            last_mix = sum(last_parts).reshape(REQS * groups, quarter)
            moe_send = jnp.concatenate(
                [mixture, jnp.tile(last_mix, (1, groups))], axis=0
            ).astype(jnp.bfloat16)
            moe_rows.append(lax.psum_scatter(moe_send, "dp", scatter_dimension=1, tiled=True))
    moe_back = jnp.concatenate(moe_rows, axis=0)
    moe_rounded = moe_back[:col_tokens].astype(jnp.float32).astype(jnp.bfloat16)
    resid = jnp.concatenate(reduced_parts, axis=0)
    hidden_out = (resid.astype(jnp.float32) + moe_rounded.astype(jnp.float32)).astype(jnp.bfloat16)
    last_moe = moe_back[col_tokens:].reshape(REQS, width)
    last_resid = sum(part.astype(jnp.float32) for part in last_resid_parts)
    last_hidden = (last_resid + last_moe.astype(jnp.float32)).astype(jnp.bfloat16)
    ends = rms_scale(last_hidden.astype(jnp.float32), closing_gain).astype(jnp.bfloat16)
    tail_rows = lax.all_gather(ends, "expert", axis=0, tiled=True)
    logits = jnp.dot(tail_rows, vocabulary_weight, preferred_element_type=jnp.float32)
    return (hidden_out, logits)


def solution(mesh):
    in_specs = (
        P("expert", "dp"),
        P("expert", None),
        P("expert", None),
        P("expert", "dp", None),
        P("expert", "dp", None),
        P(),
        P(None, "dp", None),
        P("dp"),
        P("dp", None),
        P(),
        P(None, "dp", None),
        P("dp", None),
        P(None, "dp"),
        P(),
        P("expert", None, "dp"),
        P("expert", None, "dp"),
        P("expert", "dp", None),
        P(),
        P(None, ("dp", "expert")),
    )
    out_specs = (P("expert", "dp"), P(None, ("dp", "expert")))
    return jax.shard_map(shards, mesh=mesh, in_specs=in_specs, out_specs=out_specs, check_vma=False)
```
